32 devices in a mesh: groups: 2 (over y), wide: 16 (over z, x, core).
Axes of the slice: x: 2, y: 2, z: 4, core: 2. Of those that a mesh axis runs over, the one named last changes fastest.
Arguments:
- epoch_rows: bfloat16 [65536, 256], P(('groups', 'wide')), parts along dimension 0
- row_object: int32 [65536], P(('groups', 'wide')), parts along dimension 0, may hold values from -1 to 127, as said below
- object_slot: int32 [256], P('groups'), parts along dimension 0, may hold values from 0 to 127, as said below
- master: float32 [4, 196608], P('groups'), parts along dimension 0, may hold values from -0.21875 to 0.21875
- momentum: float32 [4, 196608], P('groups'), parts along dimension 0, may hold values from -1.8 to 1.8
- teacher: float32 [4, 196608], P('groups'), parts along dimension 0, may hold values from -0.21875 to 0.21875
Outputs:
- new_master: float32 [4, 196608], P('groups'), parts along dimension 0
- new_momentum: float32 [4, 196608], P('groups'), parts along dimension 0
- new_teacher: float32 [4, 196608], P('groups'), parts along dimension 0
- embeddings: float32 [256, 256], P(('groups', 'wide')), parts along dimension 0
The draws below stay inside these ranges and needn't reach their ends.
There are 2 independent parts, one for each index of `groups`. The reference program is written for one: setup_inputs(seed, part) draws one part's arguments, and reference() takes and returns one part's arrays. A program takes and returns all parts, laid end to end along the dimension named above; each array names one. Nothing has to cross between parts.
Inputs may be any that keep to these rules, and one draw needn't show every extreme that they name: `row_object`: each object has 64 to 256 rows. The rows that one device stores for the objects of one owning device are at most 128, and some owning device gets 128 rows from some device in every draw. `object_slot`: A permutation: the object with slot p is owned by device p // 8 of the wide axis, at place p % 8.
All inputs are finite; a program needn't handle non-finite values.
Results may differ from the reference program's by a relative error of at most 0.01.
Values may be sent and summed in bfloat16 or wider, within the bound.
No kernel may reach another device: no remote copies, remote signals or barrier semaphores. Data moves between devices by JAX's collectives and lax.ppermute only.
A program may use at most 256 MiB of HBM per device.

```python
import jax
import jax.numpy as jnp

CH = 256
KER = 3
LAYERS = 2
SEQ = 256
OBJ_DEV = 8
OBJECTS = 128
ROWS_DEV = 2048
EPOCH_ROWS = 32768


def route_tables(key):
    base_key = jax.random.fold_in(key, 11)
    subkeys = jax.random.split(base_key, 6)
    devices = OBJECTS // OBJ_DEV
    slot_of = jax.random.permutation(subkeys[0], OBJECTS).astype(jnp.int32)
    owner_dev = slot_of // OBJ_DEV
    busy_dev = jax.random.randint(subkeys[1], (), 0, devices)
    counts = jax.random.randint(subkeys[2], (OBJECTS,), SEQ // 4, SEQ + 1)
    counts = jnp.where(owner_dev == busy_dev, SEQ, counts)
    first_dev = jax.random.randint(subkeys[3], (OBJECTS,), 0, devices)
    common = jax.random.randint(subkeys[4], (), 0, devices)
    first_dev = jnp.where(owner_dev == busy_dev, common, first_dev)
    epoch_index = jnp.arange(SEQ, dtype=jnp.int32)
    device = ((first_dev[:, None] + epoch_index[None, :]) % devices).reshape(-1)
    alive_mask = (epoch_index[None, :] < counts[:, None]).reshape(-1)
    object_id = (jnp.arange(OBJECTS, dtype=jnp.int32)[:, None] + jnp.zeros((1, SEQ), jnp.int32)).reshape(-1)
    total_slots = OBJECTS * SEQ
    priority = jax.random.permutation(subkeys[5], total_slots).astype(jnp.int32)
    sort_key = jnp.where(alive_mask, device * total_slots + priority, devices * total_slots + priority)
    sort_order = jnp.argsort(sort_key, stable=True)
    sorted_dev = device[sort_order]
    sorted_object = object_id[sort_order]
    sorted_alive = alive_mask[sort_order]
    dev_load = jax.ops.segment_sum(alive_mask.astype(jnp.int32), device, num_segments=devices)
    dev_start = jnp.cumsum(dev_load) - dev_load
    row_place = jnp.arange(total_slots, dtype=jnp.int32) - dev_start[sorted_dev]
    target = jnp.where(sorted_alive, sorted_dev * ROWS_DEV + row_place, devices * ROWS_DEV)
    row_table = jnp.full((devices * ROWS_DEV,), -1, jnp.int32).at[target].set(sorted_object, mode='drop')
    return (row_table, slot_of)


def draw_row_object(key, part):
    return route_tables(key)[0]


def draw_object_slot(key, part):
    return route_tables(key)[1]


def draw_epoch_rows(key, part):
    row_table, slot_of = route_tables(key)
    devices = OBJECTS // OBJ_DEV
    owner_dev = slot_of[jnp.maximum(row_table, 0)] // OBJ_DEV
    ramp = 1.0 + 2.0 * owner_dev.astype(jnp.float32) / max(devices - 1, 1)
    noise_key = jax.random.fold_in(key, 23)
    values = jax.random.normal(noise_key, (EPOCH_ROWS, CH), jnp.float32) * ramp[:, None]
    return values.astype(jnp.bfloat16)


def normal_values(stream_key, dims, width, most, held_as=jnp.bfloat16):
    values = jax.random.normal(stream_key, dims, jnp.float32) * width
    return jnp.minimum(jnp.maximum(values, -most), most).astype(held_as)


def setup_inputs(seed: int = 0, part: int = 0) -> dict:
    key_list = jax.random.split(jax.random.key(seed), 7)
    part_keys = jax.random.split(jax.random.fold_in(key_list[6], part), 7)
    return {
        "epoch_rows": draw_epoch_rows(jax.random.fold_in(jax.random.fold_in(key_list[6], part), 71), part),
        "row_object": draw_row_object(jax.random.fold_in(jax.random.fold_in(key_list[6], part), 71), part),
        "object_slot": draw_object_slot(jax.random.fold_in(jax.random.fold_in(key_list[6], part), 71), part),
        "master": normal_values(part_keys[3], (LAYERS, KER * CH * CH), (KER * CH) ** -0.5, 0.21875, jnp.float32),
        "momentum": normal_values(part_keys[4], (LAYERS, KER * CH * CH), 0.3, 1.8, jnp.float32),
        "teacher": normal_values(part_keys[5], (LAYERS, KER * CH * CH), (KER * CH) ** -0.5, 0.21875, jnp.float32),
    }


tau_student = 1.0
tau_teacher = 0.5
momentum_rate = 0.9
learn_rate = 0.05
ema_rate = 0.996


def delayed(states, offset):
    length = states.shape[1]
    if offset >= length:
        return jnp.zeros_like(states)
    return jnp.concatenate([jnp.zeros_like(states[:, :offset]), states[:, :length - offset]], axis=1)


def advanced(states, offset):
    length = states.shape[1]
    if offset >= length:
        return jnp.zeros_like(states)
    return jnp.concatenate([states[:, offset:], jnp.zeros_like(states[:, :offset])], axis=1)


def silu_slope(values):
    gate_value = jax.nn.sigmoid(values)
    return gate_value * (1.0 + values * (1.0 - gate_value))


def run_network(states, weights):
    stacked_list = []
    preacts = []
    for layer_at in range(weights.shape[0]):
        offset = 4 ** layer_at
        stacked = jnp.concatenate([delayed(states, tap_index * offset) for tap_index in range(KER)], axis=2)
        preact = jnp.dot(stacked.reshape(-1, stacked.shape[2]), weights[layer_at], preferred_element_type=jnp.float32).reshape(states.shape)
        states = (states.astype(jnp.float32) + jax.nn.silu(preact)).astype(jnp.bfloat16)
        stacked_list.append(stacked)
        preacts.append(preact)
    return states, stacked_list, preacts


def build_sequences(epoch_rows, row_object):
    row_count = row_object.shape[0]
    sort_order = jnp.argsort(row_object, stable=True)
    sorted_object = row_object[sort_order]
    object_ids = jnp.arange(OBJECTS, dtype=jnp.int32)
    starts = jnp.searchsorted(sorted_object, object_ids, side="left").astype(jnp.int32)
    ends = jnp.searchsorted(sorted_object, object_ids, side="right").astype(jnp.int32)
    counts = ends - starts
    position = jnp.arange(row_count, dtype=jnp.int32) - starts[jnp.maximum(sorted_object, 0)]
    target = jnp.where(sorted_object >= 0, sorted_object * SEQ + position, OBJECTS * SEQ).astype(jnp.int32)
    sequences = jnp.zeros((OBJECTS * SEQ, CH), jnp.bfloat16).at[target].set(epoch_rows[sort_order], mode="drop")
    return sequences.reshape(OBJECTS, SEQ, CH), counts


def reference(epoch_rows, row_object, object_slot, master, momentum, teacher):
    sequences, counts = build_sequences(epoch_rows, row_object)
    valid_mask = (jnp.arange(SEQ, dtype=jnp.int32)[None, :] < counts[:, None]).astype(jnp.float32)[:, :, None]
    student_w = master.astype(jnp.bfloat16).reshape(LAYERS, KER * CH, CH)
    teacher_w = teacher.astype(jnp.bfloat16).reshape(LAYERS, KER * CH, CH)
    teacher_out = run_network(sequences, teacher_w)[0]
    student_out, stacked_list, preacts = run_network(sequences, student_w)
    teacher_f = teacher_out.astype(jnp.float32)
    center = jnp.sum(valid_mask * teacher_f, axis=(0, 1)) / jnp.sum(counts).astype(jnp.float32)
    teacher_prob = jax.nn.softmax((teacher_f - center) / tau_teacher, axis=-1)
    student_f = student_out.astype(jnp.float32)
    student_prob = jax.nn.softmax(student_f / tau_student, axis=-1)
    pooled = jnp.sum(valid_mask * student_f, axis=1) / counts.astype(jnp.float32)[:, None]
    embeddings = jnp.zeros((OBJECTS, CH), jnp.float32).at[object_slot].set(pooled)
    upstream = valid_mask * (student_prob - teacher_prob) / (tau_student * OBJECTS)
    gradients = [None] * LAYERS
    for layer_at in reversed(range(LAYERS)):
        delta_bf = (upstream * silu_slope(preacts[layer_at])).astype(jnp.bfloat16)
        flat_delta = delta_bf.reshape(-1, CH)
        gradients[layer_at] = jnp.dot(stacked_list[layer_at].reshape(-1, KER * CH).T, flat_delta, preferred_element_type=jnp.float32).reshape(-1)
        if layer_at > 0:
            back_rows = jnp.dot(flat_delta, student_w[layer_at].T, preferred_element_type=jnp.float32).reshape(OBJECTS, SEQ, KER, CH)
            offset = 4 ** layer_at
            for tap_index in range(KER):
                upstream = upstream + advanced(back_rows[:, :, tap_index], tap_index * offset)
    grad_all = jnp.stack(gradients)
    new_momentum = momentum_rate * momentum + grad_all
    new_master = master - learn_rate * new_momentum
    new_teacher = ema_rate * teacher + (1.0 - ema_rate) * new_master
    return (new_master, new_momentum, new_teacher, embeddings)
```

```python
import jax
import jax.numpy as jnp
from jax import lax
from jax.sharding import PartitionSpec as P

KER = 3
SEQ = 256


tau_student = 1.0
tau_teacher = 0.5
momentum_rate = 0.9
learn_rate = 0.05
ema_rate = 0.996


def delayed(states, offset):
    length = states.shape[1]
    return jnp.concatenate(
        [jnp.zeros_like(states[:, :offset]), states[:, : length - offset]], axis=1
    )


def advanced(states, offset):
    length = states.shape[1]
    return jnp.concatenate([states[:, offset:], jnp.zeros_like(states[:, :offset])], axis=1)


def silu_slope(values):
    gate_value = jax.nn.sigmoid(values)
    return gate_value * (1.0 + values * (1.0 - gate_value))


def run_network(states, weights):
    stacked_list = []
    preacts = []
    for layer_at in range(weights.shape[0]):
        offset = 4**layer_at
        stacked = jnp.concatenate(
            [delayed(states, tap_index * offset) for tap_index in range(KER)], axis=2
        )
        preact = jnp.dot(
            stacked.reshape(-1, stacked.shape[2]),
            weights[layer_at],
            preferred_element_type=jnp.float32,
        ).reshape(states.shape)
        states = (states.astype(jnp.float32) + jax.nn.silu(preact)).astype(jnp.bfloat16)
        stacked_list.append(stacked)
        preacts.append(preact)
    return (states, stacked_list, preacts)


def route_rows(epoch_rows, row_object, object_slot):
    wide_count = lax.axis_size("wide")
    objects_all = object_slot.shape[0]
    per_dev = objects_all // wide_count
    rows_total = epoch_rows.shape[0]
    feat_width = epoch_rows.shape[1]
    capacity = rows_total // wide_count
    live_rows = row_object >= 0
    safe_object = jnp.maximum(row_object, 0)
    match_table = safe_object[:, None] == jnp.arange(objects_all, dtype=jnp.int32)[None, :]
    slot_of = jnp.sum(jnp.where(match_table, object_slot[None, :], 0), axis=1)
    owner_dev = slot_of // per_dev
    local_place = slot_of % per_dev
    owner_hot = (
        owner_dev[:, None] == jnp.arange(wide_count, dtype=jnp.int32)[None, :]
    ) & live_rows[:, None]
    running = jnp.cumsum(owner_hot.astype(jnp.int32), axis=0)
    send_rank = jnp.sum(jnp.where(owner_hot, running, 0), axis=1) - 1
    send_index = jnp.where(live_rows, owner_dev * capacity + send_rank, rows_total)
    send_rows = jnp.zeros_like(epoch_rows).at[send_index].set(epoch_rows, mode="drop")
    send_code = (
        jnp.full((rows_total,), -1.0, jnp.bfloat16)
        .at[send_index]
        .set(local_place.astype(jnp.bfloat16), mode="drop")
    )
    got_rows, got_code = (
        lax.all_to_all(
            send_rows.reshape(wide_count, capacity, feat_width),
            "wide",
            split_axis=0,
            concat_axis=0,
            tiled=True,
        ),
        lax.all_to_all(
            send_code.reshape(wide_count, capacity), "wide", split_axis=0, concat_axis=0, tiled=True
        ),
    )
    place_code = got_code.reshape(-1).astype(jnp.int32)
    place_hot = place_code[:, None] == jnp.arange(per_dev, dtype=jnp.int32)[None, :]
    arrival = jnp.cumsum(place_hot.astype(jnp.int32), axis=0)
    position = jnp.sum(jnp.where(place_hot, arrival, 0), axis=1) - 1
    counts = jnp.sum(place_hot.astype(jnp.int32), axis=0)
    target = jnp.where(place_code >= 0, place_code * SEQ + position, per_dev * SEQ)
    sequences = (
        jnp.zeros((per_dev * SEQ, feat_width), jnp.bfloat16)
        .at[target]
        .set(got_rows.reshape(-1, feat_width), mode="drop")
    )
    return (sequences.reshape(per_dev, SEQ, feat_width), counts)


def all_reduce_wide(values):
    wide_count = lax.axis_size("wide")
    layer_total, flat = values.shape
    piece = flat // wide_count
    parts = lax.all_to_all(
        values.reshape(layer_total, wide_count, piece), "wide", split_axis=1, concat_axis=1, tiled=True
    )
    mine = jnp.sum(parts, axis=1, keepdims=True)
    whole = lax.all_to_all(
        jnp.broadcast_to(mine, (layer_total, wide_count, piece)),
        "wide", split_axis=1, concat_axis=1, tiled=True,
    )
    return whole.reshape(layer_total, flat)


def local(epoch_rows, row_object, object_slot, master, momentum, teacher):
    objects_all = object_slot.shape[0]
    feat_width = epoch_rows.shape[1]
    layer_total = master.shape[0]
    student_w = master.astype(jnp.bfloat16).reshape(layer_total, KER * feat_width, feat_width)
    teacher_w = teacher.astype(jnp.bfloat16).reshape(layer_total, KER * feat_width, feat_width)
    sequences, counts = route_rows(epoch_rows, row_object, object_slot)
    valid_mask = (jnp.arange(SEQ, dtype=jnp.int32)[None, :] < counts[:, None]).astype(jnp.float32)[
        :, :, None
    ]
    teacher_out = run_network(sequences, teacher_w)[0]
    student_out, stacked_list, preacts = run_network(sequences, student_w)
    partial_sum = jnp.sum(valid_mask * teacher_out.astype(jnp.float32), axis=(0, 1))
    number = jnp.sum(counts).astype(jnp.float32)
    wide_count = lax.axis_size("wide")
    stats = jnp.concatenate([partial_sum, jnp.full((128,), number, jnp.float32)])
    gathered = lax.all_to_all(
        jnp.broadcast_to(stats[None, :], (wide_count, stats.shape[0])),
        "wide", split_axis=0, concat_axis=0, tiled=True,
    )
    stats_all = jnp.sum(gathered, axis=0)
    total_sum = stats_all[:feat_width]
    count_all = stats_all[feat_width]
    center = total_sum / count_all
    teacher_prob = jax.nn.softmax((teacher_out.astype(jnp.float32) - center) / tau_teacher, axis=-1)
    student_f = student_out.astype(jnp.float32)
    student_prob = jax.nn.softmax(student_f / tau_student, axis=-1)
    embeddings = jnp.sum(valid_mask * student_f, axis=1) / counts.astype(jnp.float32)[:, None]
    upstream = valid_mask * (student_prob - teacher_prob) / (tau_student * objects_all)
    gradients = [None] * layer_total
    for layer_at in reversed(range(layer_total)):
        delta_bf = (upstream * silu_slope(preacts[layer_at])).astype(jnp.bfloat16)
        flat_delta = delta_bf.reshape(-1, feat_width)
        weight_grad = lax.dot_general(
            stacked_list[layer_at].reshape(-1, KER * feat_width),
            flat_delta,
            (((0,), (0,)), ((), ())),
            preferred_element_type=jnp.float32,
        ).reshape(-1)
        gradients[layer_at] = weight_grad
        if layer_at > 0:
            back_rows = lax.dot_general(
                flat_delta,
                student_w[layer_at],
                (((1,), (1,)), ((), ())),
                preferred_element_type=jnp.float32,
            ).reshape(sequences.shape[0], SEQ, KER, feat_width)
            offset = 4**layer_at
            for tap_index in range(KER):
                upstream = upstream + advanced(back_rows[:, :, tap_index], tap_index * offset)
    stacked_grads = jnp.stack(gradients)
    full_grad = all_reduce_wide(stacked_grads)
    new_momentum = momentum_rate * momentum + full_grad
    new_master = master - learn_rate * new_momentum
    new_teacher = ema_rate * teacher + (1.0 - ema_rate) * new_master
    return (new_master, new_momentum, new_teacher, embeddings)


def solution(mesh):
    in_specs = (
        P(("groups", "wide"), None),
        P(("groups", "wide")),
        P("groups"),
        P("groups", None),
        P("groups", None),
        P("groups", None),
    )
    out_specs = (
        P("groups", None),
        P("groups", None),
        P("groups", None),
        P(("groups", "wide"), None),
    )
    return jax.shard_map(local, mesh=mesh, in_specs=in_specs, out_specs=out_specs, check_vma=False)
```

```python
import jax
import jax.numpy as jnp
from jax import lax
from jax.sharding import PartitionSpec as P

KER = 3
SEQ = 256


tau_student = 1.0
tau_teacher = 0.5
momentum_rate = 0.9
learn_rate = 0.05
ema_rate = 0.996


def delayed(states, offset):
    length = states.shape[1]
    return jnp.concatenate(
        [jnp.zeros_like(states[:, :offset]), states[:, : length - offset]], axis=1
    )


def advanced(states, offset):
    length = states.shape[1]
    return jnp.concatenate([states[:, offset:], jnp.zeros_like(states[:, :offset])], axis=1)


def silu_slope(values):
    gate_value = jax.nn.sigmoid(values)
    return gate_value * (1.0 + values * (1.0 - gate_value))


def run_network(states, weights):
    stacked_list = []
    preacts = []
    for layer_at in range(weights.shape[0]):
        offset = 4**layer_at
        stacked = jnp.concatenate(
            [delayed(states, tap_index * offset) for tap_index in range(KER)], axis=2
        )
        preact = jnp.dot(
            stacked.reshape(-1, stacked.shape[2]),
            weights[layer_at],
            preferred_element_type=jnp.float32,
        ).reshape(states.shape)
        states = (states.astype(jnp.float32) + jax.nn.silu(preact)).astype(jnp.bfloat16)
        stacked_list.append(stacked)
        preacts.append(preact)
    return (states, stacked_list, preacts)


def route_rows(epoch_rows, row_object, object_slot):
    wide_count = lax.axis_size("wide")
    objects_all = object_slot.shape[0]
    per_dev = objects_all // wide_count
    rows_total = epoch_rows.shape[0]
    feat_width = epoch_rows.shape[1]
    capacity = rows_total // wide_count
    live_rows = row_object >= 0
    safe_object = jnp.maximum(row_object, 0)
    match_table = safe_object[:, None] == jnp.arange(objects_all, dtype=jnp.int32)[None, :]
    slot_of = jnp.sum(jnp.where(match_table, object_slot[None, :], 0), axis=1)
    owner_dev = slot_of // per_dev
    local_place = slot_of % per_dev
    owner_hot = (
        owner_dev[:, None] == jnp.arange(wide_count, dtype=jnp.int32)[None, :]
    ) & live_rows[:, None]
    running = jnp.cumsum(owner_hot.astype(jnp.int32), axis=0)
    send_rank = jnp.sum(jnp.where(owner_hot, running, 0), axis=1) - 1
    send_index = jnp.where(live_rows, owner_dev * capacity + send_rank, rows_total)
    send_rows = jnp.zeros_like(epoch_rows).at[send_index].set(epoch_rows, mode="drop")
    send_code = (
        jnp.full((rows_total,), -1.0, jnp.bfloat16)
        .at[send_index]
        .set(local_place.astype(jnp.bfloat16), mode="drop")
    )
    got_rows, got_code = (
        lax.all_to_all(
            send_rows.reshape(wide_count, capacity, feat_width),
            "wide",
            split_axis=0,
            concat_axis=0,
            tiled=True,
        ),
        lax.all_to_all(
            send_code.reshape(wide_count, capacity), "wide", split_axis=0, concat_axis=0, tiled=True
        ),
    )
    place_code = got_code.reshape(-1).astype(jnp.int32)
    place_hot = place_code[:, None] == jnp.arange(per_dev, dtype=jnp.int32)[None, :]
    arrival = jnp.cumsum(place_hot.astype(jnp.int32), axis=0)
    position = jnp.sum(jnp.where(place_hot, arrival, 0), axis=1) - 1
    counts = jnp.sum(place_hot.astype(jnp.int32), axis=0)
    target = jnp.where(place_code >= 0, place_code * SEQ + position, per_dev * SEQ)
    sequences = (
        jnp.zeros((per_dev * SEQ, feat_width), jnp.bfloat16)
        .at[target]
        .set(got_rows.reshape(-1, feat_width), mode="drop")
    )
    return (sequences.reshape(per_dev, SEQ, feat_width), counts)


def all_reduce_wide(grads):
    wide_count = lax.axis_size("wide")
    layer_total, rows, cols = grads.shape
    piece = rows // wide_count
    blocks = grads.reshape(layer_total, wide_count, piece, cols)
    parts = lax.all_to_all(blocks, "wide", split_axis=1, concat_axis=1, tiled=True)
    mine = jnp.sum(parts, axis=1, keepdims=True)
    whole = lax.all_to_all(
        jnp.broadcast_to(mine, blocks.shape), "wide", split_axis=1, concat_axis=1, tiled=True
    )
    return whole.reshape(layer_total, rows * cols)


def local(epoch_rows, row_object, object_slot, master, momentum, teacher):
    objects_all = object_slot.shape[0]
    feat_width = epoch_rows.shape[1]
    layer_total = master.shape[0]
    student_w = master.astype(jnp.bfloat16).reshape(layer_total, KER * feat_width, feat_width)
    teacher_w = teacher.astype(jnp.bfloat16).reshape(layer_total, KER * feat_width, feat_width)
    sequences, counts = route_rows(epoch_rows, row_object, object_slot)
    valid_mask = (jnp.arange(SEQ, dtype=jnp.int32)[None, :] < counts[:, None]).astype(jnp.float32)[
        :, :, None
    ]
    teacher_out = run_network(sequences, teacher_w)[0]
    student_out, stacked_list, preacts = run_network(sequences, student_w)
    partial_sum = jnp.sum(valid_mask * teacher_out.astype(jnp.float32), axis=(0, 1))
    number = jnp.sum(counts).astype(jnp.float32)
    wide_count = lax.axis_size("wide")
    stats = jnp.concatenate([partial_sum, jnp.full((128,), number, jnp.float32)])
    gathered = lax.all_to_all(
        jnp.broadcast_to(stats[None, :], (wide_count, stats.shape[0])),
        "wide", split_axis=0, concat_axis=0, tiled=True,
    )
    stats_all = jnp.sum(gathered, axis=0)
    total_sum = stats_all[:feat_width]
    count_all = stats_all[feat_width]
    center = total_sum / count_all
    teacher_prob = jax.nn.softmax((teacher_out.astype(jnp.float32) - center) / tau_teacher, axis=-1)
    student_f = student_out.astype(jnp.float32)
    student_prob = jax.nn.softmax(student_f / tau_student, axis=-1)
    embeddings = jnp.sum(valid_mask * student_f, axis=1) / counts.astype(jnp.float32)[:, None]
    upstream = valid_mask * (student_prob - teacher_prob) / (tau_student * objects_all)
    gradients = [None] * layer_total
    for layer_at in reversed(range(layer_total)):
        delta_bf = (upstream * silu_slope(preacts[layer_at])).astype(jnp.bfloat16)
        flat_delta = delta_bf.reshape(-1, feat_width)
        weight_grad = lax.dot_general(
            stacked_list[layer_at].reshape(-1, KER * feat_width),
            flat_delta,
            (((0,), (0,)), ((), ())),
            preferred_element_type=jnp.float32,
        )
        gradients[layer_at] = weight_grad
        if layer_at > 0:
            back_rows = lax.dot_general(
                flat_delta,
                student_w[layer_at],
                (((1,), (1,)), ((), ())),
                preferred_element_type=jnp.float32,
            ).reshape(sequences.shape[0], SEQ, KER, feat_width)
            offset = 4**layer_at
            for tap_index in range(KER):
                upstream = upstream + advanced(back_rows[:, :, tap_index], tap_index * offset)
    stacked_grads = jnp.stack(gradients)
    full_grad = all_reduce_wide(stacked_grads)
    new_momentum = momentum_rate * momentum + full_grad
    new_master = master - learn_rate * new_momentum
    new_teacher = ema_rate * teacher + (1.0 - ema_rate) * new_master
    return (new_master, new_momentum, new_teacher, embeddings)


def solution(mesh):
    in_specs = (
        P(("groups", "wide"), None),
        P(("groups", "wide")),
        P("groups"),
        P("groups", None),
        P("groups", None),
        P("groups", None),
    )
    out_specs = (
        P("groups", None),
        P("groups", None),
        P("groups", None),
        P(("groups", "wide"), None),
    )
    return jax.shard_map(local, mesh=mesh, in_specs=in_specs, out_specs=out_specs, check_vma=False)
```

```python
import jax
import jax.numpy as jnp
from jax import lax
from jax.sharding import PartitionSpec as P

KER = 3
SEQ = 256


tau_student = 1.0
tau_teacher = 0.5
momentum_rate = 0.9
learn_rate = 0.05
ema_rate = 0.996


def delayed(states, offset):
    length = states.shape[1]
    return jnp.concatenate(
        [jnp.zeros_like(states[:, :offset]), states[:, : length - offset]], axis=1
    )


def advanced(states, offset):
    length = states.shape[1]
    return jnp.concatenate([states[:, offset:], jnp.zeros_like(states[:, :offset])], axis=1)


def silu_slope(values):
    gate_value = jax.nn.sigmoid(values)
    return gate_value * (1.0 + values * (1.0 - gate_value))


def run_network(states, weights):
    stacked_list = []
    preacts = []
    for layer_at in range(weights.shape[0]):
        offset = 4**layer_at
        stacked = jnp.concatenate(
            [delayed(states, tap_index * offset) for tap_index in range(KER)], axis=2
        )
        preact = jnp.dot(
            stacked.reshape(-1, stacked.shape[2]),
            weights[layer_at],
            preferred_element_type=jnp.float32,
        ).reshape(states.shape)
        states = (states.astype(jnp.float32) + jax.nn.silu(preact)).astype(jnp.bfloat16)
        stacked_list.append(stacked)
        preacts.append(preact)
    return (states, stacked_list, preacts)


def route_rows(epoch_rows, row_object, object_slot):
    wide_count = lax.axis_size("wide")
    objects_all = object_slot.shape[0]
    per_dev = objects_all // wide_count
    rows_total = epoch_rows.shape[0]
    feat_width = epoch_rows.shape[1]
    capacity = rows_total // wide_count
    live_rows = row_object >= 0
    safe_object = jnp.maximum(row_object, 0)
    match_table = safe_object[:, None] == jnp.arange(objects_all, dtype=jnp.int32)[None, :]
    slot_of = jnp.sum(jnp.where(match_table, object_slot[None, :], 0), axis=1)
    owner_dev = slot_of // per_dev
    local_place = slot_of % per_dev
    owner_hot = (
        owner_dev[:, None] == jnp.arange(wide_count, dtype=jnp.int32)[None, :]
    ) & live_rows[:, None]
    running = jnp.cumsum(owner_hot.astype(jnp.int32), axis=0)
    send_rank = jnp.sum(jnp.where(owner_hot, running, 0), axis=1) - 1
    send_index = jnp.where(live_rows, owner_dev * capacity + send_rank, rows_total)
    send_rows = jnp.zeros_like(epoch_rows).at[send_index].set(epoch_rows, mode="drop")
    send_code = (
        jnp.full((rows_total,), -1.0, jnp.bfloat16)
        .at[send_index]
        .set(local_place.astype(jnp.bfloat16), mode="drop")
    )
    got_rows, got_code = (
        lax.all_to_all(
            send_rows.reshape(wide_count, capacity, feat_width),
            "wide",
            split_axis=0,
            concat_axis=0,
            tiled=True,
        ),
        lax.all_to_all(
            send_code.reshape(wide_count, capacity), "wide", split_axis=0, concat_axis=0, tiled=True
        ),
    )
    place_code = got_code.reshape(-1).astype(jnp.int32)
    place_hot = place_code[:, None] == jnp.arange(per_dev, dtype=jnp.int32)[None, :]
    arrival = jnp.cumsum(place_hot.astype(jnp.int32), axis=0)
    position = jnp.sum(jnp.where(place_hot, arrival, 0), axis=1) - 1
    counts = jnp.sum(place_hot.astype(jnp.int32), axis=0)
    target = jnp.where(place_code >= 0, place_code * SEQ + position, per_dev * SEQ)
    sequences = (
        jnp.zeros((per_dev * SEQ, feat_width), jnp.bfloat16)
        .at[target]
        .set(got_rows.reshape(-1, feat_width), mode="drop")
    )
    return (sequences.reshape(per_dev, SEQ, feat_width), counts)


def all_reduce_wide(grads):
    wide_count = lax.axis_size("wide")
    steps = wide_count.bit_length() - 1
    assert 1 << steps == wide_count
    me = lax.axis_index("wide")
    buf = grads
    for step in range(steps):
        bit = (me >> step) & 1
        half = buf.shape[1] // 2
        keep = lax.dynamic_slice_in_dim(buf, bit * half, half, axis=1)
        send = lax.dynamic_slice_in_dim(buf, (1 - bit) * half, half, axis=1)
        pairs = [(i, i ^ (1 << step)) for i in range(wide_count)]
        buf = keep + lax.ppermute(send, "wide", pairs)
    for step in reversed(range(steps)):
        bit = (me >> step) & 1
        pairs = [(i, i ^ (1 << step)) for i in range(wide_count)]
        got = lax.ppermute(buf, "wide", pairs)
        low = jnp.where(bit == 0, buf, got)
        high = jnp.where(bit == 0, got, buf)
        buf = jnp.concatenate([low, high], axis=1)
    return buf.reshape(buf.shape[0], -1)


def local(epoch_rows, row_object, object_slot, master, momentum, teacher):
    objects_all = object_slot.shape[0]
    feat_width = epoch_rows.shape[1]
    layer_total = master.shape[0]
    student_w = master.astype(jnp.bfloat16).reshape(layer_total, KER * feat_width, feat_width)
    teacher_w = teacher.astype(jnp.bfloat16).reshape(layer_total, KER * feat_width, feat_width)
    sequences, counts = route_rows(epoch_rows, row_object, object_slot)
    valid_mask = (jnp.arange(SEQ, dtype=jnp.int32)[None, :] < counts[:, None]).astype(jnp.float32)[
        :, :, None
    ]
    teacher_out = run_network(sequences, teacher_w)[0]
    student_out, stacked_list, preacts = run_network(sequences, student_w)
    partial_sum = jnp.sum(valid_mask * teacher_out.astype(jnp.float32), axis=(0, 1))
    number = jnp.sum(counts).astype(jnp.float32)
    wide_count = lax.axis_size("wide")
    stats = jnp.concatenate([partial_sum, jnp.full((128,), number, jnp.float32)])
    gathered = lax.all_to_all(
        jnp.broadcast_to(stats[None, :], (wide_count, stats.shape[0])),
        "wide", split_axis=0, concat_axis=0, tiled=True,
    )
    stats_all = jnp.sum(gathered, axis=0)
    total_sum = stats_all[:feat_width]
    count_all = stats_all[feat_width]
    center = total_sum / count_all
    teacher_prob = jax.nn.softmax((teacher_out.astype(jnp.float32) - center) / tau_teacher, axis=-1)
    student_f = student_out.astype(jnp.float32)
    student_prob = jax.nn.softmax(student_f / tau_student, axis=-1)
    embeddings = jnp.sum(valid_mask * student_f, axis=1) / counts.astype(jnp.float32)[:, None]
    upstream = valid_mask * (student_prob - teacher_prob) / (tau_student * objects_all)
    gradients = [None] * layer_total
    for layer_at in reversed(range(layer_total)):
        delta_bf = (upstream * silu_slope(preacts[layer_at])).astype(jnp.bfloat16)
        flat_delta = delta_bf.reshape(-1, feat_width)
        weight_grad = lax.dot_general(
            stacked_list[layer_at].reshape(-1, KER * feat_width),
            flat_delta,
            (((0,), (0,)), ((), ())),
            preferred_element_type=jnp.float32,
        )
        gradients[layer_at] = weight_grad
        if layer_at > 0:
            back_rows = lax.dot_general(
                flat_delta,
                student_w[layer_at],
                (((1,), (1,)), ((), ())),
                preferred_element_type=jnp.float32,
            ).reshape(sequences.shape[0], SEQ, KER, feat_width)
            offset = 4**layer_at
            for tap_index in range(KER):
                upstream = upstream + advanced(back_rows[:, :, tap_index], tap_index * offset)
    stacked_grads = jnp.stack(gradients)
    full_grad = all_reduce_wide(stacked_grads)
    new_momentum = momentum_rate * momentum + full_grad
    new_master = master - learn_rate * new_momentum
    new_teacher = ema_rate * teacher + (1.0 - ema_rate) * new_master
    return (new_master, new_momentum, new_teacher, embeddings)


def solution(mesh):
    in_specs = (
        P(("groups", "wide"), None),
        P(("groups", "wide")),
        P("groups"),
        P("groups", None),
        P("groups", None),
        P("groups", None),
    )
    out_specs = (
        P("groups", None),
        P("groups", None),
        P("groups", None),
        P(("groups", "wide"), None),
    )
    return jax.shard_map(local, mesh=mesh, in_specs=in_specs, out_specs=out_specs, check_vma=False)
```

```python
import jax
import jax.numpy as jnp
from jax import lax
from jax.sharding import PartitionSpec as P

KER = 3
SEQ = 256


tau_student = 1.0
tau_teacher = 0.5
momentum_rate = 0.9
learn_rate = 0.05
ema_rate = 0.996


def delayed(states, offset):
    length = states.shape[1]
    return jnp.concatenate(
        [jnp.zeros_like(states[:, :offset]), states[:, : length - offset]], axis=1
    )


def advanced(states, offset):
    length = states.shape[1]
    return jnp.concatenate([states[:, offset:], jnp.zeros_like(states[:, :offset])], axis=1)


def silu_slope(values):
    gate_value = jax.nn.sigmoid(values)
    return gate_value * (1.0 + values * (1.0 - gate_value))


def run_network(states, weights):
    stacked_list = []
    preacts = []
    for layer_at in range(weights.shape[0]):
        offset = 4**layer_at
        stacked = jnp.concatenate(
            [delayed(states, tap_index * offset) for tap_index in range(KER)], axis=2
        )
        preact = jnp.dot(
            stacked.reshape(-1, stacked.shape[2]),
            weights[layer_at],
            preferred_element_type=jnp.float32,
        ).reshape(states.shape)
        states = (states.astype(jnp.float32) + jax.nn.silu(preact)).astype(jnp.bfloat16)
        stacked_list.append(stacked)
        preacts.append(preact)
    return (states, stacked_list, preacts)


def route_rows(epoch_rows, row_object, object_slot):
    wide_count = lax.axis_size("wide")
    objects_all = object_slot.shape[0]
    per_dev = objects_all // wide_count
    rows_total = epoch_rows.shape[0]
    feat_width = epoch_rows.shape[1]
    capacity = rows_total // wide_count
    live_rows = row_object >= 0
    safe_object = jnp.maximum(row_object, 0)
    match_table = safe_object[:, None] == jnp.arange(objects_all, dtype=jnp.int32)[None, :]
    slot_of = jnp.sum(jnp.where(match_table, object_slot[None, :], 0), axis=1)
    owner_dev = slot_of // per_dev
    local_place = slot_of % per_dev
    owner_hot = (
        owner_dev[:, None] == jnp.arange(wide_count, dtype=jnp.int32)[None, :]
    ) & live_rows[:, None]
    running = jnp.cumsum(owner_hot.astype(jnp.int32), axis=0)
    send_rank = jnp.sum(jnp.where(owner_hot, running, 0), axis=1) - 1
    send_index = jnp.where(live_rows, owner_dev * capacity + send_rank, rows_total)
    send_rows = jnp.zeros_like(epoch_rows).at[send_index].set(epoch_rows, mode="drop")
    send_code = (
        jnp.full((rows_total,), -1.0, jnp.bfloat16)
        .at[send_index]
        .set(local_place.astype(jnp.bfloat16), mode="drop")
    )
    got_rows, got_code = (
        lax.all_to_all(
            send_rows.reshape(wide_count, capacity, feat_width),
            "wide",
            split_axis=0,
            concat_axis=0,
            tiled=True,
        ),
        lax.all_to_all(
            send_code.reshape(wide_count, capacity), "wide", split_axis=0, concat_axis=0, tiled=True
        ),
    )
    place_code = got_code.reshape(-1).astype(jnp.int32)
    place_hot = place_code[:, None] == jnp.arange(per_dev, dtype=jnp.int32)[None, :]
    arrival = jnp.cumsum(place_hot.astype(jnp.int32), axis=0)
    position = jnp.sum(jnp.where(place_hot, arrival, 0), axis=1) - 1
    counts = jnp.sum(place_hot.astype(jnp.int32), axis=0)
    target = jnp.where(place_code >= 0, place_code * SEQ + position, per_dev * SEQ)
    sequences = (
        jnp.zeros((per_dev * SEQ, feat_width), jnp.bfloat16)
        .at[target]
        .set(got_rows.reshape(-1, feat_width), mode="drop")
    )
    return (sequences.reshape(per_dev, SEQ, feat_width), counts)


def all_reduce_wide(grads):
    wide_count = lax.axis_size("wide")
    steps = wide_count.bit_length() - 1
    assert 1 << steps == wide_count
    me = lax.axis_index("wide")
    buf = grads
    for step in range(steps):
        bit = (me >> step) & 1
        half = buf.shape[1] // 2
        keep = lax.dynamic_slice_in_dim(buf, bit * half, half, axis=1)
        send = lax.dynamic_slice_in_dim(buf, (1 - bit) * half, half, axis=1)
        pairs = [(i, i ^ (1 << step)) for i in range(wide_count)]
        buf = keep + lax.ppermute(send, "wide", pairs)
    for step in reversed(range(steps)):
        bit = (me >> step) & 1
        pairs = [(i, i ^ (1 << step)) for i in range(wide_count)]
        got = lax.ppermute(buf, "wide", pairs)
        low = jnp.where(bit == 0, buf, got)
        high = jnp.where(bit == 0, got, buf)
        buf = jnp.concatenate([low, high], axis=1)
    return buf.reshape(buf.shape[0], -1)


def local(epoch_rows, row_object, object_slot, master, momentum, teacher):
    objects_all = object_slot.shape[0]
    feat_width = epoch_rows.shape[1]
    layer_total = master.shape[0]
    student_w = lax.optimization_barrier(master.reshape(layer_total, KER * feat_width, feat_width)).astype(jnp.bfloat16)
    teacher_w = lax.optimization_barrier(teacher.reshape(layer_total, KER * feat_width, feat_width)).astype(jnp.bfloat16)
    sequences, counts = route_rows(epoch_rows, row_object, object_slot)
    valid_mask = (jnp.arange(SEQ, dtype=jnp.int32)[None, :] < counts[:, None]).astype(jnp.float32)[
        :, :, None
    ]
    teacher_out = run_network(sequences, teacher_w)[0]
    student_out, stacked_list, preacts = run_network(sequences, student_w)
    partial_sum = jnp.sum(valid_mask * teacher_out.astype(jnp.float32), axis=(0, 1))
    number = jnp.sum(counts).astype(jnp.float32)
    wide_count = lax.axis_size("wide")
    stats = jnp.concatenate([partial_sum, jnp.full((128,), number, jnp.float32)])
    gathered = lax.all_to_all(
        jnp.broadcast_to(stats[None, :], (wide_count, stats.shape[0])),
        "wide", split_axis=0, concat_axis=0, tiled=True,
    )
    stats_all = jnp.sum(gathered, axis=0)
    total_sum = stats_all[:feat_width]
    count_all = stats_all[feat_width]
    center = total_sum / count_all
    teacher_prob = jax.nn.softmax((teacher_out.astype(jnp.float32) - center) / tau_teacher, axis=-1)
    student_f = student_out.astype(jnp.float32)
    student_prob = jax.nn.softmax(student_f / tau_student, axis=-1)
    embeddings = jnp.sum(valid_mask * student_f, axis=1) / counts.astype(jnp.float32)[:, None]
    upstream = valid_mask * (student_prob - teacher_prob) / (tau_student * objects_all)
    gradients = [None] * layer_total
    for layer_at in reversed(range(layer_total)):
        delta_bf = (upstream * silu_slope(preacts[layer_at])).astype(jnp.bfloat16)
        flat_delta = delta_bf.reshape(-1, feat_width)
        weight_grad = lax.dot_general(
            stacked_list[layer_at].reshape(-1, KER * feat_width),
            flat_delta,
            (((0,), (0,)), ((), ())),
            preferred_element_type=jnp.float32,
        )
        gradients[layer_at] = weight_grad
        if layer_at > 0:
            back_rows = lax.dot_general(
                flat_delta,
                student_w[layer_at],
                (((1,), (1,)), ((), ())),
                preferred_element_type=jnp.float32,
            ).reshape(sequences.shape[0], SEQ, KER, feat_width)
            offset = 4**layer_at
            for tap_index in range(KER):
                upstream = upstream + advanced(back_rows[:, :, tap_index], tap_index * offset)
    stacked_grads = jnp.stack(gradients)
    full_grad = all_reduce_wide(stacked_grads)
    new_momentum = momentum_rate * momentum + full_grad
    new_master = master - learn_rate * new_momentum
    new_teacher = ema_rate * teacher + (1.0 - ema_rate) * new_master
    return (new_master, new_momentum, new_teacher, embeddings)


def solution(mesh):
    in_specs = (
        P(("groups", "wide"), None),
        P(("groups", "wide")),
        P("groups"),
        P("groups", None),
        P("groups", None),
        P("groups", None),
    )
    out_specs = (
        P("groups", None),
        P("groups", None),
        P("groups", None),
        P(("groups", "wide"), None),
    )
    return jax.shard_map(local, mesh=mesh, in_specs=in_specs, out_specs=out_specs, check_vma=False)
```

```python
import jax
import jax.numpy as jnp
from jax import lax
from jax.sharding import PartitionSpec as P

KER = 3
SEQ = 256


tau_student = 1.0
tau_teacher = 0.5
momentum_rate = 0.9
learn_rate = 0.05
ema_rate = 0.996


def delayed(states, offset):
    length = states.shape[1]
    return jnp.concatenate(
        [jnp.zeros_like(states[:, :offset]), states[:, : length - offset]], axis=1
    )


def advanced(states, offset):
    length = states.shape[1]
    return jnp.concatenate([states[:, offset:], jnp.zeros_like(states[:, :offset])], axis=1)


def silu_slope(values):
    gate_value = jax.nn.sigmoid(values)
    return gate_value * (1.0 + values * (1.0 - gate_value))


def run_network(states, weights):
    stacked_list = []
    preacts = []
    for layer_at in range(weights.shape[0]):
        offset = 4**layer_at
        stacked = jnp.concatenate(
            [delayed(states, tap_index * offset) for tap_index in range(KER)], axis=2
        )
        preact = jnp.dot(
            stacked.reshape(-1, stacked.shape[2]),
            weights[layer_at],
            preferred_element_type=jnp.float32,
        ).reshape(states.shape)
        states = (states.astype(jnp.float32) + jax.nn.silu(preact)).astype(jnp.bfloat16)
        stacked_list.append(stacked)
        preacts.append(preact)
    return (states, stacked_list, preacts)


def route_rows(epoch_rows, row_object, object_slot):
    wide_count = lax.axis_size("wide")
    objects_all = object_slot.shape[0]
    per_dev = objects_all // wide_count
    rows_total = epoch_rows.shape[0]
    feat_width = epoch_rows.shape[1]
    capacity = rows_total // wide_count
    live_rows = row_object >= 0
    safe_object = jnp.maximum(row_object, 0)
    match_table = safe_object[:, None] == jnp.arange(objects_all, dtype=jnp.int32)[None, :]
    slot_of = jnp.sum(jnp.where(match_table, object_slot[None, :], 0), axis=1)
    owner_dev = slot_of // per_dev
    local_place = slot_of % per_dev
    owner_hot = (
        owner_dev[:, None] == jnp.arange(wide_count, dtype=jnp.int32)[None, :]
    ) & live_rows[:, None]
    running = jnp.cumsum(owner_hot.astype(jnp.int32), axis=0)
    send_rank = jnp.sum(jnp.where(owner_hot, running, 0), axis=1) - 1
    send_index = jnp.where(live_rows, owner_dev * capacity + send_rank, -1)
    pick = (
        jnp.arange(rows_total, dtype=jnp.int32)[:, None] == send_index[None, :]
    ).astype(jnp.bfloat16)
    send_rows = jnp.dot(pick, epoch_rows, preferred_element_type=jnp.float32).astype(jnp.bfloat16)
    place_hot = (
        (local_place[:, None] == jnp.arange(per_dev, dtype=jnp.int32)[None, :]) & live_rows[:, None]
    ).astype(jnp.bfloat16)
    send_place = jnp.dot(pick, place_hot, preferred_element_type=jnp.float32).astype(jnp.bfloat16)
    got_rows, got_place = (
        lax.all_to_all(
            send_rows.reshape(wide_count, capacity, feat_width),
            "wide",
            split_axis=0,
            concat_axis=0,
            tiled=True,
        ),
        lax.all_to_all(
            send_place.reshape(wide_count, capacity, per_dev),
            "wide",
            split_axis=0,
            concat_axis=0,
            tiled=True,
        ),
    )
    place_hot = got_place.reshape(-1, per_dev) > 0
    arrival = jnp.cumsum(place_hot.astype(jnp.int32), axis=0)
    position = jnp.sum(jnp.where(place_hot, arrival, 0), axis=1) - 1
    place_code = jnp.sum(
        jnp.where(place_hot, jnp.arange(per_dev, dtype=jnp.int32)[None, :], 0), axis=1
    )
    counts = jnp.sum(place_hot.astype(jnp.int32), axis=0)
    target = jnp.where(jnp.any(place_hot, axis=1), place_code * SEQ + position, -1)
    put = (
        jnp.arange(per_dev * SEQ, dtype=jnp.int32)[:, None] == target[None, :]
    ).astype(jnp.bfloat16)
    sequences = jnp.dot(
        put, got_rows.reshape(-1, feat_width), preferred_element_type=jnp.float32
    ).astype(jnp.bfloat16)
    return (sequences.reshape(per_dev, SEQ, feat_width), counts)


def all_reduce_wide(grads):
    wide_count = lax.axis_size("wide")
    steps = wide_count.bit_length() - 1
    assert 1 << steps == wide_count
    me = lax.axis_index("wide")
    buf = grads
    for step in range(steps):
        bit = (me >> step) & 1
        half = buf.shape[1] // 2
        keep = lax.dynamic_slice_in_dim(buf, bit * half, half, axis=1)
        send = lax.dynamic_slice_in_dim(buf, (1 - bit) * half, half, axis=1)
        pairs = [(i, i ^ (1 << step)) for i in range(wide_count)]
        buf = keep + lax.ppermute(send, "wide", pairs)
    for step in reversed(range(steps)):
        bit = (me >> step) & 1
        pairs = [(i, i ^ (1 << step)) for i in range(wide_count)]
        got = lax.ppermute(buf, "wide", pairs)
        low = jnp.where(bit == 0, buf, got)
        high = jnp.where(bit == 0, got, buf)
        buf = jnp.concatenate([low, high], axis=1)
    return buf.reshape(buf.shape[0], -1)


def local(epoch_rows, row_object, object_slot, master, momentum, teacher):
    objects_all = object_slot.shape[0]
    feat_width = epoch_rows.shape[1]
    layer_total = master.shape[0]
    student_w = lax.optimization_barrier(master.reshape(layer_total, KER * feat_width, feat_width)).astype(jnp.bfloat16)
    teacher_w = lax.optimization_barrier(teacher.reshape(layer_total, KER * feat_width, feat_width)).astype(jnp.bfloat16)
    sequences, counts = route_rows(epoch_rows, row_object, object_slot)
    valid_mask = (jnp.arange(SEQ, dtype=jnp.int32)[None, :] < counts[:, None]).astype(jnp.float32)[
        :, :, None
    ]
    teacher_out = run_network(sequences, teacher_w)[0]
    student_out, stacked_list, preacts = run_network(sequences, student_w)
    partial_sum = jnp.sum(valid_mask * teacher_out.astype(jnp.float32), axis=(0, 1))
    number = jnp.sum(counts).astype(jnp.float32)
    wide_count = lax.axis_size("wide")
    stats = jnp.concatenate([partial_sum, jnp.full((128,), number, jnp.float32)])
    gathered = lax.all_to_all(
        jnp.broadcast_to(stats[None, :], (wide_count, stats.shape[0])),
        "wide", split_axis=0, concat_axis=0, tiled=True,
    )
    stats_all = jnp.sum(gathered, axis=0)
    total_sum = stats_all[:feat_width]
    count_all = stats_all[feat_width]
    center = total_sum / count_all
    teacher_prob = jax.nn.softmax((teacher_out.astype(jnp.float32) - center) / tau_teacher, axis=-1)
    student_f = student_out.astype(jnp.float32)
    student_prob = jax.nn.softmax(student_f / tau_student, axis=-1)
    embeddings = jnp.sum(valid_mask * student_f, axis=1) / counts.astype(jnp.float32)[:, None]
    upstream = valid_mask * (student_prob - teacher_prob) / (tau_student * objects_all)
    gradients = [None] * layer_total
    for layer_at in reversed(range(layer_total)):
        delta_bf = (upstream * silu_slope(preacts[layer_at])).astype(jnp.bfloat16)
        flat_delta = delta_bf.reshape(-1, feat_width)
        weight_grad = lax.dot_general(
            stacked_list[layer_at].reshape(-1, KER * feat_width),
            flat_delta,
            (((0,), (0,)), ((), ())),
            preferred_element_type=jnp.float32,
        )
        gradients[layer_at] = weight_grad
        if layer_at > 0:
            back_rows = lax.dot_general(
                flat_delta,
                student_w[layer_at],
                (((1,), (1,)), ((), ())),
                preferred_element_type=jnp.float32,
            ).reshape(sequences.shape[0], SEQ, KER, feat_width)
            offset = 4**layer_at
            for tap_index in range(KER):
                upstream = upstream + advanced(back_rows[:, :, tap_index], tap_index * offset)
    stacked_grads = jnp.stack(gradients)
    full_grad = all_reduce_wide(stacked_grads)
    new_momentum = momentum_rate * momentum + full_grad
    new_master = master - learn_rate * new_momentum
    new_teacher = ema_rate * teacher + (1.0 - ema_rate) * new_master
    return (new_master, new_momentum, new_teacher, embeddings)


def solution(mesh):
    in_specs = (
        P(("groups", "wide"), None),
        P(("groups", "wide")),
        P("groups"),
        P("groups", None),
        P("groups", None),
        P("groups", None),
    )
    out_specs = (
        P("groups", None),
        P("groups", None),
        P("groups", None),
        P(("groups", "wide"), None),
    )
    return jax.shard_map(local, mesh=mesh, in_specs=in_specs, out_specs=out_specs, check_vma=False)
```

```python
import jax
import jax.numpy as jnp
from jax import lax
from jax.sharding import PartitionSpec as P

KER = 3
SEQ = 256


tau_student = 1.0
tau_teacher = 0.5
momentum_rate = 0.9
learn_rate = 0.05
ema_rate = 0.996


def delayed(states, offset):
    length = states.shape[1]
    return jnp.concatenate(
        [jnp.zeros_like(states[:, :offset]), states[:, : length - offset]], axis=1
    )


def advanced(states, offset):
    length = states.shape[1]
    return jnp.concatenate([states[:, offset:], jnp.zeros_like(states[:, :offset])], axis=1)


def silu_slope(values):
    gate_value = jax.nn.sigmoid(values)
    return gate_value * (1.0 + values * (1.0 - gate_value))


def softmax_rows(values):
    shifted = values - lax.optimization_barrier(jnp.max(values, axis=-1, keepdims=True))
    raised = jnp.exp(shifted)
    total = lax.optimization_barrier(jnp.sum(raised, axis=-1, keepdims=True))
    return raised / total


def run_network(states, weights):
    stacked_list = []
    preacts = []
    for layer_at in range(weights.shape[0]):
        offset = 4**layer_at
        stacked = jnp.concatenate(
            [delayed(states, tap_index * offset) for tap_index in range(KER)], axis=2
        )
        preact = jnp.dot(
            stacked.reshape(-1, stacked.shape[2]),
            weights[layer_at],
            preferred_element_type=jnp.float32,
        ).reshape(states.shape)
        states = (states.astype(jnp.float32) + jax.nn.silu(preact)).astype(jnp.bfloat16)
        stacked_list.append(stacked)
        preacts.append(preact)
    return (states, stacked_list, preacts)


def route_rows(epoch_rows, row_object, object_slot):
    wide_count = lax.axis_size("wide")
    objects_all = object_slot.shape[0]
    per_dev = objects_all // wide_count
    rows_total = epoch_rows.shape[0]
    feat_width = epoch_rows.shape[1]
    capacity = rows_total // wide_count
    live_rows = row_object >= 0
    safe_object = jnp.maximum(row_object, 0)
    match_table = safe_object[:, None] == jnp.arange(objects_all, dtype=jnp.int32)[None, :]
    slot_of = jnp.sum(jnp.where(match_table, object_slot[None, :], 0), axis=1)
    owner_dev = slot_of // per_dev
    local_place = slot_of % per_dev
    owner_hot = (
        owner_dev[:, None] == jnp.arange(wide_count, dtype=jnp.int32)[None, :]
    ) & live_rows[:, None]
    running = jnp.cumsum(owner_hot.astype(jnp.int32), axis=0)
    send_rank = jnp.sum(jnp.where(owner_hot, running, 0), axis=1) - 1
    send_index = jnp.where(live_rows, owner_dev * capacity + send_rank, -1)
    pick = (
        jnp.arange(rows_total, dtype=jnp.int32)[:, None] == send_index[None, :]
    ).astype(jnp.bfloat16)
    send_rows = jnp.dot(pick, epoch_rows, preferred_element_type=jnp.float32).astype(jnp.bfloat16)
    place_hot = (
        (local_place[:, None] == jnp.arange(per_dev, dtype=jnp.int32)[None, :]) & live_rows[:, None]
    ).astype(jnp.bfloat16)
    send_place = jnp.dot(pick, place_hot, preferred_element_type=jnp.float32).astype(jnp.bfloat16)
    got_rows, got_place = (
        lax.all_to_all(
            send_rows.reshape(wide_count, capacity, feat_width),
            "wide",
            split_axis=0,
            concat_axis=0,
            tiled=True,
        ),
        lax.all_to_all(
            send_place.reshape(wide_count, capacity, per_dev),
            "wide",
            split_axis=0,
            concat_axis=0,
            tiled=True,
        ),
    )
    place_hot = got_place.reshape(-1, per_dev) > 0
    arrival = jnp.cumsum(place_hot.astype(jnp.int32), axis=0)
    position = jnp.sum(jnp.where(place_hot, arrival, 0), axis=1) - 1
    place_code = jnp.sum(
        jnp.where(place_hot, jnp.arange(per_dev, dtype=jnp.int32)[None, :], 0), axis=1
    )
    counts = jnp.sum(place_hot.astype(jnp.int32), axis=0)
    target = jnp.where(jnp.any(place_hot, axis=1), place_code * SEQ + position, -1)
    put = (
        jnp.arange(per_dev * SEQ, dtype=jnp.int32)[:, None] == target[None, :]
    ).astype(jnp.bfloat16)
    sequences = jnp.dot(
        put, got_rows.reshape(-1, feat_width), preferred_element_type=jnp.float32
    ).astype(jnp.bfloat16)
    return (sequences.reshape(per_dev, SEQ, feat_width), counts)


def all_reduce_wide(grads):
    wide_count = lax.axis_size("wide")
    steps = wide_count.bit_length() - 1
    assert 1 << steps == wide_count
    me = lax.axis_index("wide")
    buf = grads
    for step in range(steps):
        bit = (me >> step) & 1
        half = buf.shape[1] // 2
        keep = lax.dynamic_slice_in_dim(buf, bit * half, half, axis=1)
        send = lax.dynamic_slice_in_dim(buf, (1 - bit) * half, half, axis=1)
        pairs = [(i, i ^ (1 << step)) for i in range(wide_count)]
        buf = keep + lax.ppermute(send, "wide", pairs)
    for step in reversed(range(steps)):
        bit = (me >> step) & 1
        pairs = [(i, i ^ (1 << step)) for i in range(wide_count)]
        got = lax.ppermute(buf, "wide", pairs)
        low = jnp.where(bit == 0, buf, got)
        high = jnp.where(bit == 0, got, buf)
        buf = jnp.concatenate([low, high], axis=1)
    return buf.reshape(buf.shape[0], -1)


def local(epoch_rows, row_object, object_slot, master, momentum, teacher):
    objects_all = object_slot.shape[0]
    feat_width = epoch_rows.shape[1]
    layer_total = master.shape[0]
    student_w = lax.optimization_barrier(master.reshape(layer_total, KER * feat_width, feat_width)).astype(jnp.bfloat16)
    teacher_w = lax.optimization_barrier(teacher.reshape(layer_total, KER * feat_width, feat_width)).astype(jnp.bfloat16)
    sequences, counts = route_rows(epoch_rows, row_object, object_slot)
    valid_mask = (jnp.arange(SEQ, dtype=jnp.int32)[None, :] < counts[:, None]).astype(jnp.float32)[
        :, :, None
    ]
    teacher_out = run_network(sequences, teacher_w)[0]
    student_out, stacked_list, preacts = run_network(sequences, student_w)
    partial_sum = jnp.sum(valid_mask * teacher_out.astype(jnp.float32), axis=(0, 1))
    number = jnp.sum(counts).astype(jnp.float32)
    wide_count = lax.axis_size("wide")
    stats = jnp.concatenate([partial_sum, jnp.full((128,), number, jnp.float32)])
    gathered = lax.all_to_all(
        jnp.broadcast_to(stats[None, :], (wide_count, stats.shape[0])),
        "wide", split_axis=0, concat_axis=0, tiled=True,
    )
    stats_all = jnp.sum(gathered, axis=0)
    total_sum = stats_all[:feat_width]
    count_all = stats_all[feat_width]
    center = total_sum / count_all
    teacher_prob = softmax_rows((teacher_out.astype(jnp.float32) - center) / tau_teacher)
    student_f = student_out.astype(jnp.float32)
    student_prob = softmax_rows(student_f / tau_student)
    embeddings = jnp.sum(valid_mask * student_f, axis=1) / counts.astype(jnp.float32)[:, None]
    upstream = valid_mask * (student_prob - teacher_prob) / (tau_student * objects_all)
    gradients = [None] * layer_total
    for layer_at in reversed(range(layer_total)):
        delta_bf = (upstream * silu_slope(preacts[layer_at])).astype(jnp.bfloat16)
        flat_delta = delta_bf.reshape(-1, feat_width)
        weight_grad = lax.dot_general(
            stacked_list[layer_at].reshape(-1, KER * feat_width),
            flat_delta,
            (((0,), (0,)), ((), ())),
            preferred_element_type=jnp.float32,
        )
        gradients[layer_at] = weight_grad
        if layer_at > 0:
            back_rows = lax.dot_general(
                flat_delta,
                student_w[layer_at],
                (((1,), (1,)), ((), ())),
                preferred_element_type=jnp.float32,
            ).reshape(sequences.shape[0], SEQ, KER, feat_width)
            offset = 4**layer_at
            for tap_index in range(KER):
                upstream = upstream + advanced(back_rows[:, :, tap_index], tap_index * offset)
    stacked_grads = jnp.stack(gradients)
    full_grad = all_reduce_wide(stacked_grads)
    new_momentum = momentum_rate * momentum + full_grad
    new_master = master - learn_rate * new_momentum
    new_teacher = ema_rate * teacher + (1.0 - ema_rate) * new_master
    return (new_master, new_momentum, new_teacher, embeddings)


def solution(mesh):
    in_specs = (
        P(("groups", "wide"), None),
        P(("groups", "wide")),
        P("groups"),
        P("groups", None),
        P("groups", None),
        P("groups", None),
    )
    out_specs = (
        P("groups", None),
        P("groups", None),
        P("groups", None),
        P(("groups", "wide"), None),
    )
    return jax.shard_map(local, mesh=mesh, in_specs=in_specs, out_specs=out_specs, check_vma=False)
```

```python
import jax
import jax.numpy as jnp
from jax import lax
from jax.sharding import PartitionSpec as P

KER = 3
SEQ = 256


tau_student = 1.0
tau_teacher = 0.5
momentum_rate = 0.9
learn_rate = 0.05
ema_rate = 0.996


def delayed(states, offset):
    length = states.shape[1]
    return jnp.concatenate(
        [jnp.zeros_like(states[:, :offset]), states[:, : length - offset]], axis=1
    )


def advanced(states, offset):
    length = states.shape[1]
    return jnp.concatenate([states[:, offset:], jnp.zeros_like(states[:, :offset])], axis=1)


def silu_slope(values):
    gate_value = jax.nn.sigmoid(values)
    return gate_value * (1.0 + values * (1.0 - gate_value))


def softmax_rows(values):
    shifted = values - lax.optimization_barrier(jnp.max(values, axis=-1, keepdims=True))
    raised = jnp.exp(shifted)
    total = lax.optimization_barrier(jnp.sum(raised, axis=-1, keepdims=True))
    return raised / total


def run_network(states, weights):
    stacked_list = []
    preacts = []
    for layer_at in range(weights.shape[0]):
        offset = 4**layer_at
        stacked = jnp.concatenate(
            [delayed(states, tap_index * offset) for tap_index in range(KER)], axis=2
        )
        preact = jnp.dot(
            stacked.reshape(-1, stacked.shape[2]),
            weights[layer_at],
            preferred_element_type=jnp.float32,
        ).reshape(states.shape)
        states = (states.astype(jnp.float32) + jax.nn.silu(preact)).astype(jnp.bfloat16)
        stacked_list.append(stacked)
        preacts.append(preact)
    return (states, stacked_list, preacts)


def route_rows(epoch_rows, row_object, object_slot):
    wide_count = lax.axis_size("wide")
    objects_all = object_slot.shape[0]
    per_dev = objects_all // wide_count
    rows_total = epoch_rows.shape[0]
    feat_width = epoch_rows.shape[1]
    capacity = rows_total // wide_count
    live_rows = row_object >= 0
    safe_object = jnp.maximum(row_object, 0)
    match_table = safe_object[:, None] == jnp.arange(objects_all, dtype=jnp.int32)[None, :]
    slot_of = jnp.sum(jnp.where(match_table, object_slot[None, :], 0), axis=1)
    owner_dev = slot_of // per_dev
    local_place = slot_of % per_dev
    owner_hot = (
        owner_dev[:, None] == jnp.arange(wide_count, dtype=jnp.int32)[None, :]
    ) & live_rows[:, None]
    running = jnp.cumsum(owner_hot.astype(jnp.int32), axis=0)
    send_rank = jnp.sum(jnp.where(owner_hot, running, 0), axis=1) - 1
    send_index = jnp.where(live_rows, owner_dev * capacity + send_rank, -1)
    pick = (
        jnp.arange(rows_total, dtype=jnp.int32)[:, None] == send_index[None, :]
    ).astype(jnp.bfloat16)
    place_hot = (
        (local_place[:, None] == jnp.arange(per_dev, dtype=jnp.int32)[None, :]) & live_rows[:, None]
    ).astype(jnp.bfloat16)
    sent = jnp.dot(
        pick, jnp.concatenate([epoch_rows, place_hot], axis=1), preferred_element_type=jnp.float32
    ).astype(jnp.bfloat16)
    send_rows = sent[:, :feat_width]
    send_place = sent[:, feat_width:]
    got_rows, got_place = (
        lax.all_to_all(
            send_rows.reshape(wide_count, capacity, feat_width),
            "wide",
            split_axis=0,
            concat_axis=0,
            tiled=True,
        ),
        lax.all_to_all(
            send_place.reshape(wide_count, capacity, per_dev),
            "wide",
            split_axis=0,
            concat_axis=0,
            tiled=True,
        ),
    )
    place_hot = got_place.reshape(-1, per_dev) > 0
    arrival = jnp.cumsum(place_hot.astype(jnp.int32), axis=0)
    position = jnp.sum(jnp.where(place_hot, arrival, 0), axis=1) - 1
    place_code = jnp.sum(
        jnp.where(place_hot, jnp.arange(per_dev, dtype=jnp.int32)[None, :], 0), axis=1
    )
    counts = jnp.sum(place_hot.astype(jnp.int32), axis=0)
    target = jnp.where(jnp.any(place_hot, axis=1), place_code * SEQ + position, -1)
    put = (
        jnp.arange(per_dev * SEQ, dtype=jnp.int32)[:, None] == target[None, :]
    ).astype(jnp.bfloat16)
    sequences = jnp.dot(
        put, got_rows.reshape(-1, feat_width), preferred_element_type=jnp.float32
    ).astype(jnp.bfloat16)
    return (sequences.reshape(per_dev, SEQ, feat_width), counts)


def all_reduce_wide(grads):
    wide_count = lax.axis_size("wide")
    steps = wide_count.bit_length() - 1
    assert 1 << steps == wide_count
    me = lax.axis_index("wide")
    buf = grads
    for step in range(steps):
        bit = (me >> step) & 1
        half = buf.shape[1] // 2
        keep = lax.dynamic_slice_in_dim(buf, bit * half, half, axis=1)
        send = lax.dynamic_slice_in_dim(buf, (1 - bit) * half, half, axis=1)
        pairs = [(i, i ^ (1 << step)) for i in range(wide_count)]
        buf = keep + lax.ppermute(send, "wide", pairs)
    buf = buf.astype(jnp.bfloat16)
    for step in reversed(range(steps)):
        bit = (me >> step) & 1
        pairs = [(i, i ^ (1 << step)) for i in range(wide_count)]
        got = lax.ppermute(buf, "wide", pairs)
        low = jnp.where(bit == 0, buf, got)
        high = jnp.where(bit == 0, got, buf)
        buf = jnp.concatenate([low, high], axis=1)
    return buf.reshape(buf.shape[0], -1).astype(jnp.float32)


def local(epoch_rows, row_object, object_slot, master, momentum, teacher):
    objects_all = object_slot.shape[0]
    feat_width = epoch_rows.shape[1]
    layer_total = master.shape[0]
    student_w = lax.optimization_barrier(master.reshape(layer_total, KER * feat_width, feat_width)).astype(jnp.bfloat16)
    teacher_w = lax.optimization_barrier(teacher.reshape(layer_total, KER * feat_width, feat_width)).astype(jnp.bfloat16)
    sequences, counts = route_rows(epoch_rows, row_object, object_slot)
    valid_mask = (jnp.arange(SEQ, dtype=jnp.int32)[None, :] < counts[:, None]).astype(jnp.float32)[
        :, :, None
    ]
    teacher_out = run_network(sequences, teacher_w)[0]
    student_out, stacked_list, preacts = run_network(sequences, student_w)
    partial_sum = jnp.sum(valid_mask * teacher_out.astype(jnp.float32), axis=(0, 1))
    number = jnp.sum(counts).astype(jnp.float32)
    wide_count = lax.axis_size("wide")
    stats = jnp.concatenate([partial_sum, jnp.full((128,), number, jnp.float32)])
    gathered = lax.all_to_all(
        jnp.broadcast_to(stats[None, :], (wide_count, stats.shape[0])),
        "wide", split_axis=0, concat_axis=0, tiled=True,
    )
    stats_all = jnp.sum(gathered, axis=0)
    total_sum = stats_all[:feat_width]
    count_all = stats_all[feat_width]
    center = total_sum / count_all
    teacher_prob = softmax_rows((teacher_out.astype(jnp.float32) - center) / tau_teacher)
    student_f = student_out.astype(jnp.float32)
    student_prob = softmax_rows(student_f / tau_student)
    embeddings = jnp.sum(valid_mask * student_f, axis=1) / counts.astype(jnp.float32)[:, None]
    upstream = valid_mask * (student_prob - teacher_prob) / (tau_student * objects_all)
    gradients = [None] * layer_total
    for layer_at in reversed(range(layer_total)):
        delta_bf = (upstream * silu_slope(preacts[layer_at])).astype(jnp.bfloat16)
        flat_delta = delta_bf.reshape(-1, feat_width)
        weight_grad = lax.dot_general(
            stacked_list[layer_at].reshape(-1, KER * feat_width),
            flat_delta,
            (((0,), (0,)), ((), ())),
            preferred_element_type=jnp.float32,
        )
        gradients[layer_at] = weight_grad
        if layer_at > 0:
            back_rows = lax.dot_general(
                flat_delta,
                student_w[layer_at],
                (((1,), (1,)), ((), ())),
                preferred_element_type=jnp.float32,
            ).reshape(sequences.shape[0], SEQ, KER, feat_width)
            offset = 4**layer_at
            for tap_index in range(KER):
                upstream = upstream + advanced(back_rows[:, :, tap_index], tap_index * offset)
    stacked_grads = jnp.stack(gradients)
    full_grad = all_reduce_wide(stacked_grads)
    new_momentum = momentum_rate * momentum + full_grad
    new_master = master - learn_rate * new_momentum
    new_teacher = ema_rate * teacher + (1.0 - ema_rate) * new_master
    return (new_master, new_momentum, new_teacher, embeddings)


def solution(mesh):
    in_specs = (
        P(("groups", "wide"), None),
        P(("groups", "wide")),
        P("groups"),
        P("groups", None),
        P("groups", None),
        P("groups", None),
    )
    out_specs = (
        P("groups", None),
        P("groups", None),
        P("groups", None),
        P(("groups", "wide"), None),
    )
    return jax.shard_map(local, mesh=mesh, in_specs=in_specs, out_specs=out_specs, check_vma=False)
```

```python
import jax
import jax.numpy as jnp
from jax import lax
from jax.sharding import PartitionSpec as P

KER = 3
SEQ = 256


tau_student = 1.0
tau_teacher = 0.5
momentum_rate = 0.9
learn_rate = 0.05
ema_rate = 0.996


def delayed(states, offset):
    length = states.shape[1]
    return jnp.concatenate(
        [jnp.zeros_like(states[:, :offset]), states[:, : length - offset]], axis=1
    )


def advanced(states, offset):
    length = states.shape[1]
    return jnp.concatenate([states[:, offset:], jnp.zeros_like(states[:, :offset])], axis=1)


def silu_slope(values):
    gate_value = jax.nn.sigmoid(values)
    return gate_value * (1.0 + values * (1.0 - gate_value))


def softmax_rows(values):
    shifted = values - lax.optimization_barrier(jnp.max(values, axis=-1, keepdims=True))
    raised = jnp.exp(shifted)
    total = lax.optimization_barrier(jnp.sum(raised, axis=-1, keepdims=True))
    return raised / total


def run_network(states, weights):
    stacked_list = []
    preacts = []
    for layer_at in range(weights.shape[0]):
        offset = 4**layer_at
        stacked = jnp.concatenate(
            [delayed(states, tap_index * offset) for tap_index in range(KER)], axis=2
        )
        preact = jnp.dot(
            stacked.reshape(-1, stacked.shape[2]),
            weights[layer_at],
            preferred_element_type=jnp.float32,
        ).reshape(states.shape)
        states = (states.astype(jnp.float32) + jax.nn.silu(preact)).astype(jnp.bfloat16)
        stacked_list.append(stacked)
        preacts.append(preact)
    return (states, stacked_list, preacts)


def route_rows(epoch_rows, row_object, object_slot):
    wide_count = lax.axis_size("wide")
    objects_all = object_slot.shape[0]
    per_dev = objects_all // wide_count
    rows_total = epoch_rows.shape[0]
    feat_width = epoch_rows.shape[1]
    capacity = rows_total // wide_count
    live_rows = row_object >= 0
    safe_object = jnp.maximum(row_object, 0)
    match_table = safe_object[:, None] == jnp.arange(objects_all, dtype=jnp.int32)[None, :]
    slot_of = jnp.sum(jnp.where(match_table, object_slot[None, :], 0), axis=1)
    owner_dev = slot_of // per_dev
    local_place = slot_of % per_dev
    owner_hot = (
        owner_dev[:, None] == jnp.arange(wide_count, dtype=jnp.int32)[None, :]
    ) & live_rows[:, None]
    running = jnp.cumsum(owner_hot.astype(jnp.int32), axis=0)
    send_rank = jnp.sum(jnp.where(owner_hot, running, 0), axis=1) - 1
    send_index = jnp.where(live_rows, owner_dev * capacity + send_rank, -1)
    pick = (
        jnp.arange(rows_total, dtype=jnp.int32)[:, None] == send_index[None, :]
    ).astype(jnp.bfloat16)
    place_hot = (
        (local_place[:, None] == jnp.arange(per_dev, dtype=jnp.int32)[None, :]) & live_rows[:, None]
    ).astype(jnp.bfloat16)
    sent = jnp.dot(
        pick, jnp.concatenate([epoch_rows, place_hot], axis=1), preferred_element_type=jnp.float32
    ).astype(jnp.bfloat16)
    meta_rows = 16
    meta = sent[:, feat_width:].reshape(wide_count, capacity * per_dev)
    meta = jnp.pad(meta, ((0, 0), (0, meta_rows * feat_width - capacity * per_dev)))
    payload = jnp.concatenate(
        [
            sent[:, :feat_width].reshape(wide_count, capacity, feat_width),
            meta.reshape(wide_count, meta_rows, feat_width),
        ],
        axis=1,
    )
    got = lax.all_to_all(payload, "wide", split_axis=0, concat_axis=0, tiled=True)
    got_meta = got[:, capacity:, :].reshape(wide_count, meta_rows * feat_width)
    got_place = got_meta[:, : capacity * per_dev].reshape(wide_count, capacity, per_dev)
    place_hot = jnp.pad(got_place > 0, ((0, 0), (0, meta_rows), (0, 0))).reshape(-1, per_dev)
    arrival = jnp.cumsum(place_hot.astype(jnp.int32), axis=0)
    position = jnp.sum(jnp.where(place_hot, arrival, 0), axis=1) - 1
    place_code = jnp.sum(
        jnp.where(place_hot, jnp.arange(per_dev, dtype=jnp.int32)[None, :], 0), axis=1
    )
    counts = jnp.sum(place_hot.astype(jnp.int32), axis=0)
    target = jnp.where(jnp.any(place_hot, axis=1), place_code * SEQ + position, -1)
    put = (
        jnp.arange(per_dev * SEQ, dtype=jnp.int32)[:, None] == target[None, :]
    ).astype(jnp.bfloat16)
    sequences = jnp.dot(
        put, got.reshape(-1, feat_width), preferred_element_type=jnp.float32
    ).astype(jnp.bfloat16)
    return (sequences.reshape(per_dev, SEQ, feat_width), counts)


def all_reduce_wide(grads):
    wide_count = lax.axis_size("wide")
    steps = wide_count.bit_length() - 1
    assert 1 << steps == wide_count
    me = lax.axis_index("wide")
    buf = grads
    for step in range(steps):
        bit = (me >> step) & 1
        half = buf.shape[1] // 2
        keep = lax.dynamic_slice_in_dim(buf, bit * half, half, axis=1)
        send = lax.dynamic_slice_in_dim(buf, (1 - bit) * half, half, axis=1)
        pairs = [(i, i ^ (1 << step)) for i in range(wide_count)]
        buf = keep + lax.ppermute(send, "wide", pairs)
    buf = buf.astype(jnp.bfloat16)
    for step in reversed(range(steps)):
        bit = (me >> step) & 1
        pairs = [(i, i ^ (1 << step)) for i in range(wide_count)]
        got = lax.ppermute(buf, "wide", pairs)
        low = jnp.where(bit == 0, buf, got)
        high = jnp.where(bit == 0, got, buf)
        buf = jnp.concatenate([low, high], axis=1)
    return buf.reshape(buf.shape[0], -1).astype(jnp.float32)


def local(epoch_rows, row_object, object_slot, master, momentum, teacher):
    objects_all = object_slot.shape[0]
    feat_width = epoch_rows.shape[1]
    layer_total = master.shape[0]
    student_w = lax.optimization_barrier(master.reshape(layer_total, KER * feat_width, feat_width)).astype(jnp.bfloat16)
    teacher_w = lax.optimization_barrier(teacher.reshape(layer_total, KER * feat_width, feat_width)).astype(jnp.bfloat16)
    sequences, counts = route_rows(epoch_rows, row_object, object_slot)
    valid_mask = (jnp.arange(SEQ, dtype=jnp.int32)[None, :] < counts[:, None]).astype(jnp.float32)[
        :, :, None
    ]
    teacher_out = run_network(sequences, teacher_w)[0]
    student_out, stacked_list, preacts = run_network(sequences, student_w)
    partial_sum = jnp.sum(valid_mask * teacher_out.astype(jnp.float32), axis=(0, 1))
    number = jnp.sum(counts).astype(jnp.float32)
    wide_count = lax.axis_size("wide")
    stats = jnp.concatenate([partial_sum, jnp.full((128,), number, jnp.float32)])
    gathered = lax.all_to_all(
        jnp.broadcast_to(stats[None, :], (wide_count, stats.shape[0])),
        "wide", split_axis=0, concat_axis=0, tiled=True,
    )
    stats_all = jnp.sum(gathered, axis=0)
    total_sum = stats_all[:feat_width]
    count_all = stats_all[feat_width]
    center = total_sum / count_all
    teacher_prob = softmax_rows((teacher_out.astype(jnp.float32) - center) / tau_teacher)
    student_f = student_out.astype(jnp.float32)
    student_prob = softmax_rows(student_f / tau_student)
    embeddings = jnp.sum(valid_mask * student_f, axis=1) / counts.astype(jnp.float32)[:, None]
    upstream = valid_mask * (student_prob - teacher_prob) / (tau_student * objects_all)
    gradients = [None] * layer_total
    for layer_at in reversed(range(layer_total)):
        delta_bf = (upstream * silu_slope(preacts[layer_at])).astype(jnp.bfloat16)
        flat_delta = delta_bf.reshape(-1, feat_width)
        weight_grad = lax.dot_general(
            stacked_list[layer_at].reshape(-1, KER * feat_width),
            flat_delta,
            (((0,), (0,)), ((), ())),
            preferred_element_type=jnp.float32,
        )
        gradients[layer_at] = weight_grad
        if layer_at > 0:
            back_rows = lax.dot_general(
                flat_delta,
                student_w[layer_at],
                (((1,), (1,)), ((), ())),
                preferred_element_type=jnp.float32,
            ).reshape(sequences.shape[0], SEQ, KER, feat_width)
            offset = 4**layer_at
            for tap_index in range(KER):
                upstream = upstream + advanced(back_rows[:, :, tap_index], tap_index * offset)
    stacked_grads = jnp.stack(gradients)
    full_grad = all_reduce_wide(stacked_grads)
    new_momentum = momentum_rate * momentum + full_grad
    new_master = master - learn_rate * new_momentum
    new_teacher = ema_rate * teacher + (1.0 - ema_rate) * new_master
    return (new_master, new_momentum, new_teacher, embeddings)


def solution(mesh):
    in_specs = (
        P(("groups", "wide"), None),
        P(("groups", "wide")),
        P("groups"),
        P("groups", None),
        P("groups", None),
        P("groups", None),
    )
    out_specs = (
        P("groups", None),
        P("groups", None),
        P("groups", None),
        P(("groups", "wide"), None),
    )
    return jax.shard_map(local, mesh=mesh, in_specs=in_specs, out_specs=out_specs, check_vma=False)
```

```python
import jax
import jax.numpy as jnp
from jax import lax
from jax.sharding import PartitionSpec as P

KER = 3
SEQ = 256


tau_student = 1.0
tau_teacher = 0.5
momentum_rate = 0.9
learn_rate = 0.05
ema_rate = 0.996


def delayed(states, offset):
    length = states.shape[1]
    return jnp.concatenate(
        [jnp.zeros_like(states[:, :offset]), states[:, : length - offset]], axis=1
    )


def advanced(states, offset):
    length = states.shape[1]
    return jnp.concatenate([states[:, offset:], jnp.zeros_like(states[:, :offset])], axis=1)


def silu_slope(values):
    gate_value = jax.nn.sigmoid(values)
    return gate_value * (1.0 + values * (1.0 - gate_value))


def softmax_rows(values):
    shifted = values - lax.optimization_barrier(jnp.max(values, axis=-1, keepdims=True))
    raised = jnp.exp(shifted)
    total = lax.optimization_barrier(jnp.sum(raised, axis=-1, keepdims=True))
    return raised / total


def run_network(states, weights):
    stacked_list = []
    preacts = []
    for layer_at in range(weights.shape[0]):
        offset = 4**layer_at
        stacked = jnp.concatenate(
            [delayed(states, tap_index * offset) for tap_index in range(KER)], axis=2
        )
        preact = jnp.dot(
            stacked.reshape(-1, stacked.shape[2]),
            weights[layer_at],
            preferred_element_type=jnp.float32,
        ).reshape(states.shape)
        states = (states.astype(jnp.float32) + jax.nn.silu(preact)).astype(jnp.bfloat16)
        stacked_list.append(stacked)
        preacts.append(preact)
    return (states, stacked_list, preacts)


def route_rows(epoch_rows, row_object, object_slot):
    wide_count = lax.axis_size("wide")
    objects_all = object_slot.shape[0]
    per_dev = objects_all // wide_count
    rows_total = epoch_rows.shape[0]
    feat_width = epoch_rows.shape[1]
    capacity = rows_total // wide_count
    live_rows = row_object >= 0
    safe_object = jnp.maximum(row_object, 0)
    match_table = safe_object[:, None] == jnp.arange(objects_all, dtype=jnp.int32)[None, :]
    slot_of = jnp.sum(jnp.where(match_table, object_slot[None, :], 0), axis=1)
    owner_dev = slot_of // per_dev
    local_place = slot_of % per_dev
    owner_hot = (
        owner_dev[:, None] == jnp.arange(wide_count, dtype=jnp.int32)[None, :]
    ) & live_rows[:, None]
    running = jnp.cumsum(owner_hot.astype(jnp.int32), axis=0)
    send_rank = jnp.sum(jnp.where(owner_hot, running, 0), axis=1) - 1
    send_index = jnp.where(live_rows, owner_dev * capacity + send_rank, -1)
    pick = (
        jnp.arange(rows_total, dtype=jnp.int32)[:, None] == send_index[None, :]
    ).astype(jnp.bfloat16)
    place_hot = (
        (local_place[:, None] == jnp.arange(per_dev, dtype=jnp.int32)[None, :]) & live_rows[:, None]
    ).astype(jnp.bfloat16)
    sent = jnp.dot(
        pick, jnp.concatenate([epoch_rows, place_hot], axis=1), preferred_element_type=jnp.float32
    ).astype(jnp.bfloat16)
    send_rows = sent[:, :feat_width]
    send_place = sent[:, feat_width:]
    got_rows, got_place = (
        lax.all_to_all(
            send_rows.reshape(wide_count, capacity, feat_width),
            "wide",
            split_axis=0,
            concat_axis=0,
            tiled=True,
        ),
        lax.all_to_all(
            send_place.reshape(wide_count, capacity, per_dev),
            "wide",
            split_axis=0,
            concat_axis=0,
            tiled=True,
        ),
    )
    place_hot = got_place.reshape(-1, per_dev) > 0
    arrival = jnp.cumsum(place_hot.astype(jnp.int32), axis=0)
    position = jnp.sum(jnp.where(place_hot, arrival, 0), axis=1) - 1
    place_code = jnp.sum(
        jnp.where(place_hot, jnp.arange(per_dev, dtype=jnp.int32)[None, :], 0), axis=1
    )
    counts = jnp.sum(place_hot.astype(jnp.int32), axis=0)
    target = jnp.where(jnp.any(place_hot, axis=1), place_code * SEQ + position, -1)
    put = (
        jnp.arange(per_dev * SEQ, dtype=jnp.int32)[:, None] == target[None, :]
    ).astype(jnp.bfloat16)
    sequences = jnp.dot(
        put, got_rows.reshape(-1, feat_width), preferred_element_type=jnp.float32
    ).astype(jnp.bfloat16)
    return (sequences.reshape(per_dev, SEQ, feat_width), counts)


def all_reduce_wide(grads):
    wide_count = lax.axis_size("wide")
    steps = wide_count.bit_length() - 1
    assert 1 << steps == wide_count
    order_even = list(range(steps))
    order_odd = [0] + list(range(2, steps)) + [1] if steps > 2 else order_even
    me = lax.axis_index("wide")
    odd = me & 1

    def exchange_at(step):
        pairs = []
        for i in range(wide_count):
            dim = (order_odd if i & 1 else order_even)[step]
            pairs.append((i, i ^ (1 << dim)))
        bit_even = (me >> order_even[step]) & 1
        bit_odd = (me >> order_odd[step]) & 1
        return pairs, jnp.where(odd == 1, bit_odd, bit_even)

    buf = grads
    for step in range(steps):
        pairs, bit = exchange_at(step)
        half = buf.shape[1] // 2
        keep = lax.dynamic_slice_in_dim(buf, bit * half, half, axis=1)
        send = lax.dynamic_slice_in_dim(buf, (1 - bit) * half, half, axis=1)
        buf = keep + lax.ppermute(send, "wide", pairs)
    buf = buf.astype(jnp.bfloat16)
    for step in reversed(range(steps)):
        pairs, bit = exchange_at(step)
        got = lax.ppermute(buf, "wide", pairs)
        low = jnp.where(bit == 0, buf, got)
        high = jnp.where(bit == 0, got, buf)
        buf = jnp.concatenate([low, high], axis=1)
    return buf.reshape(buf.shape[0], -1).astype(jnp.float32)


def local(epoch_rows, row_object, object_slot, master, momentum, teacher):
    objects_all = object_slot.shape[0]
    feat_width = epoch_rows.shape[1]
    layer_total = master.shape[0]
    student_w = lax.optimization_barrier(master.reshape(layer_total, KER * feat_width, feat_width)).astype(jnp.bfloat16)
    teacher_w = lax.optimization_barrier(teacher.reshape(layer_total, KER * feat_width, feat_width)).astype(jnp.bfloat16)
    sequences, counts = route_rows(epoch_rows, row_object, object_slot)
    valid_mask = (jnp.arange(SEQ, dtype=jnp.int32)[None, :] < counts[:, None]).astype(jnp.float32)[
        :, :, None
    ]
    teacher_out = run_network(sequences, teacher_w)[0]
    student_out, stacked_list, preacts = run_network(sequences, student_w)
    partial_sum = jnp.sum(valid_mask * teacher_out.astype(jnp.float32), axis=(0, 1))
    number = jnp.sum(counts).astype(jnp.float32)
    wide_count = lax.axis_size("wide")
    stats = jnp.concatenate([partial_sum, jnp.full((128,), number, jnp.float32)])
    gathered = lax.all_to_all(
        jnp.broadcast_to(stats[None, :], (wide_count, stats.shape[0])),
        "wide", split_axis=0, concat_axis=0, tiled=True,
    )
    stats_all = jnp.sum(gathered, axis=0)
    total_sum = stats_all[:feat_width]
    count_all = stats_all[feat_width]
    center = total_sum / count_all
    teacher_prob = softmax_rows((teacher_out.astype(jnp.float32) - center) / tau_teacher)
    student_f = student_out.astype(jnp.float32)
    student_prob = softmax_rows(student_f / tau_student)
    embeddings = jnp.sum(valid_mask * student_f, axis=1) / counts.astype(jnp.float32)[:, None]
    upstream = valid_mask * (student_prob - teacher_prob) / (tau_student * objects_all)
    gradients = [None] * layer_total
    for layer_at in reversed(range(layer_total)):
        delta_bf = (upstream * silu_slope(preacts[layer_at])).astype(jnp.bfloat16)
        flat_delta = delta_bf.reshape(-1, feat_width)
        weight_grad = lax.dot_general(
            stacked_list[layer_at].reshape(-1, KER * feat_width),
            flat_delta,
            (((0,), (0,)), ((), ())),
            preferred_element_type=jnp.float32,
        )
        gradients[layer_at] = weight_grad
        if layer_at > 0:
            back_rows = lax.dot_general(
                flat_delta,
                student_w[layer_at],
                (((1,), (1,)), ((), ())),
                preferred_element_type=jnp.float32,
            ).reshape(sequences.shape[0], SEQ, KER, feat_width)
            offset = 4**layer_at
            for tap_index in range(KER):
                upstream = upstream + advanced(back_rows[:, :, tap_index], tap_index * offset)
    stacked_grads = jnp.stack(gradients)
    full_grad = all_reduce_wide(stacked_grads)
    new_momentum = momentum_rate * momentum + full_grad
    new_master = master - learn_rate * new_momentum
    new_teacher = ema_rate * teacher + (1.0 - ema_rate) * new_master
    return (new_master, new_momentum, new_teacher, embeddings)


def solution(mesh):
    in_specs = (
        P(("groups", "wide"), None),
        P(("groups", "wide")),
        P("groups"),
        P("groups", None),
        P("groups", None),
        P("groups", None),
    )
    out_specs = (
        P("groups", None),
        P("groups", None),
        P("groups", None),
        P(("groups", "wide"), None),
    )
    return jax.shard_map(local, mesh=mesh, in_specs=in_specs, out_specs=out_specs, check_vma=False)
```

```python
import jax
import jax.numpy as jnp
from jax import lax
from jax.sharding import PartitionSpec as P

KER = 3
SEQ = 256


tau_student = 1.0
tau_teacher = 0.5
momentum_rate = 0.9
learn_rate = 0.05
ema_rate = 0.996


def delayed(states, offset):
    length = states.shape[1]
    return jnp.concatenate(
        [jnp.zeros_like(states[:, :offset]), states[:, : length - offset]], axis=1
    )


def advanced(states, offset):
    length = states.shape[1]
    return jnp.concatenate([states[:, offset:], jnp.zeros_like(states[:, :offset])], axis=1)


def silu_slope(values):
    gate_value = jax.nn.sigmoid(values)
    return gate_value * (1.0 + values * (1.0 - gate_value))


def softmax_rows(values):
    shifted = values - lax.optimization_barrier(jnp.max(values, axis=-1, keepdims=True))
    raised = jnp.exp(shifted)
    total = lax.optimization_barrier(jnp.sum(raised, axis=-1, keepdims=True))
    return raised / total


def run_network(states, weights):
    stacked_list = []
    preacts = []
    for layer_at in range(weights.shape[0]):
        offset = 4**layer_at
        stacked = jnp.concatenate(
            [delayed(states, tap_index * offset) for tap_index in range(KER)], axis=2
        )
        preact = jnp.dot(
            stacked.reshape(-1, stacked.shape[2]),
            weights[layer_at],
            preferred_element_type=jnp.float32,
        ).reshape(states.shape)
        states = (states.astype(jnp.float32) + jax.nn.silu(preact)).astype(jnp.bfloat16)
        stacked_list.append(stacked)
        preacts.append(preact)
    return (states, stacked_list, preacts)


def prefix_count(hot):
    rows, width = hot.shape
    block = 128
    if rows % block:
        return jnp.cumsum(hot.astype(jnp.int32), axis=0)
    blocks = rows // block
    ramp = jnp.arange(block, dtype=jnp.int32)
    lower = (ramp[:, None] >= ramp[None, :]).astype(jnp.bfloat16)
    pieces = hot.astype(jnp.bfloat16).reshape(blocks, block, width)
    within = jnp.einsum("ij,bjk->bik", lower, pieces, preferred_element_type=jnp.float32)
    totals = within[:, -1, :].astype(jnp.bfloat16)
    steps = jnp.arange(blocks, dtype=jnp.int32)
    before = (steps[:, None] > steps[None, :]).astype(jnp.bfloat16)
    offsets = jnp.dot(before, totals, preferred_element_type=jnp.float32)
    return (within + offsets[:, None, :]).reshape(rows, width).astype(jnp.int32)


def route_rows(epoch_rows, row_object, object_slot):
    wide_count = lax.axis_size("wide")
    objects_all = object_slot.shape[0]
    per_dev = objects_all // wide_count
    rows_total = epoch_rows.shape[0]
    feat_width = epoch_rows.shape[1]
    capacity = rows_total // wide_count
    live_rows = row_object >= 0
    safe_object = jnp.maximum(row_object, 0)
    match_table = safe_object[:, None] == jnp.arange(objects_all, dtype=jnp.int32)[None, :]
    slot_of = jnp.sum(jnp.where(match_table, object_slot[None, :], 0), axis=1)
    owner_dev = slot_of // per_dev
    local_place = slot_of % per_dev
    owner_hot = (
        owner_dev[:, None] == jnp.arange(wide_count, dtype=jnp.int32)[None, :]
    ) & live_rows[:, None]
    running = prefix_count(owner_hot)
    send_rank = jnp.sum(jnp.where(owner_hot, running, 0), axis=1) - 1
    send_index = jnp.where(live_rows, owner_dev * capacity + send_rank, -1)
    pick = (
        jnp.arange(rows_total, dtype=jnp.int32)[:, None] == send_index[None, :]
    ).astype(jnp.bfloat16)
    place_hot = (
        (local_place[:, None] == jnp.arange(per_dev, dtype=jnp.int32)[None, :]) & live_rows[:, None]
    ).astype(jnp.bfloat16)
    sent = jnp.dot(
        pick, jnp.concatenate([epoch_rows, place_hot], axis=1), preferred_element_type=jnp.float32
    ).astype(jnp.bfloat16)
    send_rows = sent[:, :feat_width]
    send_place = sent[:, feat_width:]
    got_rows, got_place = (
        lax.all_to_all(
            send_rows.reshape(wide_count, capacity, feat_width),
            "wide",
            split_axis=0,
            concat_axis=0,
            tiled=True,
        ),
        lax.all_to_all(
            send_place.reshape(wide_count, capacity, per_dev),
            "wide",
            split_axis=0,
            concat_axis=0,
            tiled=True,
        ),
    )
    place_hot = got_place.reshape(-1, per_dev) > 0
    arrival = prefix_count(place_hot)
    position = jnp.sum(jnp.where(place_hot, arrival, 0), axis=1) - 1
    place_code = jnp.sum(
        jnp.where(place_hot, jnp.arange(per_dev, dtype=jnp.int32)[None, :], 0), axis=1
    )
    counts = jnp.sum(place_hot.astype(jnp.int32), axis=0)
    target = jnp.where(jnp.any(place_hot, axis=1), place_code * SEQ + position, -1)
    put = (
        jnp.arange(per_dev * SEQ, dtype=jnp.int32)[:, None] == target[None, :]
    ).astype(jnp.bfloat16)
    sequences = jnp.dot(
        put, got_rows.reshape(-1, feat_width), preferred_element_type=jnp.float32
    ).astype(jnp.bfloat16)
    return (sequences.reshape(per_dev, SEQ, feat_width), counts)


def all_reduce_wide(grads):
    wide_count = lax.axis_size("wide")
    steps = wide_count.bit_length() - 1
    assert 1 << steps == wide_count
    order_even = list(range(steps))
    order_odd = [0] + list(range(2, steps)) + [1] if steps > 2 else order_even
    me = lax.axis_index("wide")
    odd = me & 1

    def exchange_at(step):
        pairs = []
        for i in range(wide_count):
            dim = (order_odd if i & 1 else order_even)[step]
            pairs.append((i, i ^ (1 << dim)))
        bit_even = (me >> order_even[step]) & 1
        bit_odd = (me >> order_odd[step]) & 1
        return pairs, jnp.where(odd == 1, bit_odd, bit_even)

    buf = grads
    for step in range(steps):
        pairs, bit = exchange_at(step)
        half = buf.shape[1] // 2
        keep = lax.dynamic_slice_in_dim(buf, bit * half, half, axis=1)
        send = lax.dynamic_slice_in_dim(buf, (1 - bit) * half, half, axis=1)
        buf = keep + lax.ppermute(send, "wide", pairs)
    buf = buf.astype(jnp.bfloat16)
    for step in reversed(range(steps)):
        pairs, bit = exchange_at(step)
        got = lax.ppermute(buf, "wide", pairs)
        low = jnp.where(bit == 0, buf, got)
        high = jnp.where(bit == 0, got, buf)
        buf = jnp.concatenate([low, high], axis=1)
    return buf.reshape(buf.shape[0], -1).astype(jnp.float32)


def local(epoch_rows, row_object, object_slot, master, momentum, teacher):
    objects_all = object_slot.shape[0]
    feat_width = epoch_rows.shape[1]
    layer_total = master.shape[0]
    student_w = lax.optimization_barrier(master.reshape(layer_total, KER * feat_width, feat_width)).astype(jnp.bfloat16)
    teacher_w = lax.optimization_barrier(teacher.reshape(layer_total, KER * feat_width, feat_width)).astype(jnp.bfloat16)
    sequences, counts = route_rows(epoch_rows, row_object, object_slot)
    valid_mask = (jnp.arange(SEQ, dtype=jnp.int32)[None, :] < counts[:, None]).astype(jnp.float32)[
        :, :, None
    ]
    teacher_out = run_network(sequences, teacher_w)[0]
    student_out, stacked_list, preacts = run_network(sequences, student_w)
    partial_sum = jnp.sum(valid_mask * teacher_out.astype(jnp.float32), axis=(0, 1))
    number = jnp.sum(counts).astype(jnp.float32)
    wide_count = lax.axis_size("wide")
    stats = jnp.concatenate([partial_sum, jnp.full((128,), number, jnp.float32)])
    gathered = lax.all_to_all(
        jnp.broadcast_to(stats[None, :], (wide_count, stats.shape[0])),
        "wide", split_axis=0, concat_axis=0, tiled=True,
    )
    stats_all = jnp.sum(gathered, axis=0)
    total_sum = stats_all[:feat_width]
    count_all = stats_all[feat_width]
    center = total_sum / count_all
    teacher_prob = softmax_rows((teacher_out.astype(jnp.float32) - center) / tau_teacher)
    student_f = student_out.astype(jnp.float32)
    student_prob = softmax_rows(student_f / tau_student)
    embeddings = jnp.sum(valid_mask * student_f, axis=1) / counts.astype(jnp.float32)[:, None]
    upstream = valid_mask * (student_prob - teacher_prob) / (tau_student * objects_all)
    gradients = [None] * layer_total
    for layer_at in reversed(range(layer_total)):
        delta_bf = (upstream * silu_slope(preacts[layer_at])).astype(jnp.bfloat16)
        flat_delta = delta_bf.reshape(-1, feat_width)
        weight_grad = lax.dot_general(
            stacked_list[layer_at].reshape(-1, KER * feat_width),
            flat_delta,
            (((0,), (0,)), ((), ())),
            preferred_element_type=jnp.float32,
        )
        gradients[layer_at] = weight_grad
        if layer_at > 0:
            back_rows = lax.dot_general(
                flat_delta,
                student_w[layer_at],
                (((1,), (1,)), ((), ())),
                preferred_element_type=jnp.float32,
            ).reshape(sequences.shape[0], SEQ, KER, feat_width)
            offset = 4**layer_at
            for tap_index in range(KER):
                upstream = upstream + advanced(back_rows[:, :, tap_index], tap_index * offset)
    stacked_grads = jnp.stack(gradients)
    full_grad = all_reduce_wide(stacked_grads)
    new_momentum = momentum_rate * momentum + full_grad
    new_master = master - learn_rate * new_momentum
    new_teacher = ema_rate * teacher + (1.0 - ema_rate) * new_master
    return (new_master, new_momentum, new_teacher, embeddings)


def solution(mesh):
    in_specs = (
        P(("groups", "wide"), None),
        P(("groups", "wide")),
        P("groups"),
        P("groups", None),
        P("groups", None),
        P("groups", None),
    )
    out_specs = (
        P("groups", None),
        P("groups", None),
        P("groups", None),
        P(("groups", "wide"), None),
    )
    return jax.shard_map(local, mesh=mesh, in_specs=in_specs, out_specs=out_specs, check_vma=False)
```

```python
import jax
import jax.numpy as jnp
from jax import lax
from jax.sharding import PartitionSpec as P

KER = 3
SEQ = 256


tau_student = 1.0
tau_teacher = 0.5
momentum_rate = 0.9
learn_rate = 0.05
ema_rate = 0.996


def delayed(states, offset):
    length = states.shape[1]
    return jnp.concatenate(
        [jnp.zeros_like(states[:, :offset]), states[:, : length - offset]], axis=1
    )


def advanced(states, offset):
    length = states.shape[1]
    return jnp.concatenate([states[:, offset:], jnp.zeros_like(states[:, :offset])], axis=1)


def silu_slope(values):
    gate_value = jax.nn.sigmoid(values)
    return gate_value * (1.0 + values * (1.0 - gate_value))


def softmax_rows(values):
    shifted = values - lax.optimization_barrier(jnp.max(values, axis=-1, keepdims=True))
    raised = jnp.exp(shifted)
    total = lax.optimization_barrier(jnp.sum(raised, axis=-1, keepdims=True))
    return raised / total


def run_network(states, weights):
    stacked_list = []
    preacts = []
    for layer_at in range(weights.shape[0]):
        offset = 4**layer_at
        stacked = jnp.concatenate(
            [delayed(states, tap_index * offset) for tap_index in range(KER)], axis=2
        )
        preact = jnp.dot(
            stacked.reshape(-1, stacked.shape[2]),
            weights[layer_at],
            preferred_element_type=jnp.float32,
        ).reshape(states.shape)
        states = (states.astype(jnp.float32) + jax.nn.silu(preact)).astype(jnp.bfloat16)
        stacked_list.append(stacked)
        preacts.append(preact)
    return (states, stacked_list, preacts)


def prefix_count(hot):
    rows, width = hot.shape
    block = 128
    if rows % block:
        return jnp.cumsum(hot.astype(jnp.int32), axis=0)
    blocks = rows // block
    ramp = jnp.arange(block, dtype=jnp.int32)
    lower = (ramp[:, None] >= ramp[None, :]).astype(jnp.bfloat16)
    pieces = hot.astype(jnp.bfloat16).reshape(blocks, block, width)
    within = jnp.einsum("ij,bjk->bik", lower, pieces, preferred_element_type=jnp.float32)
    totals = within[:, -1, :].astype(jnp.bfloat16)
    steps = jnp.arange(blocks, dtype=jnp.int32)
    before = (steps[:, None] > steps[None, :]).astype(jnp.bfloat16)
    offsets = jnp.dot(before, totals, preferred_element_type=jnp.float32)
    return (within + offsets[:, None, :]).reshape(rows, width).astype(jnp.int32)


def route_rows(epoch_rows, row_object, object_slot):
    wide_count = lax.axis_size("wide")
    objects_all = object_slot.shape[0]
    per_dev = objects_all // wide_count
    rows_total = epoch_rows.shape[0]
    feat_width = epoch_rows.shape[1]
    capacity = rows_total // wide_count
    live_rows = row_object >= 0
    safe_object = jnp.maximum(row_object, 0)
    match_table = safe_object[:, None] == jnp.arange(objects_all, dtype=jnp.int32)[None, :]
    slot_of = jnp.sum(jnp.where(match_table, object_slot[None, :], 0), axis=1)
    owner_dev = slot_of // per_dev
    slot_hot = (slot_of[:, None] == jnp.arange(objects_all, dtype=jnp.int32)[None, :]) & live_rows[:, None]
    group_size = jnp.sum(slot_hot.astype(jnp.int32), axis=0).reshape(wide_count, per_dev)
    got_size = lax.all_to_all(group_size, "wide", split_axis=0, concat_axis=0, tiled=True)
    places = jnp.arange(per_dev, dtype=jnp.int32)
    earlier_place = (places[:, None] < places[None, :]).astype(jnp.int32)
    group_start = jnp.sum(group_size[:, :, None] * earlier_place[None, :, :], axis=1)
    running = prefix_count(slot_hot)
    rank_in_group = jnp.sum(jnp.where(slot_hot, running, 0), axis=1) - 1
    start_of_row = jnp.sum(jnp.where(slot_hot, group_start.reshape(1, -1), 0), axis=1)
    send_index = jnp.where(live_rows, owner_dev * capacity + start_of_row + rank_in_group, -1)
    pick = (
        jnp.arange(rows_total, dtype=jnp.int32)[:, None] == send_index[None, :]
    ).astype(jnp.bfloat16)
    send_rows = jnp.dot(pick, epoch_rows, preferred_element_type=jnp.float32).astype(jnp.bfloat16)
    got_rows = lax.all_to_all(
        send_rows.reshape(wide_count, capacity, feat_width),
        "wide",
        split_axis=0,
        concat_axis=0,
        tiled=True,
    )
    sources = jnp.arange(wide_count, dtype=jnp.int32)
    earlier_source = (sources[:, None] > sources[None, :]).astype(jnp.int32)
    before_source = jnp.sum(earlier_source[:, :, None] * got_size[None, :, :], axis=1)
    got_start = jnp.sum(got_size[:, :, None] * earlier_place[None, :, :], axis=1)
    slots = jnp.arange(capacity, dtype=jnp.int32)[None, :, None]
    in_group = (slots >= got_start[:, None, :]) & (slots < (got_start + got_size)[:, None, :])
    position = jnp.sum(
        jnp.where(in_group, before_source[:, None, :] + slots - got_start[:, None, :], 0), axis=2
    )
    place_code = jnp.sum(jnp.where(in_group, places[None, None, :], 0), axis=2)
    target = jnp.where(jnp.any(in_group, axis=2), place_code * SEQ + position, -1).reshape(-1)
    counts = jnp.sum(got_size, axis=0)
    put = (
        jnp.arange(per_dev * SEQ, dtype=jnp.int32)[:, None] == target[None, :]
    ).astype(jnp.bfloat16)
    sequences = jnp.dot(
        put, got_rows.reshape(-1, feat_width), preferred_element_type=jnp.float32
    ).astype(jnp.bfloat16)
    return (sequences.reshape(per_dev, SEQ, feat_width), counts)


def all_reduce_wide(grads):
    wide_count = lax.axis_size("wide")
    steps = wide_count.bit_length() - 1
    assert 1 << steps == wide_count
    order_even = list(range(steps))
    order_odd = [0] + list(range(2, steps)) + [1] if steps > 2 else order_even
    me = lax.axis_index("wide")
    odd = me & 1

    def exchange_at(step):
        pairs = []
        for i in range(wide_count):
            dim = (order_odd if i & 1 else order_even)[step]
            pairs.append((i, i ^ (1 << dim)))
        bit_even = (me >> order_even[step]) & 1
        bit_odd = (me >> order_odd[step]) & 1
        return pairs, jnp.where(odd == 1, bit_odd, bit_even)

    buf = grads
    for step in range(steps):
        pairs, bit = exchange_at(step)
        half = buf.shape[1] // 2
        keep = lax.dynamic_slice_in_dim(buf, bit * half, half, axis=1)
        send = lax.dynamic_slice_in_dim(buf, (1 - bit) * half, half, axis=1)
        buf = keep + lax.ppermute(send, "wide", pairs)
    buf = buf.astype(jnp.bfloat16)
    for step in reversed(range(steps)):
        pairs, bit = exchange_at(step)
        got = lax.ppermute(buf, "wide", pairs)
        low = jnp.where(bit == 0, buf, got)
        high = jnp.where(bit == 0, got, buf)
        buf = jnp.concatenate([low, high], axis=1)
    return buf.reshape(buf.shape[0], -1).astype(jnp.float32)


def local(epoch_rows, row_object, object_slot, master, momentum, teacher):
    objects_all = object_slot.shape[0]
    feat_width = epoch_rows.shape[1]
    layer_total = master.shape[0]
    student_w = lax.optimization_barrier(master.reshape(layer_total, KER * feat_width, feat_width)).astype(jnp.bfloat16)
    teacher_w = lax.optimization_barrier(teacher.reshape(layer_total, KER * feat_width, feat_width)).astype(jnp.bfloat16)
    sequences, counts = route_rows(epoch_rows, row_object, object_slot)
    valid_mask = (jnp.arange(SEQ, dtype=jnp.int32)[None, :] < counts[:, None]).astype(jnp.float32)[
        :, :, None
    ]
    teacher_out = run_network(sequences, teacher_w)[0]
    student_out, stacked_list, preacts = run_network(sequences, student_w)
    partial_sum = jnp.sum(valid_mask * teacher_out.astype(jnp.float32), axis=(0, 1))
    number = jnp.sum(counts).astype(jnp.float32)
    wide_count = lax.axis_size("wide")
    stats = jnp.concatenate([partial_sum, jnp.full((128,), number, jnp.float32)])
    gathered = lax.all_to_all(
        jnp.broadcast_to(stats[None, :], (wide_count, stats.shape[0])),
        "wide", split_axis=0, concat_axis=0, tiled=True,
    )
    stats_all = jnp.sum(gathered, axis=0)
    total_sum = stats_all[:feat_width]
    count_all = stats_all[feat_width]
    center = total_sum / count_all
    teacher_prob = softmax_rows((teacher_out.astype(jnp.float32) - center) / tau_teacher)
    student_f = student_out.astype(jnp.float32)
    student_prob = softmax_rows(student_f / tau_student)
    embeddings = jnp.sum(valid_mask * student_f, axis=1) / counts.astype(jnp.float32)[:, None]
    upstream = valid_mask * (student_prob - teacher_prob) / (tau_student * objects_all)
    gradients = [None] * layer_total
    for layer_at in reversed(range(layer_total)):
        delta_bf = (upstream * silu_slope(preacts[layer_at])).astype(jnp.bfloat16)
        flat_delta = delta_bf.reshape(-1, feat_width)
        weight_grad = lax.dot_general(
            stacked_list[layer_at].reshape(-1, KER * feat_width),
            flat_delta,
            (((0,), (0,)), ((), ())),
            preferred_element_type=jnp.float32,
        )
        gradients[layer_at] = weight_grad
        if layer_at > 0:
            back_rows = lax.dot_general(
                flat_delta,
                student_w[layer_at],
                (((1,), (1,)), ((), ())),
                preferred_element_type=jnp.float32,
            ).reshape(sequences.shape[0], SEQ, KER, feat_width)
            offset = 4**layer_at
            for tap_index in range(KER):
                upstream = upstream + advanced(back_rows[:, :, tap_index], tap_index * offset)
    stacked_grads = jnp.stack(gradients)
    full_grad = all_reduce_wide(stacked_grads)
    new_momentum = momentum_rate * momentum + full_grad
    new_master = master - learn_rate * new_momentum
    new_teacher = ema_rate * teacher + (1.0 - ema_rate) * new_master
    return (new_master, new_momentum, new_teacher, embeddings)


def solution(mesh):
    in_specs = (
        P(("groups", "wide"), None),
        P(("groups", "wide")),
        P("groups"),
        P("groups", None),
        P("groups", None),
        P("groups", None),
    )
    out_specs = (
        P("groups", None),
        P("groups", None),
        P("groups", None),
        P(("groups", "wide"), None),
    )
    return jax.shard_map(local, mesh=mesh, in_specs=in_specs, out_specs=out_specs, check_vma=False)
```

```python
import jax
import jax.numpy as jnp
from jax import lax
from jax.sharding import PartitionSpec as P

KER = 3
SEQ = 256


tau_student = 1.0
tau_teacher = 0.5
momentum_rate = 0.9
learn_rate = 0.05
ema_rate = 0.996


def delayed(states, offset):
    length = states.shape[1]
    return jnp.concatenate(
        [jnp.zeros_like(states[:, :offset]), states[:, : length - offset]], axis=1
    )


def advanced(states, offset):
    length = states.shape[1]
    return jnp.concatenate([states[:, offset:], jnp.zeros_like(states[:, :offset])], axis=1)


def silu_slope(values):
    gate_value = jax.nn.sigmoid(values)
    return gate_value * (1.0 + values * (1.0 - gate_value))


def softmax_rows(values):
    shifted = values - lax.optimization_barrier(jnp.max(values, axis=-1, keepdims=True))
    raised = jnp.exp(shifted)
    total = lax.optimization_barrier(jnp.sum(raised, axis=-1, keepdims=True))
    return raised / total


def run_network(states, weights):
    stacked_list = []
    preacts = []
    for layer_at in range(weights.shape[0]):
        offset = 4**layer_at
        stacked = jnp.concatenate(
            [delayed(states, tap_index * offset) for tap_index in range(KER)], axis=2
        )
        preact = jnp.dot(
            stacked.reshape(-1, stacked.shape[2]),
            weights[layer_at],
            preferred_element_type=jnp.float32,
        ).reshape(states.shape)
        states = (states.astype(jnp.float32) + jax.nn.silu(preact)).astype(jnp.bfloat16)
        stacked_list.append(stacked)
        preacts.append(preact)
    return (states, stacked_list, preacts)


def prefix_count(hot):
    rows, width = hot.shape
    block = 128
    if rows % block:
        return jnp.cumsum(hot.astype(jnp.int32), axis=0)
    blocks = rows // block
    ramp = jnp.arange(block, dtype=jnp.int32)
    lower = (ramp[:, None] >= ramp[None, :]).astype(jnp.bfloat16)
    pieces = hot.astype(jnp.bfloat16).reshape(blocks, block, width)
    within = jnp.einsum("ij,bjk->bik", lower, pieces, preferred_element_type=jnp.float32)
    totals = within[:, -1, :].astype(jnp.bfloat16)
    steps = jnp.arange(blocks, dtype=jnp.int32)
    before = (steps[:, None] > steps[None, :]).astype(jnp.bfloat16)
    offsets = jnp.dot(before, totals, preferred_element_type=jnp.float32)
    return (within + offsets[:, None, :]).reshape(rows, width).astype(jnp.int32)


def route_rows(epoch_rows, row_object, object_slot):
    wide_count = lax.axis_size("wide")
    objects_all = object_slot.shape[0]
    per_dev = objects_all // wide_count
    rows_total = epoch_rows.shape[0]
    feat_width = epoch_rows.shape[1]
    capacity = rows_total // wide_count
    live_rows = row_object >= 0
    safe_object = jnp.maximum(row_object, 0)
    match_table = safe_object[:, None] == jnp.arange(objects_all, dtype=jnp.int32)[None, :]
    slot_of = jnp.sum(jnp.where(match_table, object_slot[None, :], 0), axis=1)
    owner_dev = slot_of // per_dev
    slot_hot = (slot_of[:, None] == jnp.arange(objects_all, dtype=jnp.int32)[None, :]) & live_rows[:, None]
    group_size = jnp.sum(slot_hot.astype(jnp.int32), axis=0).reshape(wide_count, per_dev)
    places = jnp.arange(per_dev, dtype=jnp.int32)
    earlier_place = (places[:, None] < places[None, :]).astype(jnp.int32)
    group_start = jnp.sum(group_size[:, :, None] * earlier_place[None, :, :], axis=1)
    running = prefix_count(slot_hot)
    rank_in_group = jnp.sum(jnp.where(slot_hot, running, 0), axis=1) - 1
    start_of_row = jnp.sum(jnp.where(slot_hot, group_start.reshape(1, -1), 0), axis=1)
    chunk = capacity + 16
    send_index = jnp.where(live_rows, owner_dev * chunk + start_of_row + rank_in_group, -1)
    pick = (
        jnp.arange(wide_count * chunk, dtype=jnp.int32)[:, None] == send_index[None, :]
    ).astype(jnp.bfloat16)
    payload = jnp.dot(pick, epoch_rows, preferred_element_type=jnp.float32).astype(jnp.bfloat16)
    payload = lax.dynamic_update_slice(
        payload.reshape(wide_count, chunk, feat_width),
        group_size.astype(jnp.bfloat16).reshape(wide_count, 1, per_dev),
        (0, capacity, 0),
    )
    got = lax.all_to_all(payload, "wide", split_axis=0, concat_axis=0, tiled=True)
    got_size = got[:, capacity, :per_dev].astype(jnp.int32)
    sources = jnp.arange(wide_count, dtype=jnp.int32)
    earlier_source = (sources[:, None] > sources[None, :]).astype(jnp.int32)
    before_source = jnp.sum(earlier_source[:, :, None] * got_size[None, :, :], axis=1)
    got_start = jnp.sum(got_size[:, :, None] * earlier_place[None, :, :], axis=1)
    slots = jnp.arange(chunk, dtype=jnp.int32)[None, :, None]
    in_group = (
        (slots >= got_start[:, None, :])
        & (slots < (got_start + got_size)[:, None, :])
        & (slots < capacity)
    )
    position = jnp.sum(
        jnp.where(in_group, before_source[:, None, :] + slots - got_start[:, None, :], 0), axis=2
    )
    place_code = jnp.sum(jnp.where(in_group, places[None, None, :], 0), axis=2)
    target = jnp.where(jnp.any(in_group, axis=2), place_code * SEQ + position, -1).reshape(-1)
    counts = jnp.sum(got_size, axis=0)
    put = (
        jnp.arange(per_dev * SEQ, dtype=jnp.int32)[:, None] == target[None, :]
    ).astype(jnp.bfloat16)
    sequences = jnp.dot(
        put, got.reshape(-1, feat_width), preferred_element_type=jnp.float32
    ).astype(jnp.bfloat16)
    return (sequences.reshape(per_dev, SEQ, feat_width), counts)


def all_reduce_wide(grads):
    wide_count = lax.axis_size("wide")
    steps = wide_count.bit_length() - 1
    assert 1 << steps == wide_count
    order_even = list(range(steps))
    order_odd = [0] + list(range(2, steps)) + [1] if steps > 2 else order_even
    me = lax.axis_index("wide")
    odd = me & 1

    def exchange_at(step):
        pairs = []
        for i in range(wide_count):
            dim = (order_odd if i & 1 else order_even)[step]
            pairs.append((i, i ^ (1 << dim)))
        bit_even = (me >> order_even[step]) & 1
        bit_odd = (me >> order_odd[step]) & 1
        return pairs, jnp.where(odd == 1, bit_odd, bit_even)

    buf = grads
    for step in range(steps):
        pairs, bit = exchange_at(step)
        half = buf.shape[1] // 2
        keep = lax.dynamic_slice_in_dim(buf, bit * half, half, axis=1)
        send = lax.dynamic_slice_in_dim(buf, (1 - bit) * half, half, axis=1)
        buf = keep + lax.ppermute(send, "wide", pairs)
    buf = buf.astype(jnp.bfloat16)
    for step in reversed(range(steps)):
        pairs, bit = exchange_at(step)
        got = lax.ppermute(buf, "wide", pairs)
        low = jnp.where(bit == 0, buf, got)
        high = jnp.where(bit == 0, got, buf)
        buf = jnp.concatenate([low, high], axis=1)
    return buf.reshape(buf.shape[0], -1).astype(jnp.float32)


def local(epoch_rows, row_object, object_slot, master, momentum, teacher):
    objects_all = object_slot.shape[0]
    feat_width = epoch_rows.shape[1]
    layer_total = master.shape[0]
    student_w = lax.optimization_barrier(master.reshape(layer_total, KER * feat_width, feat_width)).astype(jnp.bfloat16)
    teacher_w = lax.optimization_barrier(teacher.reshape(layer_total, KER * feat_width, feat_width)).astype(jnp.bfloat16)
    sequences, counts = route_rows(epoch_rows, row_object, object_slot)
    valid_mask = (jnp.arange(SEQ, dtype=jnp.int32)[None, :] < counts[:, None]).astype(jnp.float32)[
        :, :, None
    ]
    teacher_out = run_network(sequences, teacher_w)[0]
    student_out, stacked_list, preacts = run_network(sequences, student_w)
    partial_sum = jnp.sum(valid_mask * teacher_out.astype(jnp.float32), axis=(0, 1))
    number = jnp.sum(counts).astype(jnp.float32)
    wide_count = lax.axis_size("wide")
    stats = jnp.concatenate([partial_sum, jnp.full((128,), number, jnp.float32)])
    gathered = lax.all_to_all(
        jnp.broadcast_to(stats[None, :], (wide_count, stats.shape[0])),
        "wide", split_axis=0, concat_axis=0, tiled=True,
    )
    stats_all = jnp.sum(gathered, axis=0)
    total_sum = stats_all[:feat_width]
    count_all = stats_all[feat_width]
    center = total_sum / count_all
    teacher_prob = softmax_rows((teacher_out.astype(jnp.float32) - center) / tau_teacher)
    student_f = student_out.astype(jnp.float32)
    student_prob = softmax_rows(student_f / tau_student)
    embeddings = jnp.sum(valid_mask * student_f, axis=1) / counts.astype(jnp.float32)[:, None]
    upstream = valid_mask * (student_prob - teacher_prob) / (tau_student * objects_all)
    gradients = [None] * layer_total
    for layer_at in reversed(range(layer_total)):
        delta_bf = (upstream * silu_slope(preacts[layer_at])).astype(jnp.bfloat16)
        flat_delta = delta_bf.reshape(-1, feat_width)
        weight_grad = lax.dot_general(
            stacked_list[layer_at].reshape(-1, KER * feat_width),
            flat_delta,
            (((0,), (0,)), ((), ())),
            preferred_element_type=jnp.float32,
        )
        gradients[layer_at] = weight_grad
        if layer_at > 0:
            back_rows = lax.dot_general(
                flat_delta,
                student_w[layer_at],
                (((1,), (1,)), ((), ())),
                preferred_element_type=jnp.float32,
            ).reshape(sequences.shape[0], SEQ, KER, feat_width)
            offset = 4**layer_at
            for tap_index in range(KER):
                upstream = upstream + advanced(back_rows[:, :, tap_index], tap_index * offset)
    stacked_grads = jnp.stack(gradients)
    full_grad = all_reduce_wide(stacked_grads)
    new_momentum = momentum_rate * momentum + full_grad
    new_master = master - learn_rate * new_momentum
    new_teacher = ema_rate * teacher + (1.0 - ema_rate) * new_master
    return (new_master, new_momentum, new_teacher, embeddings)


def solution(mesh):
    in_specs = (
        P(("groups", "wide"), None),
        P(("groups", "wide")),
        P("groups"),
        P("groups", None),
        P("groups", None),
        P("groups", None),
    )
    out_specs = (
        P("groups", None),
        P("groups", None),
        P("groups", None),
        P(("groups", "wide"), None),
    )
    return jax.shard_map(local, mesh=mesh, in_specs=in_specs, out_specs=out_specs, check_vma=False)
```

```python
import jax
import jax.numpy as jnp
from jax import lax
from jax.sharding import PartitionSpec as P

KER = 3
SEQ = 256


tau_student = 1.0
tau_teacher = 0.5
momentum_rate = 0.9
learn_rate = 0.05
ema_rate = 0.996


def delayed(states, offset):
    length = states.shape[1]
    return jnp.concatenate(
        [jnp.zeros_like(states[:, :offset]), states[:, : length - offset]], axis=1
    )


def advanced(states, offset):
    length = states.shape[1]
    return jnp.concatenate([states[:, offset:], jnp.zeros_like(states[:, :offset])], axis=1)


def silu_slope(values):
    gate_value = jax.nn.sigmoid(values)
    return gate_value * (1.0 + values * (1.0 - gate_value))


def softmax_rows(values):
    shifted = values - lax.optimization_barrier(jnp.max(values, axis=-1, keepdims=True))
    raised = jnp.exp(shifted)
    total = lax.optimization_barrier(jnp.sum(raised, axis=-1, keepdims=True))
    return raised / total


def run_network(states, weights):
    stacked_list = []
    preacts = []
    for layer_at in range(weights.shape[0]):
        offset = 4**layer_at
        stacked = jnp.concatenate(
            [delayed(states, tap_index * offset) for tap_index in range(KER)], axis=2
        )
        preact = jnp.dot(
            stacked.reshape(-1, stacked.shape[2]),
            weights[layer_at],
            preferred_element_type=jnp.float32,
        ).reshape(states.shape)
        states = (states.astype(jnp.float32) + jax.nn.silu(preact)).astype(jnp.bfloat16)
        stacked_list.append(stacked)
        preacts.append(preact)
    return (states, stacked_list, preacts)


def prefix_count(hot):
    rows, width = hot.shape
    block = 128
    if rows % block:
        return jnp.cumsum(hot.astype(jnp.int32), axis=0)
    blocks = rows // block
    ramp = jnp.arange(block, dtype=jnp.int32)
    lower = (ramp[:, None] >= ramp[None, :]).astype(jnp.bfloat16)
    pieces = hot.astype(jnp.bfloat16).reshape(blocks, block, width)
    within = jnp.einsum("ij,bjk->bik", lower, pieces, preferred_element_type=jnp.float32)
    totals = within[:, -1, :].astype(jnp.bfloat16)
    steps = jnp.arange(blocks, dtype=jnp.int32)
    before = (steps[:, None] > steps[None, :]).astype(jnp.bfloat16)
    offsets = jnp.dot(before, totals, preferred_element_type=jnp.float32)
    return (within + offsets[:, None, :]).reshape(rows, width).astype(jnp.int32)


def route_rows(epoch_rows, row_object, object_slot):
    wide_count = lax.axis_size("wide")
    objects_all = object_slot.shape[0]
    per_dev = objects_all // wide_count
    rows_total = epoch_rows.shape[0]
    feat_width = epoch_rows.shape[1]
    capacity = rows_total // wide_count
    live_rows = row_object >= 0
    safe_object = jnp.maximum(row_object, 0)
    match_table = safe_object[:, None] == jnp.arange(objects_all, dtype=jnp.int32)[None, :]
    slot_of = jnp.sum(jnp.where(match_table, object_slot[None, :], 0), axis=1)
    owner_dev = slot_of // per_dev
    local_place = slot_of % per_dev
    owner_hot = (
        owner_dev[:, None] == jnp.arange(wide_count, dtype=jnp.int32)[None, :]
    ) & live_rows[:, None]
    running = prefix_count(owner_hot)
    send_rank = jnp.sum(jnp.where(owner_hot, running, 0), axis=1) - 1
    send_index = jnp.where(live_rows, owner_dev * capacity + send_rank, -1)
    pick = (
        jnp.arange(rows_total, dtype=jnp.int32)[:, None] == send_index[None, :]
    ).astype(jnp.bfloat16)
    place_hot = (
        (local_place[:, None] == jnp.arange(per_dev, dtype=jnp.int32)[None, :]) & live_rows[:, None]
    ).astype(jnp.bfloat16)
    sent = jnp.dot(
        pick, jnp.concatenate([epoch_rows, place_hot], axis=1), preferred_element_type=jnp.float32
    ).astype(jnp.bfloat16)
    send_rows = sent[:, :feat_width]
    send_place = sent[:, feat_width:]
    got_rows, got_place = (
        lax.all_to_all(
            send_rows.reshape(wide_count, capacity, feat_width),
            "wide",
            split_axis=0,
            concat_axis=0,
            tiled=True,
        ),
        lax.all_to_all(
            send_place.reshape(wide_count, capacity, per_dev),
            "wide",
            split_axis=0,
            concat_axis=0,
            tiled=True,
        ),
    )
    place_hot = got_place.reshape(-1, per_dev) > 0
    arrival = prefix_count(place_hot)
    position = jnp.sum(jnp.where(place_hot, arrival, 0), axis=1) - 1
    place_code = jnp.sum(
        jnp.where(place_hot, jnp.arange(per_dev, dtype=jnp.int32)[None, :], 0), axis=1
    )
    counts = jnp.sum(place_hot.astype(jnp.int32), axis=0)
    target = jnp.where(jnp.any(place_hot, axis=1), place_code * SEQ + position, -1)
    put = (
        jnp.arange(per_dev * SEQ, dtype=jnp.int32)[:, None] == target[None, :]
    ).astype(jnp.bfloat16)
    sequences = jnp.dot(
        put, got_rows.reshape(-1, feat_width), preferred_element_type=jnp.float32
    ).astype(jnp.bfloat16)
    return (sequences.reshape(per_dev, SEQ, feat_width), counts)


def all_reduce_wide(grads):
    wide_count = lax.axis_size("wide")
    steps = wide_count.bit_length() - 1
    assert 1 << steps == wide_count
    order_even = list(range(steps))
    order_odd = [0] + list(range(2, steps)) + [1] if steps > 2 else order_even
    me = lax.axis_index("wide")
    odd = me & 1

    def exchange_at(step):
        pairs = []
        for i in range(wide_count):
            dim = (order_odd if i & 1 else order_even)[step]
            pairs.append((i, i ^ (1 << dim)))
        bit_even = (me >> order_even[step]) & 1
        bit_odd = (me >> order_odd[step]) & 1
        return pairs, jnp.where(odd == 1, bit_odd, bit_even)

    buf = grads
    for step in range(steps):
        pairs, bit = exchange_at(step)
        half = buf.shape[1] // 2
        keep = lax.dynamic_slice_in_dim(buf, bit * half, half, axis=1)
        send = lax.dynamic_slice_in_dim(buf, (1 - bit) * half, half, axis=1)
        buf = keep + lax.ppermute(send, "wide", pairs)
    buf = buf.astype(jnp.bfloat16)
    for step in reversed(range(steps)):
        pairs, bit = exchange_at(step)
        got = lax.ppermute(buf, "wide", pairs)
        low = jnp.where(bit == 0, buf, got)
        high = jnp.where(bit == 0, got, buf)
        buf = jnp.concatenate([low, high], axis=1)
    return buf.reshape(buf.shape[0], -1).astype(jnp.float32)


def local(epoch_rows, row_object, object_slot, master, momentum, teacher):
    objects_all = object_slot.shape[0]
    feat_width = epoch_rows.shape[1]
    layer_total = master.shape[0]
    student_w = lax.optimization_barrier(master.reshape(layer_total, KER * feat_width, feat_width)).astype(jnp.bfloat16)
    teacher_w = lax.optimization_barrier(teacher.reshape(layer_total, KER * feat_width, feat_width)).astype(jnp.bfloat16)
    sequences, counts = route_rows(epoch_rows, row_object, object_slot)
    valid_mask = (jnp.arange(SEQ, dtype=jnp.int32)[None, :] < counts[:, None]).astype(jnp.float32)[
        :, :, None
    ]
    teacher_out = run_network(sequences, teacher_w)[0]
    student_out, stacked_list, preacts = run_network(sequences, student_w)
    partial_sum = jnp.sum(valid_mask * teacher_out.astype(jnp.float32), axis=(0, 1))
    number = jnp.sum(counts).astype(jnp.float32)
    wide_count = lax.axis_size("wide")
    stats = jnp.concatenate([partial_sum, jnp.full((128,), number, jnp.float32)])
    stats_all = stats
    for step in range(wide_count.bit_length() - 1):
        pairs = [(i, i ^ (1 << step)) for i in range(wide_count)]
        stats_all = stats_all + lax.ppermute(stats_all, "wide", pairs)
    total_sum = stats_all[:feat_width]
    count_all = stats_all[feat_width]
    center = total_sum / count_all
    teacher_prob = softmax_rows((teacher_out.astype(jnp.float32) - center) / tau_teacher)
    student_f = student_out.astype(jnp.float32)
    student_prob = softmax_rows(student_f / tau_student)
    embeddings = jnp.sum(valid_mask * student_f, axis=1) / counts.astype(jnp.float32)[:, None]
    upstream = valid_mask * (student_prob - teacher_prob) / (tau_student * objects_all)
    gradients = [None] * layer_total
    for layer_at in reversed(range(layer_total)):
        delta_bf = (upstream * silu_slope(preacts[layer_at])).astype(jnp.bfloat16)
        flat_delta = delta_bf.reshape(-1, feat_width)
        weight_grad = lax.dot_general(
            stacked_list[layer_at].reshape(-1, KER * feat_width),
            flat_delta,
            (((0,), (0,)), ((), ())),
            preferred_element_type=jnp.float32,
        )
        gradients[layer_at] = weight_grad
        if layer_at > 0:
            back_rows = lax.dot_general(
                flat_delta,
                student_w[layer_at],
                (((1,), (1,)), ((), ())),
                preferred_element_type=jnp.float32,
            ).reshape(sequences.shape[0], SEQ, KER, feat_width)
            offset = 4**layer_at
            for tap_index in range(KER):
                upstream = upstream + advanced(back_rows[:, :, tap_index], tap_index * offset)
    stacked_grads = jnp.stack(gradients)
    full_grad = all_reduce_wide(stacked_grads)
    new_momentum = momentum_rate * momentum + full_grad
    new_master = master - learn_rate * new_momentum
    new_teacher = ema_rate * teacher + (1.0 - ema_rate) * new_master
    return (new_master, new_momentum, new_teacher, embeddings)


def solution(mesh):
    in_specs = (
        P(("groups", "wide"), None),
        P(("groups", "wide")),
        P("groups"),
        P("groups", None),
        P("groups", None),
        P("groups", None),
    )
    out_specs = (
        P("groups", None),
        P("groups", None),
        P("groups", None),
        P(("groups", "wide"), None),
    )
    return jax.shard_map(local, mesh=mesh, in_specs=in_specs, out_specs=out_specs, check_vma=False)
```

```python
import jax
import jax.numpy as jnp
from jax import lax
from jax.sharding import PartitionSpec as P

KER = 3
SEQ = 256


tau_student = 1.0
tau_teacher = 0.5
momentum_rate = 0.9
learn_rate = 0.05
ema_rate = 0.996


def delayed(states, offset):
    length = states.shape[1]
    return jnp.concatenate(
        [jnp.zeros_like(states[:, :offset]), states[:, : length - offset]], axis=1
    )


def advanced(states, offset):
    length = states.shape[1]
    return jnp.concatenate([states[:, offset:], jnp.zeros_like(states[:, :offset])], axis=1)


def silu_slope(values):
    gate_value = jax.nn.sigmoid(values)
    return gate_value * (1.0 + values * (1.0 - gate_value))


def softmax_rows(values):
    shifted = values - lax.optimization_barrier(jnp.max(values, axis=-1, keepdims=True))
    raised = jnp.exp(shifted)
    total = lax.optimization_barrier(jnp.sum(raised, axis=-1, keepdims=True))
    return raised / total


def run_network(states, weights):
    stacked_list = []
    preacts = []
    for layer_at in range(weights.shape[0]):
        offset = 4**layer_at
        stacked = jnp.concatenate(
            [delayed(states, tap_index * offset) for tap_index in range(KER)], axis=2
        )
        preact = jnp.dot(
            stacked.reshape(-1, stacked.shape[2]),
            weights[layer_at],
            preferred_element_type=jnp.float32,
        ).reshape(states.shape)
        states = (states.astype(jnp.float32) + jax.nn.silu(preact)).astype(jnp.bfloat16)
        stacked_list.append(stacked)
        preacts.append(preact)
    return (states, stacked_list, preacts)


def prefix_count(hot):
    rows, width = hot.shape
    block = 128
    if rows % block:
        return jnp.cumsum(hot.astype(jnp.int32), axis=0)
    blocks = rows // block
    ramp = jnp.arange(block, dtype=jnp.int32)
    lower = (ramp[:, None] >= ramp[None, :]).astype(jnp.bfloat16)
    pieces = hot.astype(jnp.bfloat16).reshape(blocks, block, width)
    within = jnp.einsum("ij,bjk->bik", lower, pieces, preferred_element_type=jnp.float32)
    totals = within[:, -1, :].astype(jnp.bfloat16)
    steps = jnp.arange(blocks, dtype=jnp.int32)
    before = (steps[:, None] > steps[None, :]).astype(jnp.bfloat16)
    offsets = jnp.dot(before, totals, preferred_element_type=jnp.float32)
    return (within + offsets[:, None, :]).reshape(rows, width).astype(jnp.int32)


def route_rows(epoch_rows, row_object, object_slot):
    wide_count = lax.axis_size("wide")
    objects_all = object_slot.shape[0]
    per_dev = objects_all // wide_count
    rows_total = epoch_rows.shape[0]
    feat_width = epoch_rows.shape[1]
    capacity = rows_total // wide_count
    live_rows = row_object >= 0
    safe_object = jnp.maximum(row_object, 0)
    match_table = safe_object[:, None] == jnp.arange(objects_all, dtype=jnp.int32)[None, :]
    slot_of = jnp.sum(jnp.where(match_table, object_slot[None, :], 0), axis=1)
    owner_dev = slot_of // per_dev
    local_place = slot_of % per_dev
    owner_hot = (
        owner_dev[:, None] == jnp.arange(wide_count, dtype=jnp.int32)[None, :]
    ) & live_rows[:, None]
    running = prefix_count(owner_hot)
    send_rank = jnp.sum(jnp.where(owner_hot, running, 0), axis=1) - 1
    send_index = jnp.where(live_rows, owner_dev * capacity + send_rank, -1)
    pick = (
        jnp.arange(rows_total, dtype=jnp.int32)[:, None] == send_index[None, :]
    ).astype(jnp.bfloat16)
    place_hot = (
        (local_place[:, None] == jnp.arange(per_dev, dtype=jnp.int32)[None, :]) & live_rows[:, None]
    ).astype(jnp.bfloat16)
    sent = jnp.dot(
        pick, jnp.concatenate([epoch_rows, place_hot], axis=1), preferred_element_type=jnp.float32
    ).astype(jnp.bfloat16)
    send_rows = sent[:, :feat_width]
    send_place = sent[:, feat_width:]
    got_rows, got_place = (
        lax.all_to_all(
            send_rows.reshape(wide_count, capacity, feat_width),
            "wide",
            split_axis=0,
            concat_axis=0,
            tiled=True,
        ),
        lax.all_to_all(
            send_place.reshape(wide_count, capacity, per_dev),
            "wide",
            split_axis=0,
            concat_axis=0,
            tiled=True,
        ),
    )
    place_hot = got_place.reshape(-1, per_dev) > 0
    arrival = prefix_count(place_hot)
    position = jnp.sum(jnp.where(place_hot, arrival, 0), axis=1) - 1
    place_code = jnp.sum(
        jnp.where(place_hot, jnp.arange(per_dev, dtype=jnp.int32)[None, :], 0), axis=1
    )
    counts = jnp.sum(place_hot.astype(jnp.int32), axis=0)
    target = jnp.where(jnp.any(place_hot, axis=1), place_code * SEQ + position, -1)
    put = (
        jnp.arange(per_dev * SEQ, dtype=jnp.int32)[:, None] == target[None, :]
    ).astype(jnp.bfloat16)
    sequences = jnp.dot(
        put, got_rows.reshape(-1, feat_width), preferred_element_type=jnp.float32
    ).astype(jnp.bfloat16)
    return (sequences.reshape(per_dev, SEQ, feat_width), counts)


def all_reduce_wide(grads):
    wide_count = lax.axis_size("wide")
    steps = wide_count.bit_length() - 1
    assert 1 << steps == wide_count
    order_even = list(range(steps))
    order_odd = [0] + list(range(2, steps)) + [1] if steps > 2 else order_even
    me = lax.axis_index("wide")
    odd = me & 1

    def exchange_at(step):
        pairs = []
        for i in range(wide_count):
            dim = (order_odd if i & 1 else order_even)[step]
            pairs.append((i, i ^ (1 << dim)))
        bit_even = (me >> order_even[step]) & 1
        bit_odd = (me >> order_odd[step]) & 1
        return pairs, jnp.where(odd == 1, bit_odd, bit_even)

    buf = grads
    for step in range(steps):
        pairs, bit = exchange_at(step)
        half = buf.shape[1] // 2
        keep = lax.dynamic_slice_in_dim(buf, bit * half, half, axis=1)
        send = lax.dynamic_slice_in_dim(buf, (1 - bit) * half, half, axis=1)
        buf = keep + lax.ppermute(send, "wide", pairs)
    buf = buf.astype(jnp.bfloat16).reshape(buf.shape[0], -1)
    for step in reversed(range(steps)):
        pairs, bit = exchange_at(step)
        got = lax.ppermute(buf, "wide", pairs)
        low = jnp.where(bit == 0, buf, got)
        high = jnp.where(bit == 0, got, buf)
        buf = jnp.concatenate([low, high], axis=1)
    return buf.astype(jnp.float32)


def local(epoch_rows, row_object, object_slot, master, momentum, teacher):
    objects_all = object_slot.shape[0]
    feat_width = epoch_rows.shape[1]
    layer_total = master.shape[0]
    student_w = lax.optimization_barrier(master.reshape(layer_total, KER * feat_width, feat_width)).astype(jnp.bfloat16)
    teacher_w = lax.optimization_barrier(teacher.reshape(layer_total, KER * feat_width, feat_width)).astype(jnp.bfloat16)
    sequences, counts = route_rows(epoch_rows, row_object, object_slot)
    valid_mask = (jnp.arange(SEQ, dtype=jnp.int32)[None, :] < counts[:, None]).astype(jnp.float32)[
        :, :, None
    ]
    teacher_out = run_network(sequences, teacher_w)[0]
    student_out, stacked_list, preacts = run_network(sequences, student_w)
    partial_sum = jnp.sum(valid_mask * teacher_out.astype(jnp.float32), axis=(0, 1))
    number = jnp.sum(counts).astype(jnp.float32)
    wide_count = lax.axis_size("wide")
    stats = jnp.concatenate([partial_sum, jnp.full((128,), number, jnp.float32)])
    gathered = lax.all_to_all(
        jnp.broadcast_to(stats[None, :], (wide_count, stats.shape[0])),
        "wide", split_axis=0, concat_axis=0, tiled=True,
    )
    stats_all = jnp.sum(gathered, axis=0)
    total_sum = stats_all[:feat_width]
    count_all = stats_all[feat_width]
    center = total_sum / count_all
    teacher_prob = softmax_rows((teacher_out.astype(jnp.float32) - center) / tau_teacher)
    student_f = student_out.astype(jnp.float32)
    student_prob = softmax_rows(student_f / tau_student)
    embeddings = jnp.sum(valid_mask * student_f, axis=1) / counts.astype(jnp.float32)[:, None]
    upstream = valid_mask * (student_prob - teacher_prob) / (tau_student * objects_all)
    gradients = [None] * layer_total
    for layer_at in reversed(range(layer_total)):
        delta_bf = (upstream * silu_slope(preacts[layer_at])).astype(jnp.bfloat16)
        flat_delta = delta_bf.reshape(-1, feat_width)
        weight_grad = lax.dot_general(
            stacked_list[layer_at].reshape(-1, KER * feat_width),
            flat_delta,
            (((0,), (0,)), ((), ())),
            preferred_element_type=jnp.float32,
        )
        gradients[layer_at] = weight_grad
        if layer_at > 0:
            back_rows = lax.dot_general(
                flat_delta,
                student_w[layer_at],
                (((1,), (1,)), ((), ())),
                preferred_element_type=jnp.float32,
            ).reshape(sequences.shape[0], SEQ, KER, feat_width)
            offset = 4**layer_at
            for tap_index in range(KER):
                upstream = upstream + advanced(back_rows[:, :, tap_index], tap_index * offset)
    stacked_grads = jnp.stack(gradients)
    full_grad = all_reduce_wide(stacked_grads)
    new_momentum = momentum_rate * momentum + full_grad
    new_master = master - learn_rate * new_momentum
    new_teacher = ema_rate * teacher + (1.0 - ema_rate) * new_master
    return (new_master, new_momentum, new_teacher, embeddings)


def solution(mesh):
    in_specs = (
        P(("groups", "wide"), None),
        P(("groups", "wide")),
        P("groups"),
        P("groups", None),
        P("groups", None),
        P("groups", None),
    )
    out_specs = (
        P("groups", None),
        P("groups", None),
        P("groups", None),
        P(("groups", "wide"), None),
    )
    return jax.shard_map(local, mesh=mesh, in_specs=in_specs, out_specs=out_specs, check_vma=False)
```

```python
import jax
import jax.numpy as jnp
from jax import lax
from jax.sharding import PartitionSpec as P

KER = 3
SEQ = 256


tau_student = 1.0
tau_teacher = 0.5
momentum_rate = 0.9
learn_rate = 0.05
ema_rate = 0.996


def delayed(states, offset):
    length = states.shape[1]
    return jnp.concatenate(
        [jnp.zeros_like(states[:, :offset]), states[:, : length - offset]], axis=1
    )


def advanced(states, offset):
    length = states.shape[1]
    return jnp.concatenate([states[:, offset:], jnp.zeros_like(states[:, :offset])], axis=1)


def silu_slope(values):
    gate_value = jax.nn.sigmoid(values)
    return gate_value * (1.0 + values * (1.0 - gate_value))


def softmax_rows(values):
    shifted = values - lax.optimization_barrier(jnp.max(values, axis=-1, keepdims=True))
    raised = jnp.exp(shifted)
    total = lax.optimization_barrier(jnp.sum(raised, axis=-1, keepdims=True))
    return raised / total


def run_network(states, weights):
    stacked_list = []
    preacts = []
    for layer_at in range(weights.shape[0]):
        offset = 4**layer_at
        stacked = jnp.concatenate(
            [delayed(states, tap_index * offset) for tap_index in range(KER)], axis=2
        )
        preact = jnp.dot(
            stacked.reshape(-1, stacked.shape[2]),
            weights[layer_at],
            preferred_element_type=jnp.float32,
        ).reshape(states.shape)
        states = (states.astype(jnp.float32) + jax.nn.silu(preact)).astype(jnp.bfloat16)
        stacked_list.append(stacked)
        preacts.append(preact)
    return (states, stacked_list, preacts)


def prefix_count(hot):
    rows, width = hot.shape
    block = 128
    if rows % block:
        return jnp.cumsum(hot.astype(jnp.int32), axis=0)
    blocks = rows // block
    ramp = jnp.arange(block, dtype=jnp.int32)
    lower = (ramp[:, None] >= ramp[None, :]).astype(jnp.bfloat16)
    pieces = hot.astype(jnp.bfloat16).reshape(blocks, block, width)
    within = jnp.einsum("ij,bjk->bik", lower, pieces, preferred_element_type=jnp.float32)
    totals = within[:, -1, :].astype(jnp.bfloat16)
    steps = jnp.arange(blocks, dtype=jnp.int32)
    before = (steps[:, None] > steps[None, :]).astype(jnp.bfloat16)
    offsets = jnp.dot(before, totals, preferred_element_type=jnp.float32)
    return (within + offsets[:, None, :]).reshape(rows, width).astype(jnp.int32)


def route_rows(epoch_rows, row_object, object_slot):
    wide_count = lax.axis_size("wide")
    objects_all = object_slot.shape[0]
    per_dev = objects_all // wide_count
    rows_total = epoch_rows.shape[0]
    feat_width = epoch_rows.shape[1]
    capacity = rows_total // wide_count
    live_rows = row_object >= 0
    safe_object = jnp.maximum(row_object, 0)
    match_table = safe_object[:, None] == jnp.arange(objects_all, dtype=jnp.int32)[None, :]
    slot_of = jnp.sum(jnp.where(match_table, object_slot[None, :], 0), axis=1)
    owner_dev = slot_of // per_dev
    local_place = slot_of % per_dev
    owner_hot = (
        owner_dev[:, None] == jnp.arange(wide_count, dtype=jnp.int32)[None, :]
    ) & live_rows[:, None]
    running = prefix_count(owner_hot)
    send_rank = jnp.sum(jnp.where(owner_hot, running, 0), axis=1) - 1
    send_index = jnp.where(live_rows, owner_dev * capacity + send_rank, -1)
    pick = (
        jnp.arange(rows_total, dtype=jnp.int32)[:, None] == send_index[None, :]
    ).astype(jnp.bfloat16)
    place_hot = (
        (local_place[:, None] == jnp.arange(per_dev, dtype=jnp.int32)[None, :]) & live_rows[:, None]
    ).astype(jnp.bfloat16)
    sent = jnp.dot(
        pick, jnp.concatenate([epoch_rows, place_hot], axis=1), preferred_element_type=jnp.float32
    ).astype(jnp.bfloat16)
    send_rows = sent[:, :feat_width]
    send_place = sent[:, feat_width:]
    got_rows = lax.all_to_all(
        send_rows.reshape(wide_count, capacity, feat_width),
        "wide",
        split_axis=0,
        concat_axis=0,
        tiled=True,
    )
    place_chunks = send_place.reshape(wide_count, capacity, per_dev)
    if wide_count <= 16 and wide_count & (wide_count - 1) == 0:
        me = lax.axis_index("wide")
        arrived = [lax.dynamic_index_in_dim(place_chunks, me, axis=0, keepdims=False)]
        for shift in range(1, wide_count):
            outgoing = lax.dynamic_index_in_dim(place_chunks, me ^ shift, axis=0, keepdims=False)
            pairs = [(i, i ^ shift) for i in range(wide_count)]
            arrived.append(lax.ppermute(outgoing, "wide", pairs))
        by_shift = jnp.stack(arrived)
        sources = jnp.arange(wide_count, dtype=jnp.int32)
        got_place = jnp.take(by_shift, sources ^ me, axis=0)
    else:
        got_place = lax.all_to_all(place_chunks, "wide", split_axis=0, concat_axis=0, tiled=True)
    place_hot = got_place.reshape(-1, per_dev) > 0
    arrival = prefix_count(place_hot)
    position = jnp.sum(jnp.where(place_hot, arrival, 0), axis=1) - 1
    place_code = jnp.sum(
        jnp.where(place_hot, jnp.arange(per_dev, dtype=jnp.int32)[None, :], 0), axis=1
    )
    counts = jnp.sum(place_hot.astype(jnp.int32), axis=0)
    target = jnp.where(jnp.any(place_hot, axis=1), place_code * SEQ + position, -1)
    put = (
        jnp.arange(per_dev * SEQ, dtype=jnp.int32)[:, None] == target[None, :]
    ).astype(jnp.bfloat16)
    sequences = jnp.dot(
        put, got_rows.reshape(-1, feat_width), preferred_element_type=jnp.float32
    ).astype(jnp.bfloat16)
    return (sequences.reshape(per_dev, SEQ, feat_width), counts)


def all_reduce_wide(grads):
    wide_count = lax.axis_size("wide")
    steps = wide_count.bit_length() - 1
    assert 1 << steps == wide_count
    order_even = list(range(steps))
    order_odd = [0] + list(range(2, steps)) + [1] if steps > 2 else order_even
    me = lax.axis_index("wide")
    odd = me & 1

    def exchange_at(step):
        pairs = []
        for i in range(wide_count):
            dim = (order_odd if i & 1 else order_even)[step]
            pairs.append((i, i ^ (1 << dim)))
        bit_even = (me >> order_even[step]) & 1
        bit_odd = (me >> order_odd[step]) & 1
        return pairs, jnp.where(odd == 1, bit_odd, bit_even)

    buf = grads
    for step in range(steps):
        pairs, bit = exchange_at(step)
        half = buf.shape[1] // 2
        keep = lax.dynamic_slice_in_dim(buf, bit * half, half, axis=1)
        send = lax.dynamic_slice_in_dim(buf, (1 - bit) * half, half, axis=1)
        buf = keep + lax.ppermute(send, "wide", pairs)
    buf = buf.astype(jnp.bfloat16)
    for step in reversed(range(steps)):
        pairs, bit = exchange_at(step)
        got = lax.ppermute(buf, "wide", pairs)
        low = jnp.where(bit == 0, buf, got)
        high = jnp.where(bit == 0, got, buf)
        buf = jnp.concatenate([low, high], axis=1)
    return buf.reshape(buf.shape[0], -1).astype(jnp.float32)


def local(epoch_rows, row_object, object_slot, master, momentum, teacher):
    objects_all = object_slot.shape[0]
    feat_width = epoch_rows.shape[1]
    layer_total = master.shape[0]
    student_w = lax.optimization_barrier(master.reshape(layer_total, KER * feat_width, feat_width)).astype(jnp.bfloat16)
    teacher_w = lax.optimization_barrier(teacher.reshape(layer_total, KER * feat_width, feat_width)).astype(jnp.bfloat16)
    sequences, counts = route_rows(epoch_rows, row_object, object_slot)
    valid_mask = (jnp.arange(SEQ, dtype=jnp.int32)[None, :] < counts[:, None]).astype(jnp.float32)[
        :, :, None
    ]
    teacher_out = run_network(sequences, teacher_w)[0]
    student_out, stacked_list, preacts = run_network(sequences, student_w)
    partial_sum = jnp.sum(valid_mask * teacher_out.astype(jnp.float32), axis=(0, 1))
    number = jnp.sum(counts).astype(jnp.float32)
    wide_count = lax.axis_size("wide")
    stats = jnp.concatenate([partial_sum, jnp.full((128,), number, jnp.float32)])
    gathered = lax.all_to_all(
        jnp.broadcast_to(stats[None, :], (wide_count, stats.shape[0])),
        "wide", split_axis=0, concat_axis=0, tiled=True,
    )
    stats_all = jnp.sum(gathered, axis=0)
    total_sum = stats_all[:feat_width]
    count_all = stats_all[feat_width]
    center = total_sum / count_all
    teacher_prob = softmax_rows((teacher_out.astype(jnp.float32) - center) / tau_teacher)
    student_f = student_out.astype(jnp.float32)
    student_prob = softmax_rows(student_f / tau_student)
    embeddings = jnp.sum(valid_mask * student_f, axis=1) / counts.astype(jnp.float32)[:, None]
    upstream = valid_mask * (student_prob - teacher_prob) / (tau_student * objects_all)
    gradients = [None] * layer_total
    for layer_at in reversed(range(layer_total)):
        delta_bf = (upstream * silu_slope(preacts[layer_at])).astype(jnp.bfloat16)
        flat_delta = delta_bf.reshape(-1, feat_width)
        weight_grad = lax.dot_general(
            stacked_list[layer_at].reshape(-1, KER * feat_width),
            flat_delta,
            (((0,), (0,)), ((), ())),
            preferred_element_type=jnp.float32,
        )
        gradients[layer_at] = weight_grad
        if layer_at > 0:
            back_rows = lax.dot_general(
                flat_delta,
                student_w[layer_at],
                (((1,), (1,)), ((), ())),
                preferred_element_type=jnp.float32,
            ).reshape(sequences.shape[0], SEQ, KER, feat_width)
            offset = 4**layer_at
            for tap_index in range(KER):
                upstream = upstream + advanced(back_rows[:, :, tap_index], tap_index * offset)
    stacked_grads = jnp.stack(gradients)
    full_grad = all_reduce_wide(stacked_grads)
    new_momentum = momentum_rate * momentum + full_grad
    new_master = master - learn_rate * new_momentum
    new_teacher = ema_rate * teacher + (1.0 - ema_rate) * new_master
    return (new_master, new_momentum, new_teacher, embeddings)


def solution(mesh):
    in_specs = (
        P(("groups", "wide"), None),
        P(("groups", "wide")),
        P("groups"),
        P("groups", None),
        P("groups", None),
        P("groups", None),
    )
    out_specs = (
        P("groups", None),
        P("groups", None),
        P("groups", None),
        P(("groups", "wide"), None),
    )
    return jax.shard_map(local, mesh=mesh, in_specs=in_specs, out_specs=out_specs, check_vma=False)
```

```python
import jax
import jax.numpy as jnp
from jax import lax
from jax.sharding import PartitionSpec as P

KER = 3
SEQ = 256


tau_student = 1.0
tau_teacher = 0.5
momentum_rate = 0.9
learn_rate = 0.05
ema_rate = 0.996


def delayed(states, offset):
    length = states.shape[1]
    return jnp.concatenate(
        [jnp.zeros_like(states[:, :offset]), states[:, : length - offset]], axis=1
    )


def advanced(states, offset):
    length = states.shape[1]
    return jnp.concatenate([states[:, offset:], jnp.zeros_like(states[:, :offset])], axis=1)


def silu_slope(values):
    gate_value = jax.nn.sigmoid(values)
    return gate_value * (1.0 + values * (1.0 - gate_value))


def softmax_rows(values):
    shifted = values - lax.optimization_barrier(jnp.max(values, axis=-1, keepdims=True))
    raised = jnp.exp(shifted)
    total = lax.optimization_barrier(jnp.sum(raised, axis=-1, keepdims=True))
    return raised / total


def run_network(states, weights):
    stacked_list = []
    preacts = []
    for layer_at in range(weights.shape[0]):
        offset = 4**layer_at
        stacked = jnp.concatenate(
            [delayed(states, tap_index * offset) for tap_index in range(KER)], axis=2
        )
        preact = jnp.dot(
            stacked.reshape(-1, stacked.shape[2]),
            weights[layer_at],
            preferred_element_type=jnp.float32,
        ).reshape(states.shape)
        states = (states.astype(jnp.float32) + jax.nn.silu(preact)).astype(jnp.bfloat16)
        stacked_list.append(stacked)
        preacts.append(preact)
    return (states, stacked_list, preacts)


def prefix_count(hot):
    rows, width = hot.shape
    block = 128
    if rows % block:
        return jnp.cumsum(hot.astype(jnp.int32), axis=0)
    blocks = rows // block
    ramp = jnp.arange(block, dtype=jnp.int32)
    lower = (ramp[:, None] >= ramp[None, :]).astype(jnp.bfloat16)
    pieces = hot.astype(jnp.bfloat16).reshape(blocks, block, width)
    within = jnp.einsum("ij,bjk->bik", lower, pieces, preferred_element_type=jnp.float32)
    totals = within[:, -1, :].astype(jnp.bfloat16)
    steps = jnp.arange(blocks, dtype=jnp.int32)
    before = (steps[:, None] > steps[None, :]).astype(jnp.bfloat16)
    offsets = jnp.dot(before, totals, preferred_element_type=jnp.float32)
    return (within + offsets[:, None, :]).reshape(rows, width).astype(jnp.int32)


def run_pair(states, teacher_w, student_w):
    width = states.shape[2]
    stacked = jnp.concatenate([delayed(states, tap_index) for tap_index in range(KER)], axis=2)
    joint = jnp.dot(
        stacked.reshape(-1, stacked.shape[2]),
        jnp.concatenate([teacher_w[0], student_w[0]], axis=1),
        preferred_element_type=jnp.float32,
    )
    teacher_pre = joint[:, :width].reshape(states.shape)
    student_pre = joint[:, width:].reshape(states.shape)
    base = states.astype(jnp.float32)
    teacher_h = (base + jax.nn.silu(teacher_pre)).astype(jnp.bfloat16)
    student_h = (base + jax.nn.silu(student_pre)).astype(jnp.bfloat16)
    stacked_list = [stacked]
    preacts = [student_pre]
    for layer_at in range(1, student_w.shape[0]):
        offset = 4**layer_at
        for is_student in (False, True):
            current = student_h if is_student else teacher_h
            weights = student_w if is_student else teacher_w
            layered = jnp.concatenate(
                [delayed(current, tap_index * offset) for tap_index in range(KER)], axis=2
            )
            preact = jnp.dot(
                layered.reshape(-1, layered.shape[2]),
                weights[layer_at],
                preferred_element_type=jnp.float32,
            ).reshape(states.shape)
            updated = (current.astype(jnp.float32) + jax.nn.silu(preact)).astype(jnp.bfloat16)
            if is_student:
                student_h = updated
                stacked_list.append(layered)
                preacts.append(preact)
            else:
                teacher_h = updated
    return (teacher_h, student_h, stacked_list, preacts)


def route_rows(epoch_rows, row_object, object_slot):
    wide_count = lax.axis_size("wide")
    objects_all = object_slot.shape[0]
    per_dev = objects_all // wide_count
    rows_total = epoch_rows.shape[0]
    feat_width = epoch_rows.shape[1]
    capacity = rows_total // wide_count
    live_rows = row_object >= 0
    safe_object = jnp.maximum(row_object, 0)
    match_table = safe_object[:, None] == jnp.arange(objects_all, dtype=jnp.int32)[None, :]
    slot_of = jnp.sum(jnp.where(match_table, object_slot[None, :], 0), axis=1)
    owner_dev = slot_of // per_dev
    local_place = slot_of % per_dev
    owner_hot = (
        owner_dev[:, None] == jnp.arange(wide_count, dtype=jnp.int32)[None, :]
    ) & live_rows[:, None]
    running = prefix_count(owner_hot)
    send_rank = jnp.sum(jnp.where(owner_hot, running, 0), axis=1) - 1
    send_index = jnp.where(live_rows, owner_dev * capacity + send_rank, -1)
    pick = (
        jnp.arange(rows_total, dtype=jnp.int32)[:, None] == send_index[None, :]
    ).astype(jnp.bfloat16)
    place_hot = (
        (local_place[:, None] == jnp.arange(per_dev, dtype=jnp.int32)[None, :]) & live_rows[:, None]
    ).astype(jnp.bfloat16)
    sent = jnp.dot(
        pick, jnp.concatenate([epoch_rows, place_hot], axis=1), preferred_element_type=jnp.float32
    ).astype(jnp.bfloat16)
    send_rows = sent[:, :feat_width]
    send_place = sent[:, feat_width:]
    got_rows, got_place = (
        lax.all_to_all(
            send_rows.reshape(wide_count, capacity, feat_width),
            "wide",
            split_axis=0,
            concat_axis=0,
            tiled=True,
        ),
        lax.all_to_all(
            send_place.reshape(wide_count, capacity, per_dev),
            "wide",
            split_axis=0,
            concat_axis=0,
            tiled=True,
        ),
    )
    place_hot = got_place.reshape(-1, per_dev) > 0
    arrival = prefix_count(place_hot)
    position = jnp.sum(jnp.where(place_hot, arrival, 0), axis=1) - 1
    place_code = jnp.sum(
        jnp.where(place_hot, jnp.arange(per_dev, dtype=jnp.int32)[None, :], 0), axis=1
    )
    counts = jnp.sum(place_hot.astype(jnp.int32), axis=0)
    target = jnp.where(jnp.any(place_hot, axis=1), place_code * SEQ + position, -1)
    put = (
        jnp.arange(per_dev * SEQ, dtype=jnp.int32)[:, None] == target[None, :]
    ).astype(jnp.bfloat16)
    sequences = jnp.dot(
        put, got_rows.reshape(-1, feat_width), preferred_element_type=jnp.float32
    ).astype(jnp.bfloat16)
    return (sequences.reshape(per_dev, SEQ, feat_width), counts)


def all_reduce_wide(grads):
    wide_count = lax.axis_size("wide")
    steps = wide_count.bit_length() - 1
    assert 1 << steps == wide_count
    order_even = list(range(steps))
    order_odd = [0] + list(range(2, steps)) + [1] if steps > 2 else order_even
    me = lax.axis_index("wide")
    odd = me & 1

    def exchange_at(step):
        pairs = []
        for i in range(wide_count):
            dim = (order_odd if i & 1 else order_even)[step]
            pairs.append((i, i ^ (1 << dim)))
        bit_even = (me >> order_even[step]) & 1
        bit_odd = (me >> order_odd[step]) & 1
        return pairs, jnp.where(odd == 1, bit_odd, bit_even)

    buf = grads
    for step in range(steps):
        pairs, bit = exchange_at(step)
        half = buf.shape[1] // 2
        keep = lax.dynamic_slice_in_dim(buf, bit * half, half, axis=1)
        send = lax.dynamic_slice_in_dim(buf, (1 - bit) * half, half, axis=1)
        buf = keep + lax.ppermute(send, "wide", pairs)
    buf = buf.astype(jnp.bfloat16)
    for step in reversed(range(steps)):
        pairs, bit = exchange_at(step)
        got = lax.ppermute(buf, "wide", pairs)
        low = jnp.where(bit == 0, buf, got)
        high = jnp.where(bit == 0, got, buf)
        buf = jnp.concatenate([low, high], axis=1)
    return buf.reshape(buf.shape[0], -1).astype(jnp.float32)


def local(epoch_rows, row_object, object_slot, master, momentum, teacher):
    objects_all = object_slot.shape[0]
    feat_width = epoch_rows.shape[1]
    layer_total = master.shape[0]
    student_w = lax.optimization_barrier(master.reshape(layer_total, KER * feat_width, feat_width)).astype(jnp.bfloat16)
    teacher_w = lax.optimization_barrier(teacher.reshape(layer_total, KER * feat_width, feat_width)).astype(jnp.bfloat16)
    sequences, counts = route_rows(epoch_rows, row_object, object_slot)
    valid_mask = (jnp.arange(SEQ, dtype=jnp.int32)[None, :] < counts[:, None]).astype(jnp.float32)[
        :, :, None
    ]
    teacher_out, student_out, stacked_list, preacts = run_pair(sequences, teacher_w, student_w)
    partial_sum = jnp.sum(valid_mask * teacher_out.astype(jnp.float32), axis=(0, 1))
    number = jnp.sum(counts).astype(jnp.float32)
    wide_count = lax.axis_size("wide")
    stats = jnp.concatenate([partial_sum, jnp.full((128,), number, jnp.float32)])
    gathered = lax.all_to_all(
        jnp.broadcast_to(stats[None, :], (wide_count, stats.shape[0])),
        "wide", split_axis=0, concat_axis=0, tiled=True,
    )
    stats_all = jnp.sum(gathered, axis=0)
    total_sum = stats_all[:feat_width]
    count_all = stats_all[feat_width]
    center = total_sum / count_all
    teacher_prob = softmax_rows((teacher_out.astype(jnp.float32) - center) / tau_teacher)
    student_f = student_out.astype(jnp.float32)
    student_prob = softmax_rows(student_f / tau_student)
    embeddings = jnp.sum(valid_mask * student_f, axis=1) / counts.astype(jnp.float32)[:, None]
    upstream = valid_mask * (student_prob - teacher_prob) / (tau_student * objects_all)
    gradients = [None] * layer_total
    for layer_at in reversed(range(layer_total)):
        delta_bf = (upstream * silu_slope(preacts[layer_at])).astype(jnp.bfloat16)
        flat_delta = delta_bf.reshape(-1, feat_width)
        weight_grad = lax.dot_general(
            stacked_list[layer_at].reshape(-1, KER * feat_width),
            flat_delta,
            (((0,), (0,)), ((), ())),
            preferred_element_type=jnp.float32,
        )
        gradients[layer_at] = weight_grad
        if layer_at > 0:
            back_rows = lax.dot_general(
                flat_delta,
                student_w[layer_at],
                (((1,), (1,)), ((), ())),
                preferred_element_type=jnp.float32,
            ).reshape(sequences.shape[0], SEQ, KER, feat_width)
            offset = 4**layer_at
            for tap_index in range(KER):
                upstream = upstream + advanced(back_rows[:, :, tap_index], tap_index * offset)
    stacked_grads = jnp.stack(gradients)
    full_grad = all_reduce_wide(stacked_grads)
    new_momentum = momentum_rate * momentum + full_grad
    new_master = master - learn_rate * new_momentum
    new_teacher = ema_rate * teacher + (1.0 - ema_rate) * new_master
    return (new_master, new_momentum, new_teacher, embeddings)


def solution(mesh):
    in_specs = (
        P(("groups", "wide"), None),
        P(("groups", "wide")),
        P("groups"),
        P("groups", None),
        P("groups", None),
        P("groups", None),
    )
    out_specs = (
        P("groups", None),
        P("groups", None),
        P("groups", None),
        P(("groups", "wide"), None),
    )
    return jax.shard_map(local, mesh=mesh, in_specs=in_specs, out_specs=out_specs, check_vma=False)
```

```python
import jax
import jax.numpy as jnp
from jax import lax
from jax.sharding import PartitionSpec as P

KER = 3
SEQ = 256


tau_student = 1.0
tau_teacher = 0.5
momentum_rate = 0.9
learn_rate = 0.05
ema_rate = 0.996


def delayed(states, offset):
    length = states.shape[1]
    return jnp.concatenate(
        [jnp.zeros_like(states[:, :offset]), states[:, : length - offset]], axis=1
    )


def advanced(states, offset):
    length = states.shape[1]
    return jnp.concatenate([states[:, offset:], jnp.zeros_like(states[:, :offset])], axis=1)


def silu_slope(values):
    gate_value = jax.nn.sigmoid(values)
    return gate_value * (1.0 + values * (1.0 - gate_value))


def softmax_rows(values):
    shifted = values - lax.optimization_barrier(jnp.max(values, axis=-1, keepdims=True))
    raised = jnp.exp(shifted)
    total = lax.optimization_barrier(jnp.sum(raised, axis=-1, keepdims=True))
    return raised / total


def run_network(states, weights):
    stacked_list = []
    preacts = []
    for layer_at in range(weights.shape[0]):
        offset = 4**layer_at
        stacked = jnp.concatenate(
            [delayed(states, tap_index * offset) for tap_index in range(KER)], axis=2
        )
        preact = jnp.dot(
            stacked.reshape(-1, stacked.shape[2]),
            weights[layer_at],
            preferred_element_type=jnp.float32,
        ).reshape(states.shape)
        states = (states.astype(jnp.float32) + jax.nn.silu(preact)).astype(jnp.bfloat16)
        stacked_list.append(stacked)
        preacts.append(preact)
    return (states, stacked_list, preacts)


def prefix_count(hot):
    rows, width = hot.shape
    block = 128
    if rows % block:
        return jnp.cumsum(hot.astype(jnp.int32), axis=0)
    blocks = rows // block
    ramp = jnp.arange(block, dtype=jnp.int32)
    lower = (ramp[:, None] >= ramp[None, :]).astype(jnp.bfloat16)
    pieces = hot.astype(jnp.bfloat16).reshape(blocks, block, width)
    within = jnp.einsum("ij,bjk->bik", lower, pieces, preferred_element_type=jnp.float32)
    totals = within[:, -1, :].astype(jnp.bfloat16)
    steps = jnp.arange(blocks, dtype=jnp.int32)
    before = (steps[:, None] > steps[None, :]).astype(jnp.bfloat16)
    offsets = jnp.dot(before, totals, preferred_element_type=jnp.float32)
    return (within + offsets[:, None, :]).reshape(rows, width).astype(jnp.int32)


def route_rows(epoch_rows, row_object, object_slot):
    wide_count = lax.axis_size("wide")
    objects_all = object_slot.shape[0]
    per_dev = objects_all // wide_count
    rows_total = epoch_rows.shape[0]
    feat_width = epoch_rows.shape[1]
    capacity = rows_total // wide_count
    live_rows = row_object >= 0
    safe_object = jnp.maximum(row_object, 0)
    match_table = safe_object[:, None] == jnp.arange(objects_all, dtype=jnp.int32)[None, :]
    slot_of = jnp.sum(jnp.where(match_table, object_slot[None, :], 0), axis=1)
    owner_dev = slot_of // per_dev
    local_place = slot_of % per_dev
    owner_hot = (
        owner_dev[:, None] == jnp.arange(wide_count, dtype=jnp.int32)[None, :]
    ) & live_rows[:, None]
    running = prefix_count(owner_hot)
    send_rank = jnp.sum(jnp.where(owner_hot, running, 0), axis=1) - 1
    send_index = jnp.where(live_rows, owner_dev * capacity + send_rank, -1)
    pick = (
        jnp.arange(rows_total, dtype=jnp.int32)[:, None] == send_index[None, :]
    ).astype(jnp.bfloat16)
    place_hot = (
        (local_place[:, None] == jnp.arange(per_dev, dtype=jnp.int32)[None, :]) & live_rows[:, None]
    ).astype(jnp.bfloat16)
    send_place = jnp.dot(pick, place_hot, preferred_element_type=jnp.float32).astype(jnp.bfloat16)
    send_rows = jnp.dot(pick, epoch_rows, preferred_element_type=jnp.float32).astype(jnp.bfloat16)
    got_rows, got_place = (
        lax.all_to_all(
            send_rows.reshape(wide_count, capacity, feat_width),
            "wide",
            split_axis=0,
            concat_axis=0,
            tiled=True,
        ),
        lax.all_to_all(
            send_place.reshape(wide_count, capacity, per_dev),
            "wide",
            split_axis=0,
            concat_axis=0,
            tiled=True,
        ),
    )
    place_hot = got_place.reshape(-1, per_dev) > 0
    arrival = prefix_count(place_hot)
    position = jnp.sum(jnp.where(place_hot, arrival, 0), axis=1) - 1
    place_code = jnp.sum(
        jnp.where(place_hot, jnp.arange(per_dev, dtype=jnp.int32)[None, :], 0), axis=1
    )
    counts = jnp.sum(place_hot.astype(jnp.int32), axis=0)
    target = jnp.where(jnp.any(place_hot, axis=1), place_code * SEQ + position, -1)
    put = (
        jnp.arange(per_dev * SEQ, dtype=jnp.int32)[:, None] == target[None, :]
    ).astype(jnp.bfloat16)
    sequences = jnp.dot(
        put, got_rows.reshape(-1, feat_width), preferred_element_type=jnp.float32
    ).astype(jnp.bfloat16)
    return (sequences.reshape(per_dev, SEQ, feat_width), counts)


def all_reduce_wide(grads):
    wide_count = lax.axis_size("wide")
    steps = wide_count.bit_length() - 1
    assert 1 << steps == wide_count
    order_even = list(range(steps))
    order_odd = [0] + list(range(2, steps)) + [1] if steps > 2 else order_even
    me = lax.axis_index("wide")
    odd = me & 1

    def exchange_at(step):
        pairs = []
        for i in range(wide_count):
            dim = (order_odd if i & 1 else order_even)[step]
            pairs.append((i, i ^ (1 << dim)))
        bit_even = (me >> order_even[step]) & 1
        bit_odd = (me >> order_odd[step]) & 1
        return pairs, jnp.where(odd == 1, bit_odd, bit_even)

    buf = grads
    for step in range(steps):
        pairs, bit = exchange_at(step)
        half = buf.shape[1] // 2
        keep = lax.dynamic_slice_in_dim(buf, bit * half, half, axis=1)
        send = lax.dynamic_slice_in_dim(buf, (1 - bit) * half, half, axis=1)
        buf = keep + lax.ppermute(send, "wide", pairs)
    buf = buf.astype(jnp.bfloat16)
    for step in reversed(range(steps)):
        pairs, bit = exchange_at(step)
        got = lax.ppermute(buf, "wide", pairs)
        low = jnp.where(bit == 0, buf, got)
        high = jnp.where(bit == 0, got, buf)
        buf = jnp.concatenate([low, high], axis=1)
    return buf.reshape(buf.shape[0], -1).astype(jnp.float32)


def local(epoch_rows, row_object, object_slot, master, momentum, teacher):
    objects_all = object_slot.shape[0]
    feat_width = epoch_rows.shape[1]
    layer_total = master.shape[0]
    student_w = lax.optimization_barrier(master.reshape(layer_total, KER * feat_width, feat_width)).astype(jnp.bfloat16)
    teacher_w = lax.optimization_barrier(teacher.reshape(layer_total, KER * feat_width, feat_width)).astype(jnp.bfloat16)
    sequences, counts = route_rows(epoch_rows, row_object, object_slot)
    valid_mask = (jnp.arange(SEQ, dtype=jnp.int32)[None, :] < counts[:, None]).astype(jnp.float32)[
        :, :, None
    ]
    teacher_out = run_network(sequences, teacher_w)[0]
    student_out, stacked_list, preacts = run_network(sequences, student_w)
    partial_sum = jnp.sum(valid_mask * teacher_out.astype(jnp.float32), axis=(0, 1))
    number = jnp.sum(counts).astype(jnp.float32)
    wide_count = lax.axis_size("wide")
    stats = jnp.concatenate([partial_sum, jnp.full((128,), number, jnp.float32)])
    gathered = lax.all_to_all(
        jnp.broadcast_to(stats[None, :], (wide_count, stats.shape[0])),
        "wide", split_axis=0, concat_axis=0, tiled=True,
    )
    stats_all = jnp.sum(gathered, axis=0)
    total_sum = stats_all[:feat_width]
    count_all = stats_all[feat_width]
    center = total_sum / count_all
    teacher_prob = softmax_rows((teacher_out.astype(jnp.float32) - center) / tau_teacher)
    student_f = student_out.astype(jnp.float32)
    student_prob = softmax_rows(student_f / tau_student)
    embeddings = jnp.sum(valid_mask * student_f, axis=1) / counts.astype(jnp.float32)[:, None]
    upstream = valid_mask * (student_prob - teacher_prob) / (tau_student * objects_all)
    gradients = [None] * layer_total
    for layer_at in reversed(range(layer_total)):
        delta_bf = (upstream * silu_slope(preacts[layer_at])).astype(jnp.bfloat16)
        flat_delta = delta_bf.reshape(-1, feat_width)
        weight_grad = lax.dot_general(
            stacked_list[layer_at].reshape(-1, KER * feat_width),
            flat_delta,
            (((0,), (0,)), ((), ())),
            preferred_element_type=jnp.float32,
        )
        gradients[layer_at] = weight_grad
        if layer_at > 0:
            back_rows = lax.dot_general(
                flat_delta,
                student_w[layer_at],
                (((1,), (1,)), ((), ())),
                preferred_element_type=jnp.float32,
            ).reshape(sequences.shape[0], SEQ, KER, feat_width)
            offset = 4**layer_at
            for tap_index in range(KER):
                upstream = upstream + advanced(back_rows[:, :, tap_index], tap_index * offset)
    stacked_grads = jnp.stack(gradients)
    full_grad = all_reduce_wide(stacked_grads)
    new_momentum = momentum_rate * momentum + full_grad
    new_master = master - learn_rate * new_momentum
    new_teacher = ema_rate * teacher + (1.0 - ema_rate) * new_master
    return (new_master, new_momentum, new_teacher, embeddings)


def solution(mesh):
    in_specs = (
        P(("groups", "wide"), None),
        P(("groups", "wide")),
        P("groups"),
        P("groups", None),
        P("groups", None),
        P("groups", None),
    )
    out_specs = (
        P("groups", None),
        P("groups", None),
        P("groups", None),
        P(("groups", "wide"), None),
    )
    return jax.shard_map(local, mesh=mesh, in_specs=in_specs, out_specs=out_specs, check_vma=False)
```

```python
import jax
import jax.numpy as jnp
from jax import lax
from jax.sharding import PartitionSpec as P

KER = 3
SEQ = 256


tau_student = 1.0
tau_teacher = 0.5
momentum_rate = 0.9
learn_rate = 0.05
ema_rate = 0.996


def delayed(states, offset):
    length = states.shape[1]
    return jnp.concatenate(
        [jnp.zeros_like(states[:, :offset]), states[:, : length - offset]], axis=1
    )


def advanced(states, offset):
    length = states.shape[1]
    return jnp.concatenate([states[:, offset:], jnp.zeros_like(states[:, :offset])], axis=1)


def silu_slope(values):
    gate_value = jax.nn.sigmoid(values)
    return gate_value * (1.0 + values * (1.0 - gate_value))


def softmax_rows(values):
    shifted = values - lax.optimization_barrier(jnp.max(values, axis=-1, keepdims=True))
    raised = jnp.exp(shifted)
    total = lax.optimization_barrier(jnp.sum(raised, axis=-1, keepdims=True))
    return raised / total


def run_network(states, weights):
    stacked_list = []
    preacts = []
    for layer_at in range(weights.shape[0]):
        offset = 4**layer_at
        stacked = jnp.concatenate(
            [delayed(states, tap_index * offset) for tap_index in range(KER)], axis=2
        )
        preact = jnp.dot(
            stacked.reshape(-1, stacked.shape[2]),
            weights[layer_at],
            preferred_element_type=jnp.float32,
        ).reshape(states.shape)
        states = (states.astype(jnp.float32) + jax.nn.silu(preact)).astype(jnp.bfloat16)
        stacked_list.append(stacked)
        preacts.append(preact)
    return (states, stacked_list, preacts)


def prefix_count(hot):
    rows, width = hot.shape
    block = 128
    if rows % block:
        return jnp.cumsum(hot.astype(jnp.int32), axis=0)
    blocks = rows // block
    ramp = jnp.arange(block, dtype=jnp.int32)
    lower = (ramp[:, None] >= ramp[None, :]).astype(jnp.bfloat16)
    pieces = hot.astype(jnp.bfloat16).reshape(blocks, block, width)
    within = jnp.einsum("ij,bjk->bik", lower, pieces, preferred_element_type=jnp.float32)
    totals = within[:, -1, :].astype(jnp.bfloat16)
    steps = jnp.arange(blocks, dtype=jnp.int32)
    before = (steps[:, None] > steps[None, :]).astype(jnp.bfloat16)
    offsets = jnp.dot(before, totals, preferred_element_type=jnp.float32)
    return (within + offsets[:, None, :]).reshape(rows, width).astype(jnp.int32)


def route_rows(epoch_rows, row_object, object_slot):
    wide_count = lax.axis_size("wide")
    objects_all = object_slot.shape[0]
    per_dev = objects_all // wide_count
    rows_total = epoch_rows.shape[0]
    feat_width = epoch_rows.shape[1]
    capacity = rows_total // wide_count
    live_rows = row_object >= 0
    safe_object = jnp.maximum(row_object, 0)
    match_table = safe_object[:, None] == jnp.arange(objects_all, dtype=jnp.int32)[None, :]
    slot_of = jnp.sum(jnp.where(match_table, object_slot[None, :], 0), axis=1)
    owner_dev = slot_of // per_dev
    local_place = slot_of % per_dev
    owner_hot = (
        owner_dev[:, None] == jnp.arange(wide_count, dtype=jnp.int32)[None, :]
    ) & live_rows[:, None]
    running = prefix_count(owner_hot)
    send_rank = jnp.sum(jnp.where(owner_hot, running, 0), axis=1) - 1
    send_index = jnp.where(live_rows, owner_dev * capacity + send_rank, -1)
    pick = (
        jnp.arange(rows_total, dtype=jnp.int32)[:, None] == send_index[None, :]
    ).astype(jnp.bfloat16)
    place_hot = (
        (local_place[:, None] == jnp.arange(per_dev, dtype=jnp.int32)[None, :]) & live_rows[:, None]
    ).astype(jnp.bfloat16)
    send_place = jnp.dot(pick, place_hot, preferred_element_type=jnp.float32).astype(jnp.bfloat16)
    send_rows = jnp.dot(pick, epoch_rows, preferred_element_type=jnp.float32).astype(jnp.bfloat16)
    got_rows, got_place = (
        lax.all_to_all(
            send_rows.reshape(wide_count, capacity, feat_width),
            "wide",
            split_axis=0,
            concat_axis=0,
            tiled=True,
        ),
        lax.all_to_all(
            send_place.reshape(wide_count, capacity, per_dev),
            "wide",
            split_axis=0,
            concat_axis=0,
            tiled=True,
        ),
    )
    place_hot = got_place.reshape(-1, per_dev) > 0
    arrival = prefix_count(place_hot)
    position = jnp.sum(jnp.where(place_hot, arrival, 0), axis=1) - 1
    place_code = jnp.sum(
        jnp.where(place_hot, jnp.arange(per_dev, dtype=jnp.int32)[None, :], 0), axis=1
    )
    counts = jnp.sum(place_hot.astype(jnp.int32), axis=0)
    target = jnp.where(jnp.any(place_hot, axis=1), place_code * SEQ + position, -1)
    put = lax.optimization_barrier(
        (jnp.arange(per_dev * SEQ, dtype=jnp.int32)[:, None] == target[None, :]).astype(jnp.bfloat16)
    )
    sequences = jnp.dot(
        put, got_rows.reshape(-1, feat_width), preferred_element_type=jnp.float32
    ).astype(jnp.bfloat16)
    return (sequences.reshape(per_dev, SEQ, feat_width), counts)


def all_reduce_wide(grads):
    wide_count = lax.axis_size("wide")
    steps = wide_count.bit_length() - 1
    assert 1 << steps == wide_count
    order_even = list(range(steps))
    order_odd = [0] + list(range(2, steps)) + [1] if steps > 2 else order_even
    me = lax.axis_index("wide")
    odd = me & 1

    def exchange_at(step):
        pairs = []
        for i in range(wide_count):
            dim = (order_odd if i & 1 else order_even)[step]
            pairs.append((i, i ^ (1 << dim)))
        bit_even = (me >> order_even[step]) & 1
        bit_odd = (me >> order_odd[step]) & 1
        return pairs, jnp.where(odd == 1, bit_odd, bit_even)

    buf = grads
    for step in range(steps):
        pairs, bit = exchange_at(step)
        half = buf.shape[1] // 2
        keep = lax.dynamic_slice_in_dim(buf, bit * half, half, axis=1)
        send = lax.dynamic_slice_in_dim(buf, (1 - bit) * half, half, axis=1)
        buf = keep + lax.ppermute(send, "wide", pairs)
    buf = buf.astype(jnp.bfloat16)
    for step in reversed(range(steps)):
        pairs, bit = exchange_at(step)
        got = lax.ppermute(buf, "wide", pairs)
        low = jnp.where(bit == 0, buf, got)
        high = jnp.where(bit == 0, got, buf)
        buf = jnp.concatenate([low, high], axis=1)
    return buf.reshape(buf.shape[0], -1).astype(jnp.float32)


def local(epoch_rows, row_object, object_slot, master, momentum, teacher):
    objects_all = object_slot.shape[0]
    feat_width = epoch_rows.shape[1]
    layer_total = master.shape[0]
    student_w = lax.optimization_barrier(master.reshape(layer_total, KER * feat_width, feat_width)).astype(jnp.bfloat16)
    teacher_w = lax.optimization_barrier(teacher.reshape(layer_total, KER * feat_width, feat_width)).astype(jnp.bfloat16)
    sequences, counts = route_rows(epoch_rows, row_object, object_slot)
    valid_mask = (jnp.arange(SEQ, dtype=jnp.int32)[None, :] < counts[:, None]).astype(jnp.float32)[
        :, :, None
    ]
    teacher_out = run_network(sequences, teacher_w)[0]
    student_out, stacked_list, preacts = run_network(sequences, student_w)
    partial_sum = jnp.sum(valid_mask * teacher_out.astype(jnp.float32), axis=(0, 1))
    number = jnp.sum(counts).astype(jnp.float32)
    wide_count = lax.axis_size("wide")
    stats = jnp.concatenate([partial_sum, jnp.full((128,), number, jnp.float32)])
    gathered = lax.all_to_all(
        jnp.broadcast_to(stats[None, :], (wide_count, stats.shape[0])),
        "wide", split_axis=0, concat_axis=0, tiled=True,
    )
    stats_all = jnp.sum(gathered, axis=0)
    total_sum = stats_all[:feat_width]
    count_all = stats_all[feat_width]
    center = total_sum / count_all
    teacher_prob = softmax_rows((teacher_out.astype(jnp.float32) - center) / tau_teacher)
    student_f = student_out.astype(jnp.float32)
    student_prob = softmax_rows(student_f / tau_student)
    embeddings = jnp.sum(valid_mask * student_f, axis=1) / counts.astype(jnp.float32)[:, None]
    upstream = valid_mask * (student_prob - teacher_prob) / (tau_student * objects_all)
    gradients = [None] * layer_total
    for layer_at in reversed(range(layer_total)):
        delta_bf = (upstream * silu_slope(preacts[layer_at])).astype(jnp.bfloat16)
        flat_delta = delta_bf.reshape(-1, feat_width)
        weight_grad = lax.dot_general(
            stacked_list[layer_at].reshape(-1, KER * feat_width),
            flat_delta,
            (((0,), (0,)), ((), ())),
            preferred_element_type=jnp.float32,
        )
        gradients[layer_at] = weight_grad
        if layer_at > 0:
            back_rows = lax.dot_general(
                flat_delta,
                student_w[layer_at],
                (((1,), (1,)), ((), ())),
                preferred_element_type=jnp.float32,
            ).reshape(sequences.shape[0], SEQ, KER, feat_width)
            offset = 4**layer_at
            for tap_index in range(KER):
                upstream = upstream + advanced(back_rows[:, :, tap_index], tap_index * offset)
    stacked_grads = jnp.stack(gradients)
    full_grad = all_reduce_wide(stacked_grads)
    new_momentum = momentum_rate * momentum + full_grad
    new_master = master - learn_rate * new_momentum
    new_teacher = ema_rate * teacher + (1.0 - ema_rate) * new_master
    return (new_master, new_momentum, new_teacher, embeddings)


def solution(mesh):
    in_specs = (
        P(("groups", "wide"), None),
        P(("groups", "wide")),
        P("groups"),
        P("groups", None),
        P("groups", None),
        P("groups", None),
    )
    out_specs = (
        P("groups", None),
        P("groups", None),
        P("groups", None),
        P(("groups", "wide"), None),
    )
    return jax.shard_map(local, mesh=mesh, in_specs=in_specs, out_specs=out_specs, check_vma=False)
```

```python
import jax
import jax.numpy as jnp
from jax import lax
from jax.sharding import PartitionSpec as P

KER = 3
SEQ = 256


tau_student = 1.0
tau_teacher = 0.5
momentum_rate = 0.9
learn_rate = 0.05
ema_rate = 0.996


def delayed(states, offset):
    length = states.shape[1]
    return jnp.concatenate(
        [jnp.zeros_like(states[:, :offset]), states[:, : length - offset]], axis=1
    )


def advanced(states, offset):
    length = states.shape[1]
    return jnp.concatenate([states[:, offset:], jnp.zeros_like(states[:, :offset])], axis=1)


def silu_slope(values):
    gate_value = jax.nn.sigmoid(values)
    return gate_value * (1.0 + values * (1.0 - gate_value))


def softmax_rows(values):
    shifted = values - lax.optimization_barrier(jnp.max(values, axis=-1, keepdims=True))
    raised = jnp.exp(shifted)
    total = lax.optimization_barrier(jnp.sum(raised, axis=-1, keepdims=True))
    return raised / total


def run_network(states, weights):
    stacked_list = []
    preacts = []
    for layer_at in range(weights.shape[0]):
        offset = 4**layer_at
        stacked = jnp.concatenate(
            [delayed(states, tap_index * offset) for tap_index in range(KER)], axis=2
        )
        preact = jnp.dot(
            stacked.reshape(-1, stacked.shape[2]),
            weights[layer_at],
            preferred_element_type=jnp.float32,
        ).reshape(states.shape)
        states = (states.astype(jnp.float32) + jax.nn.silu(preact)).astype(jnp.bfloat16)
        stacked_list.append(stacked)
        preacts.append(preact)
    return (states, stacked_list, preacts)


def prefix_count(hot):
    rows, width = hot.shape
    block = 128
    if rows % block:
        return jnp.cumsum(hot.astype(jnp.int32), axis=0)
    blocks = rows // block
    ramp = jnp.arange(block, dtype=jnp.int32)
    lower = (ramp[:, None] >= ramp[None, :]).astype(jnp.bfloat16)
    pieces = hot.astype(jnp.bfloat16).reshape(blocks, block, width)
    within = jnp.einsum("ij,bjk->bik", lower, pieces, preferred_element_type=jnp.float32)
    totals = within[:, -1, :].astype(jnp.bfloat16)
    steps = jnp.arange(blocks, dtype=jnp.int32)
    before = (steps[:, None] > steps[None, :]).astype(jnp.bfloat16)
    offsets = jnp.dot(before, totals, preferred_element_type=jnp.float32)
    return (within + offsets[:, None, :]).reshape(rows, width).astype(jnp.int32)


def route_rows(epoch_rows, row_object, object_slot):
    wide_count = lax.axis_size("wide")
    objects_all = object_slot.shape[0]
    per_dev = objects_all // wide_count
    rows_total = epoch_rows.shape[0]
    feat_width = epoch_rows.shape[1]
    capacity = rows_total // wide_count
    live_rows = row_object >= 0
    safe_object = jnp.maximum(row_object, 0)
    match_table = safe_object[:, None] == jnp.arange(objects_all, dtype=jnp.int32)[None, :]
    slot_of = jnp.sum(jnp.where(match_table, object_slot[None, :], 0), axis=1)
    owner_dev = slot_of // per_dev
    local_place = slot_of % per_dev
    owner_hot = (
        owner_dev[:, None] == jnp.arange(wide_count, dtype=jnp.int32)[None, :]
    ) & live_rows[:, None]
    running = prefix_count(owner_hot)
    send_rank = jnp.sum(jnp.where(owner_hot, running, 0), axis=1) - 1
    send_index = jnp.where(live_rows, owner_dev * capacity + send_rank, -1)
    pick = (
        jnp.arange(rows_total, dtype=jnp.int32)[:, None] == send_index[None, :]
    ).astype(jnp.bfloat16)
    place_hot = (
        (local_place[:, None] == jnp.arange(per_dev, dtype=jnp.int32)[None, :]) & live_rows[:, None]
    ).astype(jnp.bfloat16)
    send_place = jnp.dot(pick, place_hot, preferred_element_type=jnp.float32).astype(jnp.bfloat16)
    send_rows = jnp.dot(pick, epoch_rows, preferred_element_type=jnp.float32).astype(jnp.bfloat16)
    got_rows, got_place = (
        lax.all_to_all(
            send_rows.reshape(wide_count, capacity, feat_width),
            "wide",
            split_axis=0,
            concat_axis=0,
            tiled=True,
        ),
        lax.all_to_all(
            send_place.reshape(wide_count, capacity, per_dev),
            "wide",
            split_axis=0,
            concat_axis=0,
            tiled=True,
        ),
    )
    place_hot = got_place.reshape(-1, per_dev) > 0
    arrival = prefix_count(place_hot)
    position = jnp.sum(jnp.where(place_hot, arrival, 0), axis=1) - 1
    place_code = jnp.sum(
        jnp.where(place_hot, jnp.arange(per_dev, dtype=jnp.int32)[None, :], 0), axis=1
    )
    counts = jnp.sum(place_hot.astype(jnp.int32), axis=0)
    target = jnp.where(jnp.any(place_hot, axis=1), place_code * SEQ + position, -1)
    put = (
        jnp.arange(per_dev * SEQ, dtype=jnp.int32)[:, None] == target[None, :]
    ).astype(jnp.bfloat16)
    sequences = jnp.dot(
        put, got_rows.reshape(-1, feat_width), preferred_element_type=jnp.float32
    ).astype(jnp.bfloat16)
    return (sequences.reshape(per_dev, SEQ, feat_width), counts)


def all_reduce_wide(grads):
    wide_count = lax.axis_size("wide")
    steps = wide_count.bit_length() - 1
    assert 1 << steps == wide_count
    order_even = list(range(steps))
    order_odd = [0] + list(range(2, steps)) + [1] if steps > 2 else order_even
    me = lax.axis_index("wide")
    odd = me & 1

    def exchange_at(step):
        pairs = []
        for i in range(wide_count):
            dim = (order_odd if i & 1 else order_even)[step]
            pairs.append((i, i ^ (1 << dim)))
        bit_even = (me >> order_even[step]) & 1
        bit_odd = (me >> order_odd[step]) & 1
        return pairs, jnp.where(odd == 1, bit_odd, bit_even)

    pairs, bit = exchange_at(0)
    half = grads[0].shape[0] // 2
    per_layer = []
    for layer_grad in grads:
        keep = lax.dynamic_slice_in_dim(layer_grad, bit * half, half, axis=0)
        send = lax.dynamic_slice_in_dim(layer_grad, (1 - bit) * half, half, axis=0)
        per_layer.append(keep + lax.ppermute(send, "wide", pairs))
    buf = jnp.stack(per_layer)
    for step in range(1, steps):
        pairs, bit = exchange_at(step)
        half = buf.shape[1] // 2
        keep = lax.dynamic_slice_in_dim(buf, bit * half, half, axis=1)
        send = lax.dynamic_slice_in_dim(buf, (1 - bit) * half, half, axis=1)
        buf = keep + lax.ppermute(send, "wide", pairs)
    buf = buf.astype(jnp.bfloat16)
    for step in reversed(range(steps)):
        pairs, bit = exchange_at(step)
        got = lax.ppermute(buf, "wide", pairs)
        low = jnp.where(bit == 0, buf, got)
        high = jnp.where(bit == 0, got, buf)
        buf = jnp.concatenate([low, high], axis=1)
    return buf.reshape(buf.shape[0], -1).astype(jnp.float32)


def local(epoch_rows, row_object, object_slot, master, momentum, teacher):
    objects_all = object_slot.shape[0]
    feat_width = epoch_rows.shape[1]
    layer_total = master.shape[0]
    student_w = lax.optimization_barrier(master.reshape(layer_total, KER * feat_width, feat_width)).astype(jnp.bfloat16)
    teacher_w = lax.optimization_barrier(teacher.reshape(layer_total, KER * feat_width, feat_width)).astype(jnp.bfloat16)
    sequences, counts = route_rows(epoch_rows, row_object, object_slot)
    valid_mask = (jnp.arange(SEQ, dtype=jnp.int32)[None, :] < counts[:, None]).astype(jnp.float32)[
        :, :, None
    ]
    teacher_out = run_network(sequences, teacher_w)[0]
    student_out, stacked_list, preacts = run_network(sequences, student_w)
    partial_sum = jnp.sum(valid_mask * teacher_out.astype(jnp.float32), axis=(0, 1))
    number = jnp.sum(counts).astype(jnp.float32)
    wide_count = lax.axis_size("wide")
    stats = jnp.concatenate([partial_sum, jnp.full((128,), number, jnp.float32)])
    gathered = lax.all_to_all(
        jnp.broadcast_to(stats[None, :], (wide_count, stats.shape[0])),
        "wide", split_axis=0, concat_axis=0, tiled=True,
    )
    stats_all = jnp.sum(gathered, axis=0)
    total_sum = stats_all[:feat_width]
    count_all = stats_all[feat_width]
    center = total_sum / count_all
    teacher_prob = softmax_rows((teacher_out.astype(jnp.float32) - center) / tau_teacher)
    student_f = student_out.astype(jnp.float32)
    student_prob = softmax_rows(student_f / tau_student)
    embeddings = jnp.sum(valid_mask * student_f, axis=1) / counts.astype(jnp.float32)[:, None]
    upstream = valid_mask * (student_prob - teacher_prob) / (tau_student * objects_all)
    gradients = [None] * layer_total
    for layer_at in reversed(range(layer_total)):
        delta_bf = (upstream * silu_slope(preacts[layer_at])).astype(jnp.bfloat16)
        flat_delta = delta_bf.reshape(-1, feat_width)
        weight_grad = lax.dot_general(
            stacked_list[layer_at].reshape(-1, KER * feat_width),
            flat_delta,
            (((0,), (0,)), ((), ())),
            preferred_element_type=jnp.float32,
        )
        gradients[layer_at] = weight_grad
        if layer_at > 0:
            back_rows = lax.dot_general(
                flat_delta,
                student_w[layer_at],
                (((1,), (1,)), ((), ())),
                preferred_element_type=jnp.float32,
            ).reshape(sequences.shape[0], SEQ, KER, feat_width)
            offset = 4**layer_at
            for tap_index in range(KER):
                upstream = upstream + advanced(back_rows[:, :, tap_index], tap_index * offset)
    full_grad = all_reduce_wide(gradients)
    new_momentum = momentum_rate * momentum + full_grad
    new_master = master - learn_rate * new_momentum
    new_teacher = ema_rate * teacher + (1.0 - ema_rate) * new_master
    return (new_master, new_momentum, new_teacher, embeddings)


def solution(mesh):
    in_specs = (
        P(("groups", "wide"), None),
        P(("groups", "wide")),
        P("groups"),
        P("groups", None),
        P("groups", None),
        P("groups", None),
    )
    out_specs = (
        P("groups", None),
        P("groups", None),
        P("groups", None),
        P(("groups", "wide"), None),
    )
    return jax.shard_map(local, mesh=mesh, in_specs=in_specs, out_specs=out_specs, check_vma=False)
```

```python
import jax
import jax.numpy as jnp
from jax import lax
from jax.sharding import PartitionSpec as P

KER = 3
SEQ = 256


tau_student = 1.0
tau_teacher = 0.5
momentum_rate = 0.9
learn_rate = 0.05
ema_rate = 0.996


def delayed(states, offset):
    length = states.shape[1]
    return jnp.concatenate(
        [jnp.zeros_like(states[:, :offset]), states[:, : length - offset]], axis=1
    )


def advanced(states, offset):
    length = states.shape[1]
    return jnp.concatenate([states[:, offset:], jnp.zeros_like(states[:, :offset])], axis=1)


def silu_slope(values):
    gate_value = jax.nn.sigmoid(values)
    return gate_value * (1.0 + values * (1.0 - gate_value))


def softmax_rows(values):
    shifted = values - lax.optimization_barrier(jnp.max(values, axis=-1, keepdims=True))
    raised = jnp.exp(shifted)
    total = lax.optimization_barrier(jnp.sum(raised, axis=-1, keepdims=True))
    return raised / total


def run_network(states, weights):
    stacked_list = []
    preacts = []
    for layer_at in range(weights.shape[0]):
        offset = 4**layer_at
        stacked = jnp.concatenate(
            [delayed(states, tap_index * offset) for tap_index in range(KER)], axis=2
        )
        preact = jnp.dot(
            stacked.reshape(-1, stacked.shape[2]),
            weights[layer_at],
            preferred_element_type=jnp.float32,
        ).reshape(states.shape)
        states = (states.astype(jnp.float32) + jax.nn.silu(preact)).astype(jnp.bfloat16)
        stacked_list.append(stacked)
        preacts.append(preact)
    return (states, stacked_list, preacts)


def prefix_count(hot):
    rows, width = hot.shape
    block = 128
    if rows % block:
        return jnp.cumsum(hot.astype(jnp.int32), axis=0)
    blocks = rows // block
    ramp = jnp.arange(block, dtype=jnp.int32)
    lower = (ramp[:, None] >= ramp[None, :]).astype(jnp.bfloat16)
    pieces = hot.astype(jnp.bfloat16).reshape(blocks, block, width)
    within = jnp.einsum("ij,bjk->bik", lower, pieces, preferred_element_type=jnp.float32)
    totals = within[:, -1, :].astype(jnp.bfloat16)
    steps = jnp.arange(blocks, dtype=jnp.int32)
    before = (steps[:, None] > steps[None, :]).astype(jnp.bfloat16)
    offsets = jnp.dot(before, totals, preferred_element_type=jnp.float32)
    return (within + offsets[:, None, :]).reshape(rows, width).astype(jnp.int32)


def route_rows(epoch_rows, row_object, object_slot):
    wide_count = lax.axis_size("wide")
    objects_all = object_slot.shape[0]
    per_dev = objects_all // wide_count
    rows_total = epoch_rows.shape[0]
    feat_width = epoch_rows.shape[1]
    capacity = rows_total // wide_count
    live_rows = row_object >= 0
    safe_object = jnp.maximum(row_object, 0)
    match_table = safe_object[:, None] == jnp.arange(objects_all, dtype=jnp.int32)[None, :]
    slot_of = jnp.sum(jnp.where(match_table, object_slot[None, :], 0), axis=1)
    owner_dev = slot_of // per_dev
    local_place = slot_of % per_dev
    slot_hot = (slot_of[:, None] == jnp.arange(objects_all, dtype=jnp.int32)[None, :]) & live_rows[:, None]
    group_size = jnp.sum(slot_hot.astype(jnp.int32), axis=0).reshape(wide_count, per_dev)
    places = jnp.arange(per_dev, dtype=jnp.int32)
    earlier_place = (places[:, None] < places[None, :]).astype(jnp.int32)
    group_start = jnp.sum(group_size[:, :, None] * earlier_place[None, :, :], axis=1)
    slots = jnp.arange(capacity, dtype=jnp.int32)[None, :, None]
    place_chunks = (
        (slots >= group_start[:, None, :]) & (slots < (group_start + group_size)[:, None, :])
    ).astype(jnp.bfloat16)
    running = prefix_count(slot_hot)
    rank_in_group = jnp.sum(jnp.where(slot_hot, running, 0), axis=1) - 1
    start_of_row = jnp.sum(jnp.where(slot_hot, group_start.reshape(1, -1), 0), axis=1)
    send_index = jnp.where(live_rows, owner_dev * capacity + start_of_row + rank_in_group, -1)
    pick = (
        jnp.arange(rows_total, dtype=jnp.int32)[:, None] == send_index[None, :]
    ).astype(jnp.bfloat16)
    send_rows = jnp.dot(pick, epoch_rows, preferred_element_type=jnp.float32).astype(jnp.bfloat16)
    got_place = lax.all_to_all(place_chunks, "wide", split_axis=0, concat_axis=0, tiled=True)
    got_rows = lax.all_to_all(
        send_rows.reshape(wide_count, capacity, feat_width),
        "wide",
        split_axis=0,
        concat_axis=0,
        tiled=True,
    )
    place_hot = got_place.reshape(-1, per_dev) > 0
    arrival = prefix_count(place_hot)
    position = jnp.sum(jnp.where(place_hot, arrival, 0), axis=1) - 1
    place_code = jnp.sum(
        jnp.where(place_hot, jnp.arange(per_dev, dtype=jnp.int32)[None, :], 0), axis=1
    )
    counts = jnp.sum(place_hot.astype(jnp.int32), axis=0)
    target = jnp.where(jnp.any(place_hot, axis=1), place_code * SEQ + position, -1)
    put = (
        jnp.arange(per_dev * SEQ, dtype=jnp.int32)[:, None] == target[None, :]
    ).astype(jnp.bfloat16)
    sequences = jnp.dot(
        put, got_rows.reshape(-1, feat_width), preferred_element_type=jnp.float32
    ).astype(jnp.bfloat16)
    return (sequences.reshape(per_dev, SEQ, feat_width), counts)


def all_reduce_wide(grads):
    wide_count = lax.axis_size("wide")
    steps = wide_count.bit_length() - 1
    assert 1 << steps == wide_count
    order_even = list(range(steps))
    order_odd = [0] + list(range(2, steps)) + [1] if steps > 2 else order_even
    me = lax.axis_index("wide")
    odd = me & 1

    def exchange_at(step):
        pairs = []
        for i in range(wide_count):
            dim = (order_odd if i & 1 else order_even)[step]
            pairs.append((i, i ^ (1 << dim)))
        bit_even = (me >> order_even[step]) & 1
        bit_odd = (me >> order_odd[step]) & 1
        return pairs, jnp.where(odd == 1, bit_odd, bit_even)

    buf = grads
    for step in range(steps):
        pairs, bit = exchange_at(step)
        half = buf.shape[1] // 2
        keep = lax.dynamic_slice_in_dim(buf, bit * half, half, axis=1)
        send = lax.dynamic_slice_in_dim(buf, (1 - bit) * half, half, axis=1)
        buf = keep + lax.ppermute(send, "wide", pairs)
    buf = buf.astype(jnp.bfloat16)
    for step in reversed(range(steps)):
        pairs, bit = exchange_at(step)
        got = lax.ppermute(buf, "wide", pairs)
        low = jnp.where(bit == 0, buf, got)
        high = jnp.where(bit == 0, got, buf)
        buf = jnp.concatenate([low, high], axis=1)
    return buf.reshape(buf.shape[0], -1).astype(jnp.float32)


def local(epoch_rows, row_object, object_slot, master, momentum, teacher):
    objects_all = object_slot.shape[0]
    feat_width = epoch_rows.shape[1]
    layer_total = master.shape[0]
    student_w = lax.optimization_barrier(master.reshape(layer_total, KER * feat_width, feat_width)).astype(jnp.bfloat16)
    teacher_w = lax.optimization_barrier(teacher.reshape(layer_total, KER * feat_width, feat_width)).astype(jnp.bfloat16)
    sequences, counts = route_rows(epoch_rows, row_object, object_slot)
    valid_mask = (jnp.arange(SEQ, dtype=jnp.int32)[None, :] < counts[:, None]).astype(jnp.float32)[
        :, :, None
    ]
    teacher_out = run_network(sequences, teacher_w)[0]
    student_out, stacked_list, preacts = run_network(sequences, student_w)
    partial_sum = jnp.sum(valid_mask * teacher_out.astype(jnp.float32), axis=(0, 1))
    number = jnp.sum(counts).astype(jnp.float32)
    wide_count = lax.axis_size("wide")
    stats = jnp.concatenate([partial_sum, jnp.full((128,), number, jnp.float32)])
    gathered = lax.all_to_all(
        jnp.broadcast_to(stats[None, :], (wide_count, stats.shape[0])),
        "wide", split_axis=0, concat_axis=0, tiled=True,
    )
    stats_all = jnp.sum(gathered, axis=0)
    total_sum = stats_all[:feat_width]
    count_all = stats_all[feat_width]
    center = total_sum / count_all
    teacher_prob = softmax_rows((teacher_out.astype(jnp.float32) - center) / tau_teacher)
    student_f = student_out.astype(jnp.float32)
    student_prob = softmax_rows(student_f / tau_student)
    embeddings = jnp.sum(valid_mask * student_f, axis=1) / counts.astype(jnp.float32)[:, None]
    upstream = valid_mask * (student_prob - teacher_prob) / (tau_student * objects_all)
    gradients = [None] * layer_total
    for layer_at in reversed(range(layer_total)):
        delta_bf = (upstream * silu_slope(preacts[layer_at])).astype(jnp.bfloat16)
        flat_delta = delta_bf.reshape(-1, feat_width)
        weight_grad = lax.dot_general(
            stacked_list[layer_at].reshape(-1, KER * feat_width),
            flat_delta,
            (((0,), (0,)), ((), ())),
            preferred_element_type=jnp.float32,
        )
        gradients[layer_at] = weight_grad
        if layer_at > 0:
            back_rows = lax.dot_general(
                flat_delta,
                student_w[layer_at],
                (((1,), (1,)), ((), ())),
                preferred_element_type=jnp.float32,
            ).reshape(sequences.shape[0], SEQ, KER, feat_width)
            offset = 4**layer_at
            for tap_index in range(KER):
                upstream = upstream + advanced(back_rows[:, :, tap_index], tap_index * offset)
    stacked_grads = jnp.stack(gradients)
    full_grad = all_reduce_wide(stacked_grads)
    new_momentum = momentum_rate * momentum + full_grad
    new_master = master - learn_rate * new_momentum
    new_teacher = ema_rate * teacher + (1.0 - ema_rate) * new_master
    return (new_master, new_momentum, new_teacher, embeddings)


def solution(mesh):
    in_specs = (
        P(("groups", "wide"), None),
        P(("groups", "wide")),
        P("groups"),
        P("groups", None),
        P("groups", None),
        P("groups", None),
    )
    out_specs = (
        P("groups", None),
        P("groups", None),
        P("groups", None),
        P(("groups", "wide"), None),
    )
    return jax.shard_map(local, mesh=mesh, in_specs=in_specs, out_specs=out_specs, check_vma=False)
```
